32 devices in a mesh: groups: 2 (over y), seq: 8 (over z, x), batch: 2 (over core).
Axes of the slice: x: 2, y: 2, z: 4, core: 2. Of those that a mesh axis runs over, the one named last changes fastest.
Arguments:
- tokens: int32 [4, 4096], P(('groups', 'batch'), 'seq'), parts along dimension 0, may hold values from 0 to 3
- hidden: bfloat16 [4, 4096, 1024], P(('groups', 'batch'), 'seq'), parts along dimension 0, may hold values from -6 to 6
- base_table: bfloat16 [4, 1024], replicated, may hold values from -6 to 6
- w_in: bfloat16 [1024, 2304], replicated, may hold values from -0.1875 to 0.1875
- w_dt: bfloat16 [1024, 16], replicated, may hold values from -0.1875 to 0.1875
- conv_w: float32 [4, 1280], replicated, may hold values from -3 to 3
- conv_b: float32 [1280], replicated, may hold values from -3 to 3
- dt_bias: float32 [16], replicated, as said below
- a_log: float32 [16], replicated, as said below
- d_skip: float32 [16], replicated, may hold values from 0.5 to 1.5
- norm_gain: float32 [1024], replicated, may hold values from 0.1 to 1.9
- w_out: bfloat16 [1024, 1024], replicated, may hold values from -0.1875 to 0.1875
Outputs:
- mixed: bfloat16 [4, 4096, 1024], P(('groups', 'batch'), 'seq'), parts along dimension 0
The draws below stay inside these ranges and needn't reach their ends.
There are 2 independent parts, one for each index of `groups`. The reference program is written for one: setup_inputs(seed, part) draws one part's arguments, and reference() takes and returns one part's arrays. A program takes and returns all parts, laid end to end along the dimension named above; an argument that names none is the same for every part. Nothing has to cross between parts.
Inputs may be any that keep to these rules, and one draw needn't show every extreme that they name: `a_log`: real numbers, one for each head. `dt_bias`: real numbers, one for each head.
All inputs are finite; a program needn't handle non-finite values.
Results may differ from the reference program's by a relative error of at most 0.0017.
The reference program's roundings to bfloat16 on the way count: a program that leaves them out, or rounds other values in their place, can miss the bound.
Values may be sent and summed in bfloat16 or wider, within the bound.
No kernel may reach another device: no remote copies, remote signals or barrier semaphores. Data moves between devices by JAX's collectives and lax.ppermute only.
A program may use at most 192 MiB of HBM per device.

```python
import jax
import jax.numpy as jnp
from jax import lax

D = 1024
H = 16
P_SIZE = 64
N = 128
Q = 256
KCONV = 4
LENGTH = 4096
BATCH = 2


def head_kinds(key):
    picked = jax.random.uniform(jax.random.fold_in(key, 11), (H,))
    share = 0.5
    slow = picked < share
    jitter = jax.random.uniform(jax.random.fold_in(key, 12), (H,), minval=-0.7, maxval=0.7)
    return (slow, jitter)


def draw_a_log(key, part):
    slow, jitter = head_kinds(key)
    root = jnp.sqrt(jnp.float32(LENGTH))
    slow_rate = jnp.log(0.125 / root) + jitter
    fast_rate = jnp.log(0.07) + 0.5 * jitter
    return jnp.where(slow, slow_rate, fast_rate).astype(jnp.float32)


def draw_dt_bias(key, part):
    slow, jitter = head_kinds(key)
    root = jnp.sqrt(jnp.float32(LENGTH))
    slow_bias = jnp.log(jnp.expm1(4.0 / root * jnp.exp(0.4 * jitter)))
    fast_bias = 0.3 * jitter
    return jnp.where(slow, slow_bias, fast_bias).astype(jnp.float32)


def touch_ends(values, key, smallest, largest):
    dims = values.shape
    place = [jax.random.randint(jax.random.fold_in(key, axis), (), 0, dims[axis]) for axis in range(len(dims))]
    values = values.at[tuple(place)].set(smallest)
    longest = dims.index(max(dims))
    place[longest] = (place[longest] + 1) % dims[longest]
    return values.at[tuple(place)].set(largest)


def levels(own_key, extent, shards, least, high):
    def one(position, shards_of):
        steps = jax.random.uniform(jax.random.fold_in(jax.random.fold_in(own_key, 6), position), (shards_of,), jnp.float32, least / len(shards), high / len(shards))
        return jnp.repeat(jnp.exp(steps), extent[position] // shards_of).reshape((-1,) + (1,) * (len(extent) - position - 1))

    gain = one(*shards[0])
    for cut in shards[1:]:
        gain = gain * one(*cut)
    return gain


def gaussian(own_key, shape, deviation, most, split=(), kind=jnp.bfloat16):
    drawn = jax.random.normal(own_key, shape, jnp.float32) * deviation
    if len(split) > 0:
        drawn = levels(own_key, shape, split, -0.22, 0.18) * drawn
    return jnp.clip(drawn, min=-most, max=most).astype(kind)


def setup_inputs(seed: int = 0, part: int = 0) -> dict:
    streams_of = jax.random.split(jax.random.key(seed), 13)
    part_keys = jax.random.split(jax.random.fold_in(streams_of[12], part), 13)
    tokens = touch_ends(jax.random.randint(part_keys[0], (BATCH, LENGTH), 0, 4), jax.random.fold_in(part_keys[0], 1), 0, 3).astype(jnp.int32)
    hidden = gaussian(part_keys[1], (BATCH, LENGTH, D), 1.0, 6.0, ((0, 2), (1, 8)))
    base_table = gaussian(streams_of[2], (4, D), 1.0, 6.0)
    w_in = gaussian(streams_of[3], (D, 2 * H * P_SIZE + 2 * N), D ** -0.5, 0.1875)
    w_dt = gaussian(streams_of[4], (D, H), D ** -0.5, 0.1875)
    conv_w = gaussian(streams_of[5], (KCONV, H * P_SIZE + 2 * N), 0.5, 3.0, (), jnp.float32)
    conv_b = gaussian(streams_of[6], (H * P_SIZE + 2 * N,), 0.5, 3.0, (), jnp.float32)
    dt_bias = draw_dt_bias(jax.random.fold_in(streams_of[12], 71), part)
    a_log = draw_a_log(jax.random.fold_in(streams_of[12], 71), part)
    d_skip = jnp.clip(jax.random.uniform(streams_of[9], (H,), jnp.float32, 0.5, 1.5), 0.5, 1.5)
    norm_gain = jnp.clip(1.0 + 0.18 * jax.random.normal(streams_of[10], (H * P_SIZE,), jnp.float32), 0.1, 1.9)
    w_out = gaussian(streams_of[11], (H * P_SIZE, D), (H * P_SIZE) ** -0.5, 0.1875)
    return dict(tokens=tokens, hidden=hidden, base_table=base_table, w_in=w_in, w_dt=w_dt, conv_w=conv_w, conv_b=conv_b, dt_bias=dt_bias, a_log=a_log, d_skip=d_skip, norm_gain=norm_gain, w_out=w_out)


norm_epsilon = 1e-05

def span_terms(heads_x, b_rows, c_rows, step_size, rates):
    log_decay = jnp.cumsum(step_size * rates[None, :], axis=0)
    across = jnp.transpose(log_decay)
    width = across.shape[1]
    lower = (jnp.arange(width)[:, None] >= jnp.arange(width)[None, :])[None]
    gaps = across[:, :, None] - across[:, None, :]
    decays = jnp.where(lower, jnp.exp(jnp.where(lower, gaps, 0.0)), 0.0)
    scores = jnp.dot(c_rows, jnp.transpose(b_rows), preferred_element_type=jnp.float32)
    weights = (decays * scores[None] * jnp.transpose(step_size)[:, None, :]).astype(jnp.bfloat16)
    inside = jnp.einsum('hts,shp->thp', weights.astype(jnp.float32), heads_x.astype(jnp.float32))
    to_end = jnp.exp(log_decay[-1][None, :] - log_decay) * step_size
    state_weights = (b_rows.astype(jnp.float32)[:, None, :] * to_end[:, :, None]).astype(jnp.bfloat16)
    state = jnp.einsum('shp,shn->hpn', heads_x.astype(jnp.float32), state_weights.astype(jnp.float32))
    return (inside, state, jnp.exp(log_decay[-1]), jnp.exp(log_decay))

def mixer(strand, w_in, w_dt, conv_w, conv_b, dt_bias, a_log, d_skip, norm_gain, w_out):
    length = strand.shape[0]
    inner = H * P_SIZE
    projected = jnp.dot(strand, w_in, preferred_element_type=jnp.float32)
    gate_part = projected[:, :inner]
    source = projected[:, inner:]
    padded = jnp.concatenate([jnp.zeros((KCONV - 1, source.shape[1]), jnp.float32), source], axis=0)
    summed = jnp.broadcast_to(conv_b, source.shape)
    for tap in range(KCONV):
        summed = summed + conv_w[tap] * padded[tap:tap + length]
    activated = jax.nn.silu(summed).astype(jnp.bfloat16)
    step_size = jax.nn.softplus(jnp.dot(strand, w_dt, preferred_element_type=jnp.float32) + dt_bias)
    rates = -jnp.exp(a_log)
    spans = length // Q
    heads_x = activated[:, :inner].reshape(spans, Q, H, P_SIZE)
    b_rows = activated[:, inner:inner + N].reshape(spans, Q, N)
    c_rows = activated[:, inner + N:].reshape(spans, Q, N)
    steps_cut = step_size.reshape(spans, Q, H)

    def per_span(carry, pieces):
        piece_x, piece_b, piece_c, piece_s = pieces
        inside, state, total, from_start = span_terms(piece_x, piece_b, piece_c, piece_s, rates)
        carried = jnp.einsum('tn,hpn->thp', piece_c.astype(jnp.float32), carry, precision=lax.Precision.HIGHEST)
        result = inside + from_start[:, :, None] * carried + d_skip[None, :, None] * piece_x.astype(jnp.float32)
        return (total[:, None, None] * carry + state, result)
    start = jnp.zeros((H, P_SIZE, N), jnp.float32)
    final_state, results = lax.scan(per_span, start, (heads_x, b_rows, c_rows, steps_cut))
    scanned = results.reshape(length, inner)
    gated = scanned * jax.nn.silu(gate_part)
    normed = (gated * lax.rsqrt(lax.optimization_barrier(jnp.mean(gated * gated, axis=-1, keepdims=True)) + norm_epsilon) * norm_gain).astype(jnp.bfloat16)
    return jnp.dot(normed, w_out, preferred_element_type=jnp.float32)

def reference(tokens, hidden, base_table, w_in, w_dt, conv_w, conv_b, dt_bias, a_log, d_skip, norm_gain, w_out):
    results = []
    for slab in range(BATCH):
        looked = base_table[tokens[slab]].astype(jnp.float32)
        strand_input = (hidden[slab].astype(jnp.float32) + looked).astype(jnp.bfloat16)
        forward = mixer(strand_input, w_in, w_dt, conv_w, conv_b, dt_bias, a_log, d_skip, norm_gain, w_out)
        reverse = mixer(strand_input[::-1, ::-1], w_in, w_dt, conv_w, conv_b, dt_bias, a_log, d_skip, norm_gain, w_out)
        results.append((forward + reverse[::-1, ::-1]).astype(jnp.bfloat16))
    return jnp.stack(results)
```

```python
import jax
import jax.numpy as jnp
from jax import lax
from jax.sharding import PartitionSpec as P

H = 16
P_SIZE = 64
N = 128
Q = 256
KCONV = 4


norm_epsilon = 1e-05


def exchange(size, dtype):
    row = lax.broadcasted_iota(jnp.int32, (size, size), 0)
    col = lax.broadcasted_iota(jnp.int32, (size, size), 1)
    return (row + col == size - 1).astype(dtype)


def flip_lanes(a):
    j = exchange(a.shape[-1], a.dtype)
    return jnp.einsum("...d,de->...e", a, j, preferred_element_type=jnp.float32).astype(a.dtype)


def chain(earlier, later):
    first_decay, first_state = earlier
    next_decay, next_state = later
    return (first_decay * next_decay, next_decay[..., None, None] * first_state + next_state)


def exclusive_scans(fwd, rev, axis):
    count = lax.axis_size(axis)
    place = lax.axis_index(axis)
    seen = [None, None]
    ahead = [fwd, rev]
    shift = 1
    while shift < count:
        up = [(i, i + shift) for i in range(count - shift)]
        down = [(i + shift, i) for i in range(count - shift)]
        got = []
        for k, pairs in ((0, up), (1, down)):
            decay, state = lax.ppermute(ahead[k], axis, pairs)
            has = (place >= shift) if k == 0 else (place < count - shift)
            decay = jnp.where(has, decay, 1.0)
            got.append((decay, state))
        for k in range(2):
            seen[k] = got[k] if seen[k] is None else chain(got[k], seen[k])
            if 2 * shift < count:
                ahead[k] = chain(got[k], ahead[k])
        shift *= 2
    if seen[0] is None:
        return fwd_identity(fwd), fwd_identity(rev)
    return seen[0], seen[1]


def fwd_identity(summary):
    decay, state = summary
    return (jnp.ones_like(decay), jnp.zeros_like(state))


def block_terms(heads_x, b_rows, c_rows, step_size, rates, reverse):
    log_decay = lax.cumsum(step_size * rates, axis=2, reverse=reverse)
    end = log_decay[:, :, 0] if reverse else log_decay[:, :, -1]
    across = jnp.swapaxes(log_decay, 2, 3)
    width = across.shape[-1]
    t_idx = jnp.arange(width)[:, None]
    s_idx = jnp.arange(width)[None, :]
    keep = (s_idx >= t_idx) if reverse else (t_idx >= s_idx)
    gaps = across[..., :, None] - across[..., None, :]
    decays = jnp.where(keep, jnp.exp(jnp.where(keep, gaps, 0.0)), 0.0)
    scores = jnp.einsum("gjtn,gjsn->gjts", c_rows, b_rows, preferred_element_type=jnp.float32)
    weights = (decays * scores[:, :, None] * jnp.swapaxes(step_size, 2, 3)[:, :, :, None, :]).astype(
        jnp.bfloat16
    )
    inside = jnp.einsum("gjhts,gjshp->gjthp", weights, heads_x, preferred_element_type=jnp.float32)
    to_end = jnp.exp(end[:, :, None, :] - log_decay) * step_size
    state_weights = (b_rows.astype(jnp.float32)[..., None, :] * to_end[..., None]).astype(jnp.bfloat16)
    state = jnp.einsum("gjshp,gjshn->gjhpn", heads_x, state_weights, preferred_element_type=jnp.float32)
    return inside, state, jnp.exp(end), jnp.exp(log_decay)


def strand_terms(projected, halo, step_size, conv_w, conv_b, rates, reverse):
    inner = H * P_SIZE
    count, rows, _ = projected.shape
    margin = KCONV - 1
    source = projected[:, :, inner:]
    if reverse:
        padded = jnp.concatenate([source, halo], axis=1)
        taps = [(tap, margin - tap) for tap in range(KCONV)]
    else:
        padded = jnp.concatenate([halo, source], axis=1)
        taps = [(tap, tap) for tap in range(KCONV)]
    summed = jnp.broadcast_to(conv_b, source.shape)
    for tap, start in taps:
        summed = summed + conv_w[tap] * padded[:, start : start + rows]
    activated = jax.nn.silu(summed).astype(jnp.bfloat16)
    spans = rows // Q
    heads_x = activated[:, :, :inner].reshape(count, spans, Q, H, P_SIZE)
    b_rows = activated[:, :, inner : inner + N].reshape(count, spans, Q, N)
    c_rows = activated[:, :, inner + N :].reshape(count, spans, Q, N)
    steps_cut = step_size.reshape(count, spans, Q, H)
    inside, state, total, from_start = block_terms(
        heads_x, b_rows, c_rows, steps_cut, rates, reverse
    )
    order = list(range(spans))
    if reverse:
        order = order[::-1]
    before = {}
    sofar = (jnp.ones((count, H), jnp.float32), jnp.zeros((count, H, P_SIZE, N), jnp.float32))
    for j in order:
        before[j] = sofar
        sofar = chain(sofar, (total[:, j], state[:, j]))
    before_decay = jnp.stack([before[j][0] for j in range(spans)], axis=1)
    before_state = jnp.stack([before[j][1] for j in range(spans)], axis=1)
    pending = (before_decay, before_state, inside, from_start, heads_x, c_rows)
    return sofar, pending


def finish(pending, incoming, gate_part, d_skip, norm_gain):
    before_decay, before_state, inside, from_start, heads_x, c_rows = pending
    start_state = before_state + before_decay[..., None, None] * incoming[:, None]
    carried = jnp.einsum(
        "gjtn,gjhpn->gjthp",
        c_rows.astype(jnp.float32),
        start_state,
        precision=lax.Precision.HIGHEST,
    )
    scanned = (
        inside
        + from_start[..., None] * carried
        + d_skip[:, None] * heads_x.astype(jnp.float32)
    )
    count = scanned.shape[0]
    flat = scanned.reshape(count, -1, H * P_SIZE)
    gated = flat * jax.nn.silu(gate_part)
    return (
        gated
        * lax.rsqrt(jnp.mean(gated * gated, axis=-1, keepdims=True) + norm_epsilon)
        * norm_gain
    ).astype(jnp.bfloat16)


def on_device(
    tokens, hidden, base_table, w_in, w_dt, conv_w, conv_b, dt_bias, a_log, d_skip, norm_gain, w_out
):
    inner = H * P_SIZE
    margin = KCONV - 1
    one_hot = (tokens[:, :, None] == jnp.arange(4)[None, None, :]).astype(jnp.bfloat16)
    looked = jnp.einsum("gtb,bd->gtd", one_hot, base_table, preferred_element_type=jnp.float32)
    strand = (hidden.astype(jnp.float32) + looked).astype(jnp.bfloat16)
    rows = strand.shape[1]
    count = lax.axis_size("seq")
    low = lax.ppermute(strand[:, rows - margin :], "seq", [(i, i + 1) for i in range(count - 1)])
    high = lax.ppermute(strand[:, :margin], "seq", [(i + 1, i) for i in range(count - 1)])
    mirrored = flip_lanes(strand)
    high_mirrored = flip_lanes(high)
    w_source = w_in[:, inner:]
    proj_f = jnp.einsum("grd,de->gre", strand, w_in, preferred_element_type=jnp.float32)
    proj_r = jnp.einsum("grd,de->gre", mirrored, w_in, preferred_element_type=jnp.float32)
    halo_f = jnp.einsum("grd,de->gre", low, w_source, preferred_element_type=jnp.float32)
    halo_r = jnp.einsum("grd,de->gre", high_mirrored, w_source, preferred_element_type=jnp.float32)
    step_f = jax.nn.softplus(
        jnp.einsum("grd,dh->grh", strand, w_dt, preferred_element_type=jnp.float32) + dt_bias
    )
    step_r = jax.nn.softplus(
        jnp.einsum("grd,dh->grh", mirrored, w_dt, preferred_element_type=jnp.float32) + dt_bias
    )
    rates = -jnp.exp(a_log)
    sum_f, pend_f = strand_terms(proj_f, halo_f, step_f, conv_w, conv_b, rates, False)
    sum_r, pend_r = strand_terms(proj_r, halo_r, step_r, conv_w, conv_b, rates, True)
    in_f, in_r = exclusive_scans(sum_f, sum_r, "seq")
    normed_f = finish(pend_f, in_f[1], proj_f[:, :, :inner], d_skip, norm_gain)
    normed_r = finish(pend_r, in_r[1], proj_r[:, :, :inner], d_skip, norm_gain)
    w_out_mirrored = flip_lanes(w_out)
    out = jnp.einsum(
        "grk,kd->grd", normed_f, w_out, preferred_element_type=jnp.float32
    ) + jnp.einsum("grk,kd->grd", normed_r, w_out_mirrored, preferred_element_type=jnp.float32)
    return out.astype(jnp.bfloat16)


def solution(mesh):
    placed = (
        P(("groups", "batch"), "seq"),
        P(("groups", "batch"), "seq", None),
        P(),
        P(),
        P(),
        P(),
        P(),
        P(),
        P(),
        P(),
        P(),
        P(),
    )
    return jax.shard_map(
        on_device,
        mesh=mesh,
        in_specs=placed,
        out_specs=P(("groups", "batch"), "seq", None),
        check_vma=False,
    )
```

```python
from functools import partial

import jax
import jax.numpy as jnp
from jax import lax
from jax.experimental import pallas as pl
from jax.experimental.pallas import tpu as pltpu
from jax.sharding import PartitionSpec as P

H = 16
P_SIZE = 64
N = 128
Q = 256
KCONV = 4


norm_epsilon = 1e-05


def exchange(size, dtype):
    row = lax.broadcasted_iota(jnp.int32, (size, size), 0)
    col = lax.broadcasted_iota(jnp.int32, (size, size), 1)
    return (row + col == size - 1).astype(dtype)


def flip_lanes(a):
    j = exchange(a.shape[-1], a.dtype)
    return jnp.einsum("...d,de->...e", a, j, preferred_element_type=jnp.float32).astype(a.dtype)


def chain(earlier, later):
    first_decay, first_state = earlier
    next_decay, next_state = later
    return (first_decay * next_decay, next_decay[..., None, None] * first_state + next_state)


def exclusive_scans(fwd, rev, axis):
    count = lax.axis_size(axis)
    place = lax.axis_index(axis)
    seen = [None, None]
    ahead = [fwd, rev]
    shift = 1
    while shift < count:
        up = [(i, i + shift) for i in range(count - shift)]
        down = [(i + shift, i) for i in range(count - shift)]
        got = []
        for k, pairs in ((0, up), (1, down)):
            decay, state = lax.ppermute(ahead[k], axis, pairs)
            has = (place >= shift) if k == 0 else (place < count - shift)
            decay = jnp.where(has, decay, 1.0)
            got.append((decay, state))
        for k in range(2):
            seen[k] = got[k] if seen[k] is None else chain(got[k], seen[k])
            if 2 * shift < count:
                ahead[k] = chain(got[k], ahead[k])
        shift *= 2
    if seen[0] is None:
        return fwd_identity(fwd), fwd_identity(rev)
    return seen[0], seen[1]


def fwd_identity(summary):
    decay, state = summary
    return (jnp.ones_like(decay), jnp.zeros_like(state))


def block_kernel(xbc_ref, cum_ref, cum_t_ref, step_t_ref, to_end_ref, inside_ref, state_ref, *, reverse):
    inner = H * P_SIZE
    x_all = xbc_ref[:, :inner]
    b_rows = xbc_ref[:, inner : inner + N]
    c_rows = xbc_ref[:, inner + N :]
    scores = lax.dot_general(
        c_rows, b_rows, (((1,), (1,)), ((), ())), preferred_element_type=jnp.float32
    )
    t_idx = lax.broadcasted_iota(jnp.int32, (Q, Q), 0)
    s_idx = lax.broadcasted_iota(jnp.int32, (Q, Q), 1)
    keep = (s_idx >= t_idx) if reverse else (t_idx >= s_idx)
    b_wide = b_rows.astype(jnp.float32)
    for h in range(H):
        gaps = cum_ref[:, h : h + 1] - cum_t_ref[h : h + 1, :]
        decays = jnp.where(keep, jnp.exp(jnp.where(keep, gaps, 0.0)), 0.0)
        weights = (decays * scores * step_t_ref[h : h + 1, :]).astype(jnp.bfloat16)
        x_h = x_all[:, h * P_SIZE : (h + 1) * P_SIZE]
        inside_ref[:, h * P_SIZE : (h + 1) * P_SIZE] = jnp.dot(
            weights, x_h, preferred_element_type=jnp.float32
        )
        state_weights = (b_wide * to_end_ref[:, h : h + 1]).astype(jnp.bfloat16)
        state_ref[h] = lax.dot_general(
            x_h, state_weights, (((0,), (0,)), ((), ())), preferred_element_type=jnp.float32
        )


def block_terms(activated, step_size, rates, reverse):
    count, rows, width = activated.shape
    spans = rows // Q
    blocks = count * spans
    steps_cut = step_size.reshape(count, spans, Q, H)
    log_decay = lax.cumsum(steps_cut * rates, axis=2, reverse=reverse)
    end = log_decay[:, :, 0] if reverse else log_decay[:, :, -1]
    to_end = jnp.exp(end[:, :, None, :] - log_decay) * steps_cut
    flat = lambda a: a.reshape((blocks,) + a.shape[2:])
    cum = flat(log_decay)
    cum_t = jnp.swapaxes(cum, 1, 2)
    step_t = jnp.swapaxes(flat(steps_cut), 1, 2)
    xbc = activated.reshape(blocks, Q, width)
    spec = lambda shape: pl.BlockSpec((None,) + shape, lambda i: (i,) + (0,) * len(shape))
    inside, state = pl.pallas_call(
        partial(block_kernel, reverse=reverse),
        grid=(blocks,),
        in_specs=[spec((Q, width)), spec((Q, H)), spec((H, Q)), spec((H, Q)), spec((Q, H))],
        out_specs=[spec((Q, H * P_SIZE)), spec((H, P_SIZE, N))],
        out_shape=[
            jax.ShapeDtypeStruct((blocks, Q, H * P_SIZE), jnp.float32),
            jax.ShapeDtypeStruct((blocks, H, P_SIZE, N), jnp.float32),
        ],
    )(xbc, cum, cum_t, step_t, flat(to_end))
    inside = inside.reshape(count, rows, H * P_SIZE)
    state = state.reshape(count, spans, H, P_SIZE, N)
    return inside, state, jnp.exp(end), jnp.exp(log_decay)


def strand_terms(projected, halo, step_size, conv_w, conv_b, rates, reverse):
    inner = H * P_SIZE
    count, rows, _ = projected.shape
    margin = KCONV - 1
    source = projected[:, :, inner:]
    if reverse:
        padded = jnp.concatenate([source, halo], axis=1)
        taps = [(tap, margin - tap) for tap in range(KCONV)]
    else:
        padded = jnp.concatenate([halo, source], axis=1)
        taps = [(tap, tap) for tap in range(KCONV)]
    summed = jnp.broadcast_to(conv_b, source.shape)
    for tap, start in taps:
        summed = summed + conv_w[tap] * padded[:, start : start + rows]
    activated = jax.nn.silu(summed).astype(jnp.bfloat16)
    spans = rows // Q
    inside, state, total, from_start = block_terms(activated, step_size, rates, reverse)
    order = list(range(spans))
    if reverse:
        order = order[::-1]
    before = {}
    sofar = (jnp.ones((count, H), jnp.float32), jnp.zeros((count, H, P_SIZE, N), jnp.float32))
    for j in order:
        before[j] = sofar
        sofar = chain(sofar, (total[:, j], state[:, j]))
    before_decay = jnp.stack([before[j][0] for j in range(spans)], axis=1)
    before_state = jnp.stack([before[j][1] for j in range(spans)], axis=1)
    pending = (before_decay, before_state, inside, from_start, activated)
    return sofar, pending


def finish(pending, incoming, gate_part, d_skip, norm_gain):
    before_decay, before_state, inside, from_start, activated = pending
    inner = H * P_SIZE
    count, rows, _ = activated.shape
    spans = rows // Q
    start_state = before_state + before_decay[..., None, None] * incoming[:, None]
    c_rows = activated[:, :, inner + N :].reshape(count, spans, Q, N)
    carried = jnp.einsum(
        "gjtn,gjkn->gjtk",
        c_rows.astype(jnp.float32),
        start_state.reshape(count, spans, inner, N),
        precision=lax.Precision.HIGHEST,
    ).reshape(count, rows, inner)
    scale = jnp.repeat(from_start.reshape(count, rows, H), P_SIZE, axis=-1)
    skip = jnp.repeat(d_skip, P_SIZE)
    scanned = inside + scale * carried + skip * activated[:, :, :inner].astype(jnp.float32)
    gated = scanned * jax.nn.silu(gate_part)
    return (
        gated
        * lax.rsqrt(jnp.mean(gated * gated, axis=-1, keepdims=True) + norm_epsilon)
        * norm_gain
    ).astype(jnp.bfloat16)


def on_device(
    tokens, hidden, base_table, w_in, w_dt, conv_w, conv_b, dt_bias, a_log, d_skip, norm_gain, w_out
):
    inner = H * P_SIZE
    margin = KCONV - 1
    one_hot = (tokens[:, :, None] == jnp.arange(4)[None, None, :]).astype(jnp.bfloat16)
    looked = jnp.einsum("gtb,bd->gtd", one_hot, base_table, preferred_element_type=jnp.float32)
    strand = (hidden.astype(jnp.float32) + looked).astype(jnp.bfloat16)
    rows = strand.shape[1]
    count = lax.axis_size("seq")
    low = lax.ppermute(strand[:, rows - margin :], "seq", [(i, i + 1) for i in range(count - 1)])
    high = lax.ppermute(strand[:, :margin], "seq", [(i + 1, i) for i in range(count - 1)])
    mirrored = flip_lanes(strand)
    high_mirrored = flip_lanes(high)
    w_source = w_in[:, inner:]
    proj_f = jnp.einsum("grd,de->gre", strand, w_in, preferred_element_type=jnp.float32)
    proj_r = jnp.einsum("grd,de->gre", mirrored, w_in, preferred_element_type=jnp.float32)
    halo_f = jnp.einsum("grd,de->gre", low, w_source, preferred_element_type=jnp.float32)
    halo_r = jnp.einsum("grd,de->gre", high_mirrored, w_source, preferred_element_type=jnp.float32)
    step_f = jax.nn.softplus(
        jnp.einsum("grd,dh->grh", strand, w_dt, preferred_element_type=jnp.float32) + dt_bias
    )
    step_r = jax.nn.softplus(
        jnp.einsum("grd,dh->grh", mirrored, w_dt, preferred_element_type=jnp.float32) + dt_bias
    )
    rates = -jnp.exp(a_log)
    sum_f, pend_f = strand_terms(proj_f, halo_f, step_f, conv_w, conv_b, rates, False)
    sum_r, pend_r = strand_terms(proj_r, halo_r, step_r, conv_w, conv_b, rates, True)
    in_f, in_r = exclusive_scans(sum_f, sum_r, "seq")
    normed_f = finish(pend_f, in_f[1], proj_f[:, :, :inner], d_skip, norm_gain)
    normed_r = finish(pend_r, in_r[1], proj_r[:, :, :inner], d_skip, norm_gain)
    w_out_mirrored = flip_lanes(w_out)
    out = jnp.einsum(
        "grk,kd->grd", normed_f, w_out, preferred_element_type=jnp.float32
    ) + jnp.einsum("grk,kd->grd", normed_r, w_out_mirrored, preferred_element_type=jnp.float32)
    return out.astype(jnp.bfloat16)


def solution(mesh):
    placed = (
        P(("groups", "batch"), "seq"),
        P(("groups", "batch"), "seq", None),
        P(),
        P(),
        P(),
        P(),
        P(),
        P(),
        P(),
        P(),
        P(),
        P(),
    )
    return jax.shard_map(
        on_device,
        mesh=mesh,
        in_specs=placed,
        out_specs=P(("groups", "batch"), "seq", None),
        check_vma=False,
    )
```

```python
from functools import partial

import jax
import jax.numpy as jnp
from jax import lax
from jax.experimental import pallas as pl
from jax.experimental.pallas import tpu as pltpu
from jax.sharding import PartitionSpec as P

H = 16
P_SIZE = 64
N = 128
Q = 256
KCONV = 4


norm_epsilon = 1e-05


def exchange(size, dtype):
    row = lax.broadcasted_iota(jnp.int32, (size, size), 0)
    col = lax.broadcasted_iota(jnp.int32, (size, size), 1)
    return (row + col == size - 1).astype(dtype)


def flip_lanes(a):
    j = exchange(a.shape[-1], a.dtype)
    return jnp.einsum("...d,de->...e", a, j, preferred_element_type=jnp.float32).astype(a.dtype)


def chain(earlier, later):
    first_decay, first_state = earlier
    next_decay, next_state = later
    return (first_decay * next_decay, next_decay[..., None, None] * first_state + next_state)


def exclusive_scans(fwd, rev, axis):
    count = lax.axis_size(axis)
    place = lax.axis_index(axis)
    seen = [None, None]
    ahead = [fwd, rev]
    shift = 1
    while shift < count:
        up = [(i, i + shift) for i in range(count - shift)]
        down = [(i + shift, i) for i in range(count - shift)]
        got = []
        for k, pairs in ((0, up), (1, down)):
            decay, state = lax.ppermute(ahead[k], axis, pairs)
            has = (place >= shift) if k == 0 else (place < count - shift)
            decay = jnp.where(has, decay, 1.0)
            got.append((decay, state))
        for k in range(2):
            seen[k] = got[k] if seen[k] is None else chain(got[k], seen[k])
            if 2 * shift < count:
                ahead[k] = chain(got[k], ahead[k])
        shift *= 2
    if seen[0] is None:
        return fwd_identity(fwd), fwd_identity(rev)
    return seen[0], seen[1]


def fwd_identity(summary):
    decay, state = summary
    return (jnp.ones_like(decay), jnp.zeros_like(state))


def inside_kernel(xbc_ref, cum_ref, cum_t_ref, step_t_ref, inside_ref, *, reverse):
    inner = H * P_SIZE
    b_rows = xbc_ref[:, inner : inner + N]
    c_rows = xbc_ref[:, inner + N :]
    scores = lax.dot_general(
        c_rows, b_rows, (((1,), (1,)), ((), ())), preferred_element_type=jnp.float32
    )
    t_idx = lax.broadcasted_iota(jnp.int32, (Q, Q), 0)
    s_idx = lax.broadcasted_iota(jnp.int32, (Q, Q), 1)
    keep = (s_idx >= t_idx) if reverse else (t_idx >= s_idx)
    for h in range(H):
        gaps = cum_ref[:, h : h + 1] - cum_t_ref[h : h + 1, :]
        decays = jnp.where(keep, jnp.exp(jnp.where(keep, gaps, 0.0)), 0.0)
        weights = (decays * scores * step_t_ref[h : h + 1, :]).astype(jnp.bfloat16)
        x_h = xbc_ref[:, h * P_SIZE : (h + 1) * P_SIZE]
        inside_ref[:, h * P_SIZE : (h + 1) * P_SIZE] = jnp.dot(
            weights, x_h, preferred_element_type=jnp.float32
        )


def state_kernel(xbc_ref, to_end_ref, state_ref):
    inner = H * P_SIZE
    b_wide = xbc_ref[:, inner : inner + N].astype(jnp.float32)
    for h in range(H):
        state_weights = (b_wide * to_end_ref[:, h : h + 1]).astype(jnp.bfloat16)
        x_h = xbc_ref[:, h * P_SIZE : (h + 1) * P_SIZE]
        state_ref[h] = lax.dot_general(
            x_h, state_weights, (((0,), (0,)), ((), ())), preferred_element_type=jnp.float32
        )


def block_terms(activated, step_size, rates, reverse):
    count, rows, width = activated.shape
    spans = rows // Q
    blocks = count * spans
    steps_cut = step_size.reshape(count, spans, Q, H)
    log_decay = lax.cumsum(steps_cut * rates, axis=2, reverse=reverse)
    end = log_decay[:, :, 0] if reverse else log_decay[:, :, -1]
    to_end = jnp.exp(end[:, :, None, :] - log_decay) * steps_cut
    flat = lambda a: a.reshape((blocks,) + a.shape[2:])
    cum = flat(log_decay)
    cum_t = jnp.swapaxes(cum, 1, 2)
    step_t = jnp.swapaxes(flat(steps_cut), 1, 2)
    xbc = activated.reshape(blocks, Q, width)
    spec = lambda shape: pl.BlockSpec((None,) + shape, lambda i: (i,) + (0,) * len(shape))
    state = pl.pallas_call(
        state_kernel,
        grid=(blocks,),
        in_specs=[spec((Q, width)), spec((Q, H))],
        out_specs=spec((H, P_SIZE, N)),
        out_shape=jax.ShapeDtypeStruct((blocks, H, P_SIZE, N), jnp.float32),
    )(xbc, flat(to_end))
    inside = pl.pallas_call(
        partial(inside_kernel, reverse=reverse),
        grid=(blocks,),
        in_specs=[spec((Q, width)), spec((Q, H)), spec((H, Q)), spec((H, Q))],
        out_specs=spec((Q, H * P_SIZE)),
        out_shape=jax.ShapeDtypeStruct((blocks, Q, H * P_SIZE), jnp.float32),
    )(xbc, cum, cum_t, step_t)
    inside = inside.reshape(count, rows, H * P_SIZE)
    state = state.reshape(count, spans, H, P_SIZE, N)
    return inside, state, jnp.exp(end), jnp.exp(log_decay)


def strand_terms(projected, halo, step_size, conv_w, conv_b, rates, reverse):
    inner = H * P_SIZE
    count, rows, _ = projected.shape
    margin = KCONV - 1
    source = projected[:, :, inner:]
    if reverse:
        padded = jnp.concatenate([source, halo], axis=1)
        taps = [(tap, margin - tap) for tap in range(KCONV)]
    else:
        padded = jnp.concatenate([halo, source], axis=1)
        taps = [(tap, tap) for tap in range(KCONV)]
    summed = jnp.broadcast_to(conv_b, source.shape)
    for tap, start in taps:
        summed = summed + conv_w[tap] * padded[:, start : start + rows]
    activated = jax.nn.silu(summed).astype(jnp.bfloat16)
    spans = rows // Q
    inside, state, total, from_start = block_terms(activated, step_size, rates, reverse)
    order = list(range(spans))
    if reverse:
        order = order[::-1]
    before = {}
    sofar = (jnp.ones((count, H), jnp.float32), jnp.zeros((count, H, P_SIZE, N), jnp.float32))
    for j in order:
        before[j] = sofar
        sofar = chain(sofar, (total[:, j], state[:, j]))
    before_decay = jnp.stack([before[j][0] for j in range(spans)], axis=1)
    before_state = jnp.stack([before[j][1] for j in range(spans)], axis=1)
    pending = (before_decay, before_state, inside, from_start, activated)
    return sofar, pending


def finish(pending, incoming, gate_part, d_skip, norm_gain):
    before_decay, before_state, inside, from_start, activated = pending
    inner = H * P_SIZE
    count, rows, _ = activated.shape
    spans = rows // Q
    start_state = before_state + before_decay[..., None, None] * incoming[:, None]
    c_rows = activated[:, :, inner + N :].reshape(count, spans, Q, N)
    carried = jnp.einsum(
        "gjtn,gjkn->gjtk",
        c_rows.astype(jnp.float32),
        start_state.reshape(count, spans, inner, N),
        precision=lax.Precision.HIGHEST,
    ).reshape(count, rows, inner)
    scale = jnp.repeat(from_start.reshape(count, rows, H), P_SIZE, axis=-1)
    skip = jnp.repeat(d_skip, P_SIZE)
    scanned = inside + scale * carried + skip * activated[:, :, :inner].astype(jnp.float32)
    gated = scanned * jax.nn.silu(gate_part)
    return (
        gated
        * lax.rsqrt(jnp.mean(gated * gated, axis=-1, keepdims=True) + norm_epsilon)
        * norm_gain
    ).astype(jnp.bfloat16)


def on_device(
    tokens, hidden, base_table, w_in, w_dt, conv_w, conv_b, dt_bias, a_log, d_skip, norm_gain, w_out
):
    inner = H * P_SIZE
    margin = KCONV - 1
    one_hot = (tokens[:, :, None] == jnp.arange(4)[None, None, :]).astype(jnp.bfloat16)
    looked = jnp.einsum("gtb,bd->gtd", one_hot, base_table, preferred_element_type=jnp.float32)
    strand = (hidden.astype(jnp.float32) + looked).astype(jnp.bfloat16)
    rows = strand.shape[1]
    count = lax.axis_size("seq")
    low = lax.ppermute(strand[:, rows - margin :], "seq", [(i, i + 1) for i in range(count - 1)])
    high = lax.ppermute(strand[:, :margin], "seq", [(i + 1, i) for i in range(count - 1)])
    mirrored = flip_lanes(strand)
    high_mirrored = flip_lanes(high)
    w_source = w_in[:, inner:]
    proj_f = jnp.einsum("grd,de->gre", strand, w_in, preferred_element_type=jnp.float32)
    proj_r = jnp.einsum("grd,de->gre", mirrored, w_in, preferred_element_type=jnp.float32)
    halo_f = jnp.einsum("grd,de->gre", low, w_source, preferred_element_type=jnp.float32)
    halo_r = jnp.einsum("grd,de->gre", high_mirrored, w_source, preferred_element_type=jnp.float32)
    step_f = jax.nn.softplus(
        jnp.einsum("grd,dh->grh", strand, w_dt, preferred_element_type=jnp.float32) + dt_bias
    )
    step_r = jax.nn.softplus(
        jnp.einsum("grd,dh->grh", mirrored, w_dt, preferred_element_type=jnp.float32) + dt_bias
    )
    rates = -jnp.exp(a_log)
    sum_f, pend_f = strand_terms(proj_f, halo_f, step_f, conv_w, conv_b, rates, False)
    sum_r, pend_r = strand_terms(proj_r, halo_r, step_r, conv_w, conv_b, rates, True)
    in_f, in_r = exclusive_scans(sum_f, sum_r, "seq")
    normed_f = finish(pend_f, in_f[1], proj_f[:, :, :inner], d_skip, norm_gain)
    normed_r = finish(pend_r, in_r[1], proj_r[:, :, :inner], d_skip, norm_gain)
    w_out_mirrored = flip_lanes(w_out)
    out = jnp.einsum(
        "grk,kd->grd", normed_f, w_out, preferred_element_type=jnp.float32
    ) + jnp.einsum("grk,kd->grd", normed_r, w_out_mirrored, preferred_element_type=jnp.float32)
    return out.astype(jnp.bfloat16)


def solution(mesh):
    placed = (
        P(("groups", "batch"), "seq"),
        P(("groups", "batch"), "seq", None),
        P(),
        P(),
        P(),
        P(),
        P(),
        P(),
        P(),
        P(),
        P(),
        P(),
    )
    return jax.shard_map(
        on_device,
        mesh=mesh,
        in_specs=placed,
        out_specs=P(("groups", "batch"), "seq", None),
        check_vma=False,
    )
```

```python
from functools import partial

import jax
import jax.numpy as jnp
from jax import lax
from jax.experimental import pallas as pl
from jax.experimental.pallas import tpu as pltpu
from jax.sharding import PartitionSpec as P

H = 16
P_SIZE = 64
N = 128
Q = 256
KCONV = 4


norm_epsilon = 1e-05


def exchange(size, dtype):
    row = lax.broadcasted_iota(jnp.int32, (size, size), 0)
    col = lax.broadcasted_iota(jnp.int32, (size, size), 1)
    return (row + col == size - 1).astype(dtype)


def flip_lanes(a):
    j = exchange(a.shape[-1], a.dtype)
    return jnp.einsum("...d,de->...e", a, j, preferred_element_type=jnp.float32).astype(a.dtype)


def chain(earlier, later):
    first_decay, first_state = earlier
    next_decay, next_state = later
    return (first_decay * next_decay, next_decay[..., None, None] * first_state + next_state)


def exclusive_scans(fwd, rev, axis):
    count = lax.axis_size(axis)
    place = lax.axis_index(axis)
    seen = [None, None]
    ahead = [fwd, rev]
    shift = 1
    while shift < count:
        up = [(i, i + shift) for i in range(count - shift)]
        down = [(i + shift, i) for i in range(count - shift)]
        got = []
        for k, pairs in ((0, up), (1, down)):
            decay, state = unpack(lax.ppermute(pack(*ahead[k]), axis, pairs))
            has = (place >= shift) if k == 0 else (place < count - shift)
            decay = jnp.where(has, decay, 1.0)
            got.append((decay, state))
        for k in range(2):
            seen[k] = got[k] if seen[k] is None else chain(got[k], seen[k])
            if 2 * shift < count:
                ahead[k] = chain(got[k], ahead[k])
        shift *= 2
    if seen[0] is None:
        return fwd_identity(fwd), fwd_identity(rev)
    return seen[0], seen[1]


def pack(decay, state):
    extra = jnp.broadcast_to(decay[:, :, None, None], decay.shape + (8, state.shape[-1]))
    return jnp.concatenate([state, extra], axis=2)


def unpack(packed):
    return packed[:, :, P_SIZE, 0], packed[:, :, :P_SIZE]


def fwd_identity(summary):
    decay, state = summary
    return (jnp.ones_like(decay), jnp.zeros_like(state))


def inside_kernel(xbc_ref, cum_ref, cum_t_ref, step_t_ref, inside_ref, *, reverse):
    inner = H * P_SIZE
    b_rows = xbc_ref[:, inner : inner + N]
    c_rows = xbc_ref[:, inner + N :]
    scores = lax.dot_general(
        c_rows, b_rows, (((1,), (1,)), ((), ())), preferred_element_type=jnp.float32
    )
    t_idx = lax.broadcasted_iota(jnp.int32, (Q, Q), 0)
    s_idx = lax.broadcasted_iota(jnp.int32, (Q, Q), 1)
    keep = (s_idx >= t_idx) if reverse else (t_idx >= s_idx)
    for h in range(H):
        gaps = cum_ref[:, h : h + 1] - cum_t_ref[h : h + 1, :]
        decays = jnp.where(keep, jnp.exp(jnp.where(keep, gaps, 0.0)), 0.0)
        weights = (decays * scores * step_t_ref[h : h + 1, :]).astype(jnp.bfloat16)
        x_h = xbc_ref[:, h * P_SIZE : (h + 1) * P_SIZE]
        inside_ref[:, h * P_SIZE : (h + 1) * P_SIZE] = jnp.dot(
            weights, x_h, preferred_element_type=jnp.float32
        )


def state_kernel(xbc_ref, to_end_ref, state_ref):
    inner = H * P_SIZE
    b_wide = xbc_ref[:, inner : inner + N].astype(jnp.float32)
    for h in range(H):
        state_weights = (b_wide * to_end_ref[:, h : h + 1]).astype(jnp.bfloat16)
        x_h = xbc_ref[:, h * P_SIZE : (h + 1) * P_SIZE]
        state_ref[h] = lax.dot_general(
            x_h, state_weights, (((0,), (0,)), ((), ())), preferred_element_type=jnp.float32
        )


def block_terms(activated, step_size, rates, reverse):
    count, rows, width = activated.shape
    spans = rows // Q
    blocks = count * spans
    steps_cut = step_size.reshape(count, spans, Q, H)
    log_decay = lax.cumsum(steps_cut * rates, axis=2, reverse=reverse)
    end = log_decay[:, :, 0] if reverse else log_decay[:, :, -1]
    to_end = jnp.exp(end[:, :, None, :] - log_decay) * steps_cut
    flat = lambda a: a.reshape((blocks,) + a.shape[2:])
    cum = flat(log_decay)
    cum_t = jnp.swapaxes(cum, 1, 2)
    step_t = jnp.swapaxes(flat(steps_cut), 1, 2)
    xbc = activated.reshape(blocks, Q, width)
    spec = lambda shape: pl.BlockSpec((None,) + shape, lambda i: (i,) + (0,) * len(shape))
    state = pl.pallas_call(
        state_kernel,
        grid=(blocks,),
        in_specs=[spec((Q, width)), spec((Q, H))],
        out_specs=spec((H, P_SIZE, N)),
        out_shape=jax.ShapeDtypeStruct((blocks, H, P_SIZE, N), jnp.float32),
    )(xbc, flat(to_end))
    inside = pl.pallas_call(
        partial(inside_kernel, reverse=reverse),
        grid=(blocks,),
        in_specs=[spec((Q, width)), spec((Q, H)), spec((H, Q)), spec((H, Q))],
        out_specs=spec((Q, H * P_SIZE)),
        out_shape=jax.ShapeDtypeStruct((blocks, Q, H * P_SIZE), jnp.float32),
    )(xbc, cum, cum_t, step_t)
    inside = inside.reshape(count, rows, H * P_SIZE)
    state = state.reshape(count, spans, H, P_SIZE, N)
    return inside, state, jnp.exp(end), jnp.exp(log_decay)


def strand_terms(projected, halo, step_size, conv_w, conv_b, rates, reverse):
    inner = H * P_SIZE
    count, rows, _ = projected.shape
    margin = KCONV - 1
    source = projected[:, :, inner:]
    if reverse:
        padded = jnp.concatenate([source, halo], axis=1)
        taps = [(tap, margin - tap) for tap in range(KCONV)]
    else:
        padded = jnp.concatenate([halo, source], axis=1)
        taps = [(tap, tap) for tap in range(KCONV)]
    summed = jnp.broadcast_to(conv_b, source.shape)
    for tap, start in taps:
        summed = summed + conv_w[tap] * padded[:, start : start + rows]
    activated = jax.nn.silu(summed).astype(jnp.bfloat16)
    spans = rows // Q
    inside, state, total, from_start = block_terms(activated, step_size, rates, reverse)
    order = list(range(spans))
    if reverse:
        order = order[::-1]
    before = {}
    sofar = (jnp.ones((count, H), jnp.float32), jnp.zeros((count, H, P_SIZE, N), jnp.float32))
    for j in order:
        before[j] = sofar
        sofar = chain(sofar, (total[:, j], state[:, j]))
    before_decay = jnp.stack([before[j][0] for j in range(spans)], axis=1)
    before_state = jnp.stack([before[j][1] for j in range(spans)], axis=1)
    pending = (before_decay, before_state, inside, from_start, activated)
    return sofar, pending


def finish(pending, incoming, gate_part, d_skip, norm_gain):
    before_decay, before_state, inside, from_start, activated = pending
    inner = H * P_SIZE
    count, rows, _ = activated.shape
    spans = rows // Q
    start_state = before_state + before_decay[..., None, None] * incoming[:, None]
    c_rows = activated[:, :, inner + N :].reshape(count, spans, Q, N)
    carried = jnp.einsum(
        "gjtn,gjkn->gjtk",
        c_rows.astype(jnp.float32),
        start_state.reshape(count, spans, inner, N),
        precision=lax.Precision.HIGHEST,
    ).reshape(count, rows, inner)
    scale = jnp.repeat(from_start.reshape(count, rows, H), P_SIZE, axis=-1)
    skip = jnp.repeat(d_skip, P_SIZE)
    scanned = inside + scale * carried + skip * activated[:, :, :inner].astype(jnp.float32)
    gated = scanned * jax.nn.silu(gate_part)
    return (
        gated
        * lax.rsqrt(jnp.mean(gated * gated, axis=-1, keepdims=True) + norm_epsilon)
        * norm_gain
    ).astype(jnp.bfloat16)


def on_device(
    tokens, hidden, base_table, w_in, w_dt, conv_w, conv_b, dt_bias, a_log, d_skip, norm_gain, w_out
):
    inner = H * P_SIZE
    margin = KCONV - 1
    one_hot = (tokens[:, :, None] == jnp.arange(4)[None, None, :]).astype(jnp.bfloat16)
    looked = jnp.einsum("gtb,bd->gtd", one_hot, base_table, preferred_element_type=jnp.float32)
    strand = (hidden.astype(jnp.float32) + looked).astype(jnp.bfloat16)
    rows = strand.shape[1]
    count = lax.axis_size("seq")
    low = lax.ppermute(strand[:, rows - margin :], "seq", [(i, i + 1) for i in range(count - 1)])
    high = lax.ppermute(strand[:, :margin], "seq", [(i + 1, i) for i in range(count - 1)])
    mirrored = flip_lanes(strand)
    high_mirrored = flip_lanes(high)
    w_source = w_in[:, inner:]
    proj_f = jnp.einsum("grd,de->gre", strand, w_in, preferred_element_type=jnp.float32)
    proj_r = jnp.einsum("grd,de->gre", mirrored, w_in, preferred_element_type=jnp.float32)
    halo_f = jnp.einsum("grd,de->gre", low, w_source, preferred_element_type=jnp.float32)
    halo_r = jnp.einsum("grd,de->gre", high_mirrored, w_source, preferred_element_type=jnp.float32)
    step_f = jax.nn.softplus(
        jnp.einsum("grd,dh->grh", strand, w_dt, preferred_element_type=jnp.float32) + dt_bias
    )
    step_r = jax.nn.softplus(
        jnp.einsum("grd,dh->grh", mirrored, w_dt, preferred_element_type=jnp.float32) + dt_bias
    )
    rates = -jnp.exp(a_log)
    sum_f, pend_f = strand_terms(proj_f, halo_f, step_f, conv_w, conv_b, rates, False)
    sum_r, pend_r = strand_terms(proj_r, halo_r, step_r, conv_w, conv_b, rates, True)
    in_f, in_r = exclusive_scans(sum_f, sum_r, "seq")
    normed_f = finish(pend_f, in_f[1], proj_f[:, :, :inner], d_skip, norm_gain)
    normed_r = finish(pend_r, in_r[1], proj_r[:, :, :inner], d_skip, norm_gain)
    w_out_mirrored = flip_lanes(w_out)
    out = jnp.einsum(
        "grk,kd->grd", normed_f, w_out, preferred_element_type=jnp.float32
    ) + jnp.einsum("grk,kd->grd", normed_r, w_out_mirrored, preferred_element_type=jnp.float32)
    return out.astype(jnp.bfloat16)


def solution(mesh):
    placed = (
        P(("groups", "batch"), "seq"),
        P(("groups", "batch"), "seq", None),
        P(),
        P(),
        P(),
        P(),
        P(),
        P(),
        P(),
        P(),
        P(),
        P(),
    )
    return jax.shard_map(
        on_device,
        mesh=mesh,
        in_specs=placed,
        out_specs=P(("groups", "batch"), "seq", None),
        check_vma=False,
    )
```

```python
from functools import partial

import jax
import jax.numpy as jnp
from jax import lax
from jax.experimental import pallas as pl
from jax.experimental.pallas import tpu as pltpu
from jax.sharding import PartitionSpec as P

H = 16
P_SIZE = 64
N = 128
Q = 256
KCONV = 4


norm_epsilon = 1e-05


def exchange(size, dtype):
    row = lax.broadcasted_iota(jnp.int32, (size, size), 0)
    col = lax.broadcasted_iota(jnp.int32, (size, size), 1)
    return (row + col == size - 1).astype(dtype)


def flip_lanes(a):
    j = exchange(a.shape[-1], a.dtype)
    return jnp.einsum("...d,de->...e", a, j, preferred_element_type=jnp.float32).astype(a.dtype)


def chain(earlier, later):
    first_decay, first_state = earlier
    next_decay, next_state = later
    return (first_decay * next_decay, next_decay[..., None, None] * first_state + next_state)


def exclusive_scans(fwd, rev, axis):
    count = lax.axis_size(axis)
    place = lax.axis_index(axis)
    seen = [None, None]
    ahead = [fwd, rev]
    shift = 1
    while shift < count:
        up = [(i, i + shift) for i in range(count - shift)]
        down = [(i + shift, i) for i in range(count - shift)]
        got = []
        for k, pairs in ((0, up), (1, down)):
            decay, state = unpack(lax.ppermute(pack(*ahead[k]), axis, pairs))
            has = (place >= shift) if k == 0 else (place < count - shift)
            decay = jnp.where(has, decay, 1.0)
            got.append((decay, state))
        for k in range(2):
            seen[k] = got[k] if seen[k] is None else chain(got[k], seen[k])
            if 2 * shift < count:
                ahead[k] = chain(got[k], ahead[k])
        shift *= 2
    if seen[0] is None:
        return fwd_identity(fwd), fwd_identity(rev)
    return seen[0], seen[1]


def pack(decay, state):
    extra = jnp.broadcast_to(decay[:, :, None, None], decay.shape + (8, state.shape[-1]))
    return jnp.concatenate([state, extra], axis=2)


def unpack(packed):
    return packed[:, :, P_SIZE, 0], packed[:, :, :P_SIZE]


def fwd_identity(summary):
    decay, state = summary
    return (jnp.ones_like(decay), jnp.zeros_like(state))


def inside_kernel(xbc_ref, cum_ref, cum_t_ref, step_t_ref, inside_ref, *, reverse):
    inner = H * P_SIZE
    b_rows = xbc_ref[:, inner : inner + N]
    c_rows = xbc_ref[:, inner + N :]
    scores = lax.dot_general(
        c_rows, b_rows, (((1,), (1,)), ((), ())), preferred_element_type=jnp.float32
    )
    t_idx = lax.broadcasted_iota(jnp.int32, (Q, Q), 0)
    s_idx = lax.broadcasted_iota(jnp.int32, (Q, Q), 1)
    keep = (s_idx >= t_idx) if reverse else (t_idx >= s_idx)
    for h in range(H):
        gaps = cum_ref[:, h : h + 1] - cum_t_ref[h : h + 1, :]
        decays = jnp.where(keep, jnp.exp(jnp.where(keep, gaps, 0.0)), 0.0)
        weights = (decays * scores * step_t_ref[h : h + 1, :]).astype(jnp.bfloat16)
        x_h = xbc_ref[:, h * P_SIZE : (h + 1) * P_SIZE]
        inside_ref[:, h * P_SIZE : (h + 1) * P_SIZE] = jnp.dot(
            weights, x_h, preferred_element_type=jnp.float32
        )


def state_kernel(xbc_ref, to_end_ref, state_ref):
    inner = H * P_SIZE
    b_wide = xbc_ref[:, inner : inner + N].astype(jnp.float32)
    for h in range(H):
        state_weights = (b_wide * to_end_ref[:, h : h + 1]).astype(jnp.bfloat16)
        x_h = xbc_ref[:, h * P_SIZE : (h + 1) * P_SIZE]
        state_ref[h] = lax.dot_general(
            x_h, state_weights, (((0,), (0,)), ((), ())), preferred_element_type=jnp.float32
        )


def block_terms(activated, step_size, rates, reverse):
    count, rows, width = activated.shape
    spans = rows // Q
    blocks = count * spans
    steps_cut = step_size.reshape(count, spans, Q, H)
    rated = steps_cut * rates
    log_decay = jnp.cumsum(rated, axis=2)
    if reverse:
        log_decay = log_decay[:, :, -1:] - log_decay + rated
    end = log_decay[:, :, 0] if reverse else log_decay[:, :, -1]
    to_end = jnp.exp(end[:, :, None, :] - log_decay) * steps_cut
    flat = lambda a: a.reshape((blocks,) + a.shape[2:])
    cum = flat(log_decay)
    cum_t = jnp.swapaxes(cum, 1, 2)
    step_t = jnp.swapaxes(flat(steps_cut), 1, 2)
    xbc = activated.reshape(blocks, Q, width)
    spec = lambda shape: pl.BlockSpec((None,) + shape, lambda i: (i,) + (0,) * len(shape))
    state = pl.pallas_call(
        state_kernel,
        grid=(blocks,),
        in_specs=[spec((Q, width)), spec((Q, H))],
        out_specs=spec((H, P_SIZE, N)),
        out_shape=jax.ShapeDtypeStruct((blocks, H, P_SIZE, N), jnp.float32),
    )(xbc, flat(to_end))
    inside = pl.pallas_call(
        partial(inside_kernel, reverse=reverse),
        grid=(blocks,),
        in_specs=[spec((Q, width)), spec((Q, H)), spec((H, Q)), spec((H, Q))],
        out_specs=spec((Q, H * P_SIZE)),
        out_shape=jax.ShapeDtypeStruct((blocks, Q, H * P_SIZE), jnp.float32),
    )(xbc, cum, cum_t, step_t)
    inside = inside.reshape(count, rows, H * P_SIZE)
    state = state.reshape(count, spans, H, P_SIZE, N)
    return inside, state, jnp.exp(end), jnp.exp(log_decay)


CONV_LANES = 256


def conv_kernel(src_ref, halo_ref, w_ref, b_ref, out_ref, *, reverse):
    margin = KCONV - 1
    src = src_ref[...]
    rows = src.shape[0]
    edge = halo_ref.shape[0]
    w = w_ref[...]
    if reverse:
        near = jnp.concatenate([src[rows - edge :], halo_ref[...]], axis=0)
    else:
        near = jnp.concatenate([halo_ref[...], src[:edge]], axis=0)
    span = near.shape[0]
    main = jnp.broadcast_to(b_ref[...], src.shape)
    side = jnp.broadcast_to(b_ref[...], (edge, src.shape[1]))
    for tap in range(KCONV):
        shift = margin - tap
        if shift == 0:
            piece, near_piece = src, near
        elif reverse:
            piece = pltpu.roll(src, rows - shift, 0)
            near_piece = pltpu.roll(near, span - shift, 0)
        else:
            piece = pltpu.roll(src, shift, 0)
            near_piece = pltpu.roll(near, shift, 0)
        main = main + w[tap : tap + 1] * piece
        part = near_piece[:edge] if reverse else near_piece[edge:]
        side = side + w[tap : tap + 1] * part
    out_ref[...] = jax.nn.silu(main).astype(out_ref.dtype)
    if reverse:
        out_ref[rows - edge :, :] = jax.nn.silu(side).astype(out_ref.dtype)
    else:
        out_ref[:edge, :] = jax.nn.silu(side).astype(out_ref.dtype)


def convolve(projected, halo, conv_w, conv_b, reverse):
    inner = H * P_SIZE
    count, rows, _ = projected.shape
    width = conv_w.shape[1]
    edge = 8
    margin = KCONV - 1
    pad = ((0, 0), (0, edge - margin), (0, 0)) if reverse else ((0, 0), (edge - margin, 0), (0, 0))
    halo8 = jnp.pad(halo, pad)
    lanes = CONV_LANES
    skip = inner // lanes
    return pl.pallas_call(
        partial(conv_kernel, reverse=reverse),
        grid=(count, width // lanes),
        in_specs=[
            pl.BlockSpec((None, rows, lanes), lambda g, j: (g, 0, j + skip)),
            pl.BlockSpec((None, edge, lanes), lambda g, j: (g, 0, j)),
            pl.BlockSpec((KCONV, lanes), lambda g, j: (0, j)),
            pl.BlockSpec((1, lanes), lambda g, j: (0, j)),
        ],
        out_specs=pl.BlockSpec((None, rows, lanes), lambda g, j: (g, 0, j)),
        out_shape=jax.ShapeDtypeStruct((count, rows, width), jnp.bfloat16),
    )(projected, halo8, conv_w, conv_b.reshape(1, width))


def strand_terms(projected, halo, step_size, conv_w, conv_b, rates, reverse):
    inner = H * P_SIZE
    count, rows, _ = projected.shape
    activated = convolve(projected, halo, conv_w, conv_b, reverse)
    spans = rows // Q
    inside, state, total, from_start = block_terms(activated, step_size, rates, reverse)
    order = list(range(spans))
    if reverse:
        order = order[::-1]
    before = {}
    sofar = (jnp.ones((count, H), jnp.float32), jnp.zeros((count, H, P_SIZE, N), jnp.float32))
    for j in order:
        before[j] = sofar
        sofar = chain(sofar, (total[:, j], state[:, j]))
    before_decay = jnp.stack([before[j][0] for j in range(spans)], axis=1)
    before_state = jnp.stack([before[j][1] for j in range(spans)], axis=1)
    pending = (before_decay, before_state, inside, from_start, activated)
    return sofar, pending


def finish(pending, incoming, gate_part, d_skip, norm_gain):
    before_decay, before_state, inside, from_start, activated = pending
    inner = H * P_SIZE
    count, rows, _ = activated.shape
    spans = rows // Q
    start_state = before_state + before_decay[..., None, None] * incoming[:, None]
    c_rows = activated[:, :, inner + N :].reshape(count, spans, Q, N)
    carried = jnp.einsum(
        "gjtn,gjkn->gjtk",
        c_rows.astype(jnp.float32),
        start_state.reshape(count, spans, inner, N),
        precision=lax.Precision.HIGHEST,
    ).reshape(count, rows, inner)
    scale = jnp.repeat(from_start.reshape(count, rows, H), P_SIZE, axis=-1)
    skip = jnp.repeat(d_skip, P_SIZE)
    scanned = inside + scale * carried + skip * activated[:, :, :inner].astype(jnp.float32)
    gated = scanned * jax.nn.silu(gate_part)
    return (
        gated
        * lax.rsqrt(jnp.mean(gated * gated, axis=-1, keepdims=True) + norm_epsilon)
        * norm_gain
    ).astype(jnp.bfloat16)


def on_device(
    tokens, hidden, base_table, w_in, w_dt, conv_w, conv_b, dt_bias, a_log, d_skip, norm_gain, w_out
):
    inner = H * P_SIZE
    margin = KCONV - 1
    one_hot = (tokens[:, :, None] == jnp.arange(4)[None, None, :]).astype(jnp.bfloat16)
    looked = jnp.einsum("gtb,bd->gtd", one_hot, base_table, preferred_element_type=jnp.float32)
    strand = (hidden.astype(jnp.float32) + looked).astype(jnp.bfloat16)
    rows = strand.shape[1]
    count = lax.axis_size("seq")
    low = lax.ppermute(strand[:, rows - margin :], "seq", [(i, i + 1) for i in range(count - 1)])
    high = lax.ppermute(strand[:, :margin], "seq", [(i + 1, i) for i in range(count - 1)])
    mirrored = flip_lanes(strand)
    high_mirrored = flip_lanes(high)
    w_source = w_in[:, inner:]
    proj_f = jnp.einsum("grd,de->gre", strand, w_in, preferred_element_type=jnp.float32)
    proj_r = jnp.einsum("grd,de->gre", mirrored, w_in, preferred_element_type=jnp.float32)
    halo_f = jnp.einsum("grd,de->gre", low, w_source, preferred_element_type=jnp.float32)
    halo_r = jnp.einsum("grd,de->gre", high_mirrored, w_source, preferred_element_type=jnp.float32)
    step_f = jax.nn.softplus(
        jnp.einsum("grd,dh->grh", strand, w_dt, preferred_element_type=jnp.float32) + dt_bias
    )
    step_r = jax.nn.softplus(
        jnp.einsum("grd,dh->grh", mirrored, w_dt, preferred_element_type=jnp.float32) + dt_bias
    )
    rates = -jnp.exp(a_log)
    sum_f, pend_f = strand_terms(proj_f, halo_f, step_f, conv_w, conv_b, rates, False)
    sum_r, pend_r = strand_terms(proj_r, halo_r, step_r, conv_w, conv_b, rates, True)
    in_f, in_r = exclusive_scans(sum_f, sum_r, "seq")
    normed_f = finish(pend_f, in_f[1], proj_f[:, :, :inner], d_skip, norm_gain)
    normed_r = finish(pend_r, in_r[1], proj_r[:, :, :inner], d_skip, norm_gain)
    w_out_mirrored = flip_lanes(w_out)
    out = jnp.einsum(
        "grk,kd->grd", normed_f, w_out, preferred_element_type=jnp.float32
    ) + jnp.einsum("grk,kd->grd", normed_r, w_out_mirrored, preferred_element_type=jnp.float32)
    return out.astype(jnp.bfloat16)


def solution(mesh):
    placed = (
        P(("groups", "batch"), "seq"),
        P(("groups", "batch"), "seq", None),
        P(),
        P(),
        P(),
        P(),
        P(),
        P(),
        P(),
        P(),
        P(),
        P(),
    )
    return jax.shard_map(
        on_device,
        mesh=mesh,
        in_specs=placed,
        out_specs=P(("groups", "batch"), "seq", None),
        check_vma=False,
    )
```

```python
from functools import partial

import jax
import jax.numpy as jnp
from jax import lax
from jax.experimental import pallas as pl
from jax.experimental.pallas import tpu as pltpu
from jax.sharding import PartitionSpec as P

H = 16
P_SIZE = 64
N = 128
Q = 256
KCONV = 4


norm_epsilon = 1e-05


def exchange(size, dtype):
    row = lax.broadcasted_iota(jnp.int32, (size, size), 0)
    col = lax.broadcasted_iota(jnp.int32, (size, size), 1)
    return (row + col == size - 1).astype(dtype)


def flip_lanes(a):
    j = exchange(a.shape[-1], a.dtype)
    return jnp.einsum("...d,de->...e", a, j, preferred_element_type=jnp.float32).astype(a.dtype)


def chain(earlier, later):
    first_decay, first_state = earlier
    next_decay, next_state = later
    return (first_decay * next_decay, next_decay[..., None, None] * first_state + next_state)


def exclusive_scans(fwd, rev, axis):
    count = lax.axis_size(axis)
    place = lax.axis_index(axis)
    seen = [None, None]
    ahead = [fwd, rev]
    shift = 1
    while shift < count:
        up = [(i, i + shift) for i in range(count - shift)]
        down = [(i + shift, i) for i in range(count - shift)]
        got = []
        for k, pairs in ((0, up), (1, down)):
            decay, state = unpack(lax.ppermute(pack(*ahead[k]), axis, pairs))
            has = (place >= shift) if k == 0 else (place < count - shift)
            decay = jnp.where(has, decay, 1.0)
            got.append((decay, state))
        for k in range(2):
            seen[k] = got[k] if seen[k] is None else chain(got[k], seen[k])
            if 2 * shift < count:
                ahead[k] = chain(got[k], ahead[k])
        shift *= 2
    if seen[0] is None:
        return fwd_identity(fwd), fwd_identity(rev)
    return seen[0], seen[1]


def pack(decay, state):
    extra = jnp.broadcast_to(decay[:, :, None, None], decay.shape + (8, state.shape[-1]))
    return jnp.concatenate([state, extra], axis=2)


def unpack(packed):
    return packed[:, :, P_SIZE, 0], packed[:, :, :P_SIZE]


def fwd_identity(summary):
    decay, state = summary
    return (jnp.ones_like(decay), jnp.zeros_like(state))


def inside_kernel(xbc_ref, cum_ref, cum_t_ref, step_t_ref, inside_ref, *, reverse):
    inner = H * P_SIZE
    b_rows = xbc_ref[:, inner : inner + N]
    c_rows = xbc_ref[:, inner + N :]
    scores = lax.dot_general(
        c_rows, b_rows, (((1,), (1,)), ((), ())), preferred_element_type=jnp.float32
    )
    t_idx = lax.broadcasted_iota(jnp.int32, (Q, Q), 0)
    s_idx = lax.broadcasted_iota(jnp.int32, (Q, Q), 1)
    keep = (s_idx >= t_idx) if reverse else (t_idx >= s_idx)
    for h in range(H):
        gaps = cum_ref[:, h : h + 1] - cum_t_ref[h : h + 1, :]
        decays = jnp.where(keep, jnp.exp(jnp.where(keep, gaps, 0.0)), 0.0)
        weights = (decays * scores * step_t_ref[h : h + 1, :]).astype(jnp.bfloat16)
        x_h = xbc_ref[:, h * P_SIZE : (h + 1) * P_SIZE]
        inside_ref[:, h * P_SIZE : (h + 1) * P_SIZE] = jnp.dot(
            weights, x_h, preferred_element_type=jnp.float32
        )


def state_kernel(xbc_ref, to_end_ref, state_ref):
    inner = H * P_SIZE
    b_wide = xbc_ref[:, inner : inner + N].astype(jnp.float32)
    for h in range(H):
        state_weights = (b_wide * to_end_ref[:, h : h + 1]).astype(jnp.bfloat16)
        x_h = xbc_ref[:, h * P_SIZE : (h + 1) * P_SIZE]
        state_ref[h] = lax.dot_general(
            x_h, state_weights, (((0,), (0,)), ((), ())), preferred_element_type=jnp.float32
        )


def block_terms(activated, step_size, rates, reverse):
    count, rows, width = activated.shape
    spans = rows // Q
    blocks = count * spans
    steps_cut = step_size.reshape(count, spans, Q, H)
    rated = steps_cut * rates
    log_decay = jnp.cumsum(rated, axis=2)
    if reverse:
        log_decay = log_decay[:, :, -1:] - log_decay + rated
    end = log_decay[:, :, 0] if reverse else log_decay[:, :, -1]
    to_end = jnp.exp(end[:, :, None, :] - log_decay) * steps_cut
    flat = lambda a: a.reshape((blocks,) + a.shape[2:])
    cum = flat(log_decay)
    cum_t = jnp.swapaxes(cum, 1, 2)
    step_t = jnp.swapaxes(flat(steps_cut), 1, 2)
    xbc = activated.reshape(blocks, Q, width)
    spec = lambda shape: pl.BlockSpec((None,) + shape, lambda i: (i,) + (0,) * len(shape))
    state = pl.pallas_call(
        state_kernel,
        grid=(blocks,),
        in_specs=[spec((Q, width)), spec((Q, H))],
        out_specs=spec((H, P_SIZE, N)),
        out_shape=jax.ShapeDtypeStruct((blocks, H, P_SIZE, N), jnp.float32),
    )(xbc, flat(to_end))
    inside = pl.pallas_call(
        partial(inside_kernel, reverse=reverse),
        grid=(blocks,),
        in_specs=[spec((Q, width)), spec((Q, H)), spec((H, Q)), spec((H, Q))],
        out_specs=spec((Q, H * P_SIZE)),
        out_shape=jax.ShapeDtypeStruct((blocks, Q, H * P_SIZE), jnp.float32),
    )(xbc, cum, cum_t, step_t)
    inside = inside.reshape(count, rows, H * P_SIZE)
    state = state.reshape(count, spans, H, P_SIZE, N)
    return inside, state, jnp.exp(end), jnp.exp(log_decay)


CONV_LANES = 256


def conv_kernel(src_ref, halo_ref, w_ref, b_ref, out_ref, *, reverse):
    margin = KCONV - 1
    src = src_ref[...]
    rows = src.shape[0]
    edge = halo_ref.shape[0]
    w = w_ref[...]
    if reverse:
        near = jnp.concatenate([src[rows - edge :], halo_ref[...]], axis=0)
    else:
        near = jnp.concatenate([halo_ref[...], src[:edge]], axis=0)
    span = near.shape[0]
    main = jnp.broadcast_to(b_ref[...], src.shape)
    side = jnp.broadcast_to(b_ref[...], (edge, src.shape[1]))
    for tap in range(KCONV):
        shift = margin - tap
        if shift == 0:
            piece, near_piece = src, near
        elif reverse:
            piece = pltpu.roll(src, rows - shift, 0)
            near_piece = pltpu.roll(near, span - shift, 0)
        else:
            piece = pltpu.roll(src, shift, 0)
            near_piece = pltpu.roll(near, shift, 0)
        main = main + w[tap : tap + 1] * piece
        part = near_piece[:edge] if reverse else near_piece[edge:]
        side = side + w[tap : tap + 1] * part
    out_ref[...] = jax.nn.silu(main).astype(out_ref.dtype)
    if reverse:
        out_ref[rows - edge :, :] = jax.nn.silu(side).astype(out_ref.dtype)
    else:
        out_ref[:edge, :] = jax.nn.silu(side).astype(out_ref.dtype)


def convolve(projected, halo, conv_w, conv_b, reverse):
    inner = H * P_SIZE
    count, rows, _ = projected.shape
    width = conv_w.shape[1]
    edge = 8
    margin = KCONV - 1
    pad = ((0, 0), (0, edge - margin), (0, 0)) if reverse else ((0, 0), (edge - margin, 0), (0, 0))
    halo8 = jnp.pad(halo, pad)
    lanes = CONV_LANES
    skip = inner // lanes
    return pl.pallas_call(
        partial(conv_kernel, reverse=reverse),
        grid=(count, width // lanes),
        in_specs=[
            pl.BlockSpec((None, rows, lanes), lambda g, j: (g, 0, j + skip)),
            pl.BlockSpec((None, edge, lanes), lambda g, j: (g, 0, j)),
            pl.BlockSpec((KCONV, lanes), lambda g, j: (0, j)),
            pl.BlockSpec((1, lanes), lambda g, j: (0, j)),
        ],
        out_specs=pl.BlockSpec((None, rows, lanes), lambda g, j: (g, 0, j)),
        out_shape=jax.ShapeDtypeStruct((count, rows, width), jnp.bfloat16),
    )(projected, halo8, conv_w, conv_b.reshape(1, width))


def strand_terms(projected, halo, step_size, conv_w, conv_b, rates, reverse):
    inner = H * P_SIZE
    count, rows, _ = projected.shape
    activated = convolve(projected, halo, conv_w, conv_b, reverse)
    spans = rows // Q
    inside, state, total, from_start = block_terms(activated, step_size, rates, reverse)
    order = list(range(spans))
    if reverse:
        order = order[::-1]
    before = {}
    sofar = (jnp.ones((count, H), jnp.float32), jnp.zeros((count, H, P_SIZE, N), jnp.float32))
    for j in order:
        before[j] = sofar
        sofar = chain(sofar, (total[:, j], state[:, j]))
    before_decay = jnp.stack([before[j][0] for j in range(spans)], axis=1)
    before_state = jnp.stack([before[j][1] for j in range(spans)], axis=1)
    pending = (before_decay, before_state, inside, from_start, activated)
    return sofar, pending


def finish(pending, incoming, gate_part, d_skip, norm_gain):
    before_decay, before_state, inside, from_start, activated = pending
    inner = H * P_SIZE
    count, rows, _ = activated.shape
    spans = rows // Q
    start_state = before_state + before_decay[..., None, None] * incoming[:, None]
    c_rows = activated[:, :, inner + N :].reshape(count, spans, Q, N)
    carried = jnp.einsum(
        "gjtn,gjkn->gjtk",
        c_rows.astype(jnp.float32),
        start_state.reshape(count, spans, inner, N),
        precision=lax.Precision.HIGHEST,
    ).reshape(count, rows, inner)
    scale = jnp.repeat(from_start.reshape(count, rows, H), P_SIZE, axis=-1)
    skip = jnp.repeat(d_skip, P_SIZE)
    scanned = inside + scale * carried + skip * activated[:, :, :inner].astype(jnp.float32)
    gated = scanned * jax.nn.silu(gate_part)
    return (
        gated
        * lax.rsqrt(jnp.mean(gated * gated, axis=-1, keepdims=True) + norm_epsilon)
        * norm_gain
    ).astype(jnp.bfloat16)


def on_device(
    tokens, hidden, base_table, w_in, w_dt, conv_w, conv_b, dt_bias, a_log, d_skip, norm_gain, w_out
):
    inner = H * P_SIZE
    margin = KCONV - 1
    one_hot = (tokens[:, :, None] == jnp.arange(4)[None, None, :]).astype(jnp.bfloat16)
    looked = jnp.einsum("gtb,bd->gtd", one_hot, base_table, preferred_element_type=jnp.float32)
    strand = (hidden.astype(jnp.float32) + looked).astype(jnp.bfloat16)
    rows = strand.shape[1]
    count = lax.axis_size("seq")
    low = lax.ppermute(strand[:, rows - margin :], "seq", [(i, i + 1) for i in range(count - 1)])
    high = lax.ppermute(strand[:, :margin], "seq", [(i + 1, i) for i in range(count - 1)])
    w_source = w_in[:, inner:]
    rates = -jnp.exp(a_log)
    proj_f = jnp.einsum("grd,de->gre", strand, w_in, preferred_element_type=jnp.float32)
    halo_f = jnp.einsum("grd,de->gre", low, w_source, preferred_element_type=jnp.float32)
    step_f = jax.nn.softplus(
        jnp.einsum("grd,dh->grh", strand, w_dt, preferred_element_type=jnp.float32) + dt_bias
    )
    sum_f, pend_f = strand_terms(proj_f, halo_f, step_f, conv_w, conv_b, rates, False)
    sum_f, (strand_late, high) = lax.optimization_barrier((sum_f, (strand, high)))
    mirrored = flip_lanes(strand_late)
    high_mirrored = flip_lanes(high)
    proj_r = jnp.einsum("grd,de->gre", mirrored, w_in, preferred_element_type=jnp.float32)
    halo_r = jnp.einsum("grd,de->gre", high_mirrored, w_source, preferred_element_type=jnp.float32)
    step_r = jax.nn.softplus(
        jnp.einsum("grd,dh->grh", mirrored, w_dt, preferred_element_type=jnp.float32) + dt_bias
    )
    sum_r, pend_r = strand_terms(proj_r, halo_r, step_r, conv_w, conv_b, rates, True)
    in_f, in_r = exclusive_scans(sum_f, sum_r, "seq")
    normed_f = finish(pend_f, in_f[1], proj_f[:, :, :inner], d_skip, norm_gain)
    normed_r = finish(pend_r, in_r[1], proj_r[:, :, :inner], d_skip, norm_gain)
    w_out_mirrored = flip_lanes(w_out)
    out = jnp.einsum(
        "grk,kd->grd", normed_f, w_out, preferred_element_type=jnp.float32
    ) + jnp.einsum("grk,kd->grd", normed_r, w_out_mirrored, preferred_element_type=jnp.float32)
    return out.astype(jnp.bfloat16)


def solution(mesh):
    placed = (
        P(("groups", "batch"), "seq"),
        P(("groups", "batch"), "seq", None),
        P(),
        P(),
        P(),
        P(),
        P(),
        P(),
        P(),
        P(),
        P(),
        P(),
    )
    return jax.shard_map(
        on_device,
        mesh=mesh,
        in_specs=placed,
        out_specs=P(("groups", "batch"), "seq", None),
        check_vma=False,
    )
```

```python
from functools import partial

import jax
import jax.numpy as jnp
from jax import lax
from jax.experimental import pallas as pl
from jax.experimental.pallas import tpu as pltpu
from jax.sharding import PartitionSpec as P

H = 16
P_SIZE = 64
N = 128
Q = 256
KCONV = 4


norm_epsilon = 1e-05


def exchange(size, dtype):
    row = lax.broadcasted_iota(jnp.int32, (size, size), 0)
    col = lax.broadcasted_iota(jnp.int32, (size, size), 1)
    return (row + col == size - 1).astype(dtype)


def flip_lanes(a):
    j = exchange(a.shape[-1], a.dtype)
    return jnp.einsum("...d,de->...e", a, j, preferred_element_type=jnp.float32).astype(a.dtype)


def chain(earlier, later):
    first_decay, first_state = earlier
    next_decay, next_state = later
    return (first_decay * next_decay, next_decay[..., None, None] * first_state + next_state)


def exclusive_scans(fwd, rev, axis):
    count = lax.axis_size(axis)
    place = lax.axis_index(axis)
    seen = [None, None]
    ahead = [fwd, rev]
    shift = 1
    while shift < count:
        up = [(i, i + shift) for i in range(count - shift)]
        down = [(i + shift, i) for i in range(count - shift)]
        got = []
        for k, pairs in ((0, up), (1, down)):
            decay, state = unpack(lax.ppermute(pack(*ahead[k]), axis, pairs))
            has = (place >= shift) if k == 0 else (place < count - shift)
            decay = jnp.where(has, decay, 1.0)
            got.append((decay, state))
        for k in range(2):
            seen[k] = got[k] if seen[k] is None else chain(got[k], seen[k])
            if 2 * shift < count:
                ahead[k] = chain(got[k], ahead[k])
        shift *= 2
    if seen[0] is None:
        return fwd_identity(fwd), fwd_identity(rev)
    return seen[0], seen[1]


def pack(decay, state):
    extra = jnp.broadcast_to(decay[:, :, None, None], decay.shape + (8, state.shape[-1]))
    return jnp.concatenate([state, extra], axis=2)


def unpack(packed):
    return packed[:, :, P_SIZE, 0], packed[:, :, :P_SIZE]


def fwd_identity(summary):
    decay, state = summary
    return (jnp.ones_like(decay), jnp.zeros_like(state))


def inside_kernel(xbc_ref, cum_ref, cum_t_ref, step_t_ref, inside_ref, *, reverse):
    inner = H * P_SIZE
    b_rows = xbc_ref[:, inner : inner + N]
    c_rows = xbc_ref[:, inner + N :]
    scores = lax.dot_general(
        c_rows, b_rows, (((1,), (1,)), ((), ())), preferred_element_type=jnp.float32
    )
    t_idx = lax.broadcasted_iota(jnp.int32, (Q, Q), 0)
    s_idx = lax.broadcasted_iota(jnp.int32, (Q, Q), 1)
    keep = (s_idx >= t_idx) if reverse else (t_idx >= s_idx)
    for h in range(H):
        gaps = cum_ref[:, h : h + 1] - cum_t_ref[h : h + 1, :]
        decays = jnp.where(keep, jnp.exp(jnp.where(keep, gaps, 0.0)), 0.0)
        weights = (decays * scores * step_t_ref[h : h + 1, :]).astype(jnp.bfloat16)
        x_h = xbc_ref[:, h * P_SIZE : (h + 1) * P_SIZE]
        inside_ref[:, h * P_SIZE : (h + 1) * P_SIZE] = jnp.dot(
            weights, x_h, preferred_element_type=jnp.float32
        )


def state_kernel(xbc_ref, to_end_ref, state_ref):
    inner = H * P_SIZE
    b_wide = xbc_ref[:, inner : inner + N].astype(jnp.float32)
    for h in range(H):
        state_weights = (b_wide * to_end_ref[:, h : h + 1]).astype(jnp.bfloat16)
        x_h = xbc_ref[:, h * P_SIZE : (h + 1) * P_SIZE]
        state_ref[h] = lax.dot_general(
            x_h, state_weights, (((0,), (0,)), ((), ())), preferred_element_type=jnp.float32
        )


def block_terms(activated, step_size, rates, reverse):
    count, rows, width = activated.shape
    spans = rows // Q
    blocks = count * spans
    steps_cut = step_size.reshape(count, spans, Q, H)
    rated = steps_cut * rates
    log_decay = jnp.cumsum(rated, axis=2)
    if reverse:
        log_decay = log_decay[:, :, -1:] - log_decay + rated
    end = log_decay[:, :, 0] if reverse else log_decay[:, :, -1]
    to_end = jnp.exp(end[:, :, None, :] - log_decay) * steps_cut
    flat = lambda a: a.reshape((blocks,) + a.shape[2:])
    cum = flat(log_decay)
    cum_t = jnp.swapaxes(cum, 1, 2)
    step_t = jnp.swapaxes(flat(steps_cut), 1, 2)
    xbc = activated.reshape(blocks, Q, width)
    spec = lambda shape: pl.BlockSpec((None,) + shape, lambda i: (i,) + (0,) * len(shape))
    state = pl.pallas_call(
        state_kernel,
        grid=(blocks,),
        in_specs=[spec((Q, width)), spec((Q, H))],
        out_specs=spec((H, P_SIZE, N)),
        out_shape=jax.ShapeDtypeStruct((blocks, H, P_SIZE, N), jnp.float32),
    )(xbc, flat(to_end))
    inside = pl.pallas_call(
        partial(inside_kernel, reverse=reverse),
        grid=(blocks,),
        in_specs=[spec((Q, width)), spec((Q, H)), spec((H, Q)), spec((H, Q))],
        out_specs=spec((Q, H * P_SIZE)),
        out_shape=jax.ShapeDtypeStruct((blocks, Q, H * P_SIZE), jnp.float32),
    )(xbc, cum, cum_t, step_t)
    inside = inside.reshape(count, rows, H * P_SIZE)
    state = state.reshape(count, spans, H, P_SIZE, N)
    return inside, state, jnp.exp(end), jnp.exp(log_decay)


CONV_LANES = 256


def conv_kernel(src_ref, halo_ref, w_ref, b_ref, out_ref, *, reverse):
    margin = KCONV - 1
    src = src_ref[...]
    rows = src.shape[0]
    edge = halo_ref.shape[0]
    w = w_ref[...]
    if reverse:
        near = jnp.concatenate([src[rows - edge :], halo_ref[...]], axis=0)
    else:
        near = jnp.concatenate([halo_ref[...], src[:edge]], axis=0)
    span = near.shape[0]
    main = jnp.broadcast_to(b_ref[...], src.shape)
    side = jnp.broadcast_to(b_ref[...], (edge, src.shape[1]))
    for tap in range(KCONV):
        shift = margin - tap
        if shift == 0:
            piece, near_piece = src, near
        elif reverse:
            piece = pltpu.roll(src, rows - shift, 0)
            near_piece = pltpu.roll(near, span - shift, 0)
        else:
            piece = pltpu.roll(src, shift, 0)
            near_piece = pltpu.roll(near, shift, 0)
        main = main + w[tap : tap + 1] * piece
        part = near_piece[:edge] if reverse else near_piece[edge:]
        side = side + w[tap : tap + 1] * part
    out_ref[...] = jax.nn.silu(main).astype(out_ref.dtype)
    if reverse:
        out_ref[rows - edge :, :] = jax.nn.silu(side).astype(out_ref.dtype)
    else:
        out_ref[:edge, :] = jax.nn.silu(side).astype(out_ref.dtype)


def convolve(projected, halo, conv_w, conv_b, reverse):
    inner = H * P_SIZE
    count, rows, _ = projected.shape
    width = conv_w.shape[1]
    edge = 8
    margin = KCONV - 1
    pad = ((0, 0), (0, edge - margin), (0, 0)) if reverse else ((0, 0), (edge - margin, 0), (0, 0))
    halo8 = jnp.pad(halo, pad)
    lanes = CONV_LANES
    skip = inner // lanes
    return pl.pallas_call(
        partial(conv_kernel, reverse=reverse),
        grid=(count, width // lanes),
        in_specs=[
            pl.BlockSpec((None, rows, lanes), lambda g, j: (g, 0, j + skip)),
            pl.BlockSpec((None, edge, lanes), lambda g, j: (g, 0, j)),
            pl.BlockSpec((KCONV, lanes), lambda g, j: (0, j)),
            pl.BlockSpec((1, lanes), lambda g, j: (0, j)),
        ],
        out_specs=pl.BlockSpec((None, rows, lanes), lambda g, j: (g, 0, j)),
        out_shape=jax.ShapeDtypeStruct((count, rows, width), jnp.bfloat16),
    )(projected, halo8, conv_w, conv_b.reshape(1, width))


def strand_terms(projected, halo, step_size, conv_w, conv_b, rates, reverse):
    inner = H * P_SIZE
    count, rows, _ = projected.shape
    activated = convolve(projected, halo, conv_w, conv_b, reverse)
    spans = rows // Q
    inside, state, total, from_start = block_terms(activated, step_size, rates, reverse)
    order = list(range(spans))
    if reverse:
        order = order[::-1]
    before = {}
    sofar = (jnp.ones((count, H), jnp.float32), jnp.zeros((count, H, P_SIZE, N), jnp.float32))
    for j in order:
        before[j] = sofar
        sofar = chain(sofar, (total[:, j], state[:, j]))
    before_decay = jnp.stack([before[j][0] for j in range(spans)], axis=1)
    before_state = jnp.stack([before[j][1] for j in range(spans)], axis=1)
    pending = (before_decay, before_state, inside, from_start, activated)
    return sofar, pending


def finish(pending, incoming, gate_part, d_skip, norm_gain):
    before_decay, before_state, inside, from_start, activated = pending
    inner = H * P_SIZE
    count, rows, _ = activated.shape
    spans = rows // Q
    start_state = before_state + before_decay[..., None, None] * incoming[:, None]
    c_rows = activated[:, :, inner + N :].reshape(count, spans, Q, N)
    carried = jnp.einsum(
        "gjtn,gjkn->gjtk",
        c_rows.astype(jnp.float32),
        start_state.reshape(count, spans, inner, N),
        precision=lax.Precision.HIGHEST,
    ).reshape(count, rows, inner)
    heads = lax.broadcasted_iota(jnp.int32, (H, inner), 0)
    lanes = lax.broadcasted_iota(jnp.int32, (H, inner), 1)
    spread = (lanes // P_SIZE == heads).astype(jnp.float32)
    scale = jnp.einsum(
        "grh,hk->grk", from_start.reshape(count, rows, H), spread, precision=lax.Precision.HIGHEST
    )
    skip = jnp.repeat(d_skip, P_SIZE)
    scanned = inside + scale * carried + skip * activated[:, :, :inner].astype(jnp.float32)
    gated = scanned * jax.nn.silu(gate_part)
    return (
        gated
        * lax.rsqrt(jnp.mean(gated * gated, axis=-1, keepdims=True) + norm_epsilon)
        * norm_gain
    ).astype(jnp.bfloat16)


def on_device(
    tokens, hidden, base_table, w_in, w_dt, conv_w, conv_b, dt_bias, a_log, d_skip, norm_gain, w_out
):
    inner = H * P_SIZE
    margin = KCONV - 1
    one_hot = (tokens[:, :, None] == jnp.arange(4)[None, None, :]).astype(jnp.bfloat16)
    looked = jnp.einsum("gtb,bd->gtd", one_hot, base_table, preferred_element_type=jnp.float32)
    strand = (hidden.astype(jnp.float32) + looked).astype(jnp.bfloat16)
    rows = strand.shape[1]
    count = lax.axis_size("seq")
    low = lax.ppermute(strand[:, rows - margin :], "seq", [(i, i + 1) for i in range(count - 1)])
    high = lax.ppermute(strand[:, :margin], "seq", [(i + 1, i) for i in range(count - 1)])
    w_source = w_in[:, inner:]
    rates = -jnp.exp(a_log)
    proj_f = jnp.einsum("grd,de->gre", strand, w_in, preferred_element_type=jnp.float32)
    halo_f = jnp.einsum("grd,de->gre", low, w_source, preferred_element_type=jnp.float32)
    step_f = jax.nn.softplus(
        jnp.einsum("grd,dh->grh", strand, w_dt, preferred_element_type=jnp.float32) + dt_bias
    )
    sum_f, pend_f = strand_terms(proj_f, halo_f, step_f, conv_w, conv_b, rates, False)
    sum_f, (strand_late, high) = lax.optimization_barrier((sum_f, (strand, high)))
    mirrored = flip_lanes(strand_late)
    high_mirrored = flip_lanes(high)
    proj_r = jnp.einsum("grd,de->gre", mirrored, w_in, preferred_element_type=jnp.float32)
    halo_r = jnp.einsum("grd,de->gre", high_mirrored, w_source, preferred_element_type=jnp.float32)
    step_r = jax.nn.softplus(
        jnp.einsum("grd,dh->grh", mirrored, w_dt, preferred_element_type=jnp.float32) + dt_bias
    )
    sum_r, pend_r = strand_terms(proj_r, halo_r, step_r, conv_w, conv_b, rates, True)
    in_f, in_r = exclusive_scans(sum_f, sum_r, "seq")
    normed_f = finish(pend_f, in_f[1], proj_f[:, :, :inner], d_skip, norm_gain)
    normed_r = finish(pend_r, in_r[1], proj_r[:, :, :inner], d_skip, norm_gain)
    w_out_mirrored = flip_lanes(w_out)
    out = jnp.einsum(
        "grk,kd->grd", normed_f, w_out, preferred_element_type=jnp.float32
    ) + jnp.einsum("grk,kd->grd", normed_r, w_out_mirrored, preferred_element_type=jnp.float32)
    return out.astype(jnp.bfloat16)


def solution(mesh):
    placed = (
        P(("groups", "batch"), "seq"),
        P(("groups", "batch"), "seq", None),
        P(),
        P(),
        P(),
        P(),
        P(),
        P(),
        P(),
        P(),
        P(),
        P(),
    )
    return jax.shard_map(
        on_device,
        mesh=mesh,
        in_specs=placed,
        out_specs=P(("groups", "batch"), "seq", None),
        check_vma=False,
    )
```

```python
from functools import partial

import jax
import jax.numpy as jnp
from jax import lax
from jax.experimental import pallas as pl
from jax.experimental.pallas import tpu as pltpu
from jax.sharding import PartitionSpec as P

H = 16
P_SIZE = 64
N = 128
Q = 256
KCONV = 4


norm_epsilon = 1e-05


def exchange(size, dtype):
    row = lax.broadcasted_iota(jnp.int32, (size, size), 0)
    col = lax.broadcasted_iota(jnp.int32, (size, size), 1)
    return (row + col == size - 1).astype(dtype)


def flip_lanes(a):
    j = exchange(a.shape[-1], a.dtype)
    return jnp.einsum("...d,de->...e", a, j, preferred_element_type=jnp.float32).astype(a.dtype)


def chain(earlier, later):
    first_decay, first_state = earlier
    next_decay, next_state = later
    return (first_decay * next_decay, next_decay[..., None, None] * first_state + next_state)


def scan(summary, axis, reverse, fillers):
    count = lax.axis_size(axis)
    place = lax.axis_index(axis)
    seen = None
    ahead = summary
    shift = 1
    done = []
    fillers = list(fillers)
    while shift < count:
        fill = fillers.pop(0)(done) if fillers else None
        if fill is not None:
            fn, args = fill
            ahead, args = lax.optimization_barrier((ahead, args))
        if reverse:
            pairs = [(i + shift, i) for i in range(count - shift)]
            has = place < count - shift
        else:
            pairs = [(i, i + shift) for i in range(count - shift)]
            has = place >= shift
        decay, state = unpack(lax.ppermute(pack(*ahead), axis, pairs))
        got = (jnp.where(has, decay, 1.0), state)
        if fill is not None:
            got, out = lax.optimization_barrier((got, fn(*args)))
            done.append(out)
        seen = got if seen is None else chain(got, seen)
        if 2 * shift < count:
            ahead = chain(got, ahead)
        shift *= 2
    for make in fillers:
        fill = make(done)
        if fill is not None:
            done.append(fill[0](*fill[1]))
    if seen is None:
        seen = fwd_identity(summary)
    return seen, done


def pack(decay, state):
    extra = jnp.broadcast_to(decay[:, :, None, None], decay.shape + (8, state.shape[-1]))
    return jnp.concatenate([state, extra], axis=2)


def unpack(packed):
    return packed[:, :, P_SIZE, 0], packed[:, :, :P_SIZE]


def fwd_identity(summary):
    decay, state = summary
    return (jnp.ones_like(decay), jnp.zeros_like(state))


def inside_kernel(xbc_ref, cum_ref, cum_t_ref, step_t_ref, inside_ref, *, reverse):
    inner = H * P_SIZE
    b_rows = xbc_ref[:, inner : inner + N]
    c_rows = xbc_ref[:, inner + N :]
    scores = lax.dot_general(
        c_rows, b_rows, (((1,), (1,)), ((), ())), preferred_element_type=jnp.float32
    )
    t_idx = lax.broadcasted_iota(jnp.int32, (Q, Q), 0)
    s_idx = lax.broadcasted_iota(jnp.int32, (Q, Q), 1)
    keep = (s_idx >= t_idx) if reverse else (t_idx >= s_idx)
    for h in range(H):
        gaps = cum_ref[:, h : h + 1] - cum_t_ref[h : h + 1, :]
        decays = jnp.where(keep, jnp.exp(jnp.where(keep, gaps, 0.0)), 0.0)
        weights = (decays * scores * step_t_ref[h : h + 1, :]).astype(jnp.bfloat16)
        x_h = xbc_ref[:, h * P_SIZE : (h + 1) * P_SIZE]
        inside_ref[:, h * P_SIZE : (h + 1) * P_SIZE] = jnp.dot(
            weights, x_h, preferred_element_type=jnp.float32
        )


def state_kernel(xbc_ref, to_end_ref, state_ref):
    inner = H * P_SIZE
    b_wide = xbc_ref[:, inner : inner + N].astype(jnp.float32)
    for h in range(H):
        state_weights = (b_wide * to_end_ref[:, h : h + 1]).astype(jnp.bfloat16)
        x_h = xbc_ref[:, h * P_SIZE : (h + 1) * P_SIZE]
        state_ref[h] = lax.dot_general(
            x_h, state_weights, (((0,), (0,)), ((), ())), preferred_element_type=jnp.float32
        )


def block_terms(activated, step_size, rates, reverse):
    count, rows, width = activated.shape
    spans = rows // Q
    blocks = count * spans
    steps_cut = step_size.reshape(count, spans, Q, H)
    rated = steps_cut * rates
    log_decay = jnp.cumsum(rated, axis=2)
    if reverse:
        log_decay = log_decay[:, :, -1:] - log_decay + rated
    end = log_decay[:, :, 0] if reverse else log_decay[:, :, -1]
    to_end = jnp.exp(end[:, :, None, :] - log_decay) * steps_cut
    flat = lambda a: a.reshape((blocks,) + a.shape[2:])
    cum = flat(log_decay)
    cum_t = jnp.swapaxes(cum, 1, 2)
    step_t = jnp.swapaxes(flat(steps_cut), 1, 2)
    xbc = activated.reshape(blocks, Q, width)
    spec = lambda shape: pl.BlockSpec((None,) + shape, lambda i: (i,) + (0,) * len(shape))
    state = pl.pallas_call(
        state_kernel,
        grid=(blocks,),
        in_specs=[spec((Q, width)), spec((Q, H))],
        out_specs=spec((H, P_SIZE, N)),
        out_shape=jax.ShapeDtypeStruct((blocks, H, P_SIZE, N), jnp.float32),
    )(xbc, flat(to_end))
    state = state.reshape(count, spans, H, P_SIZE, N)
    return state, jnp.exp(end), jnp.exp(log_decay), (xbc, cum, cum_t, step_t)


def inside_terms(inside_args, reverse, count, rows):
    xbc, cum, cum_t, step_t = inside_args
    blocks, _, width = xbc.shape
    spec = lambda shape: pl.BlockSpec((None,) + shape, lambda i: (i,) + (0,) * len(shape))
    inside = pl.pallas_call(
        partial(inside_kernel, reverse=reverse),
        grid=(blocks,),
        in_specs=[spec((Q, width)), spec((Q, H)), spec((H, Q)), spec((H, Q))],
        out_specs=spec((Q, H * P_SIZE)),
        out_shape=jax.ShapeDtypeStruct((blocks, Q, H * P_SIZE), jnp.float32),
    )(xbc, cum, cum_t, step_t)
    return inside.reshape(count, rows, H * P_SIZE)


CONV_LANES = 256


def conv_kernel(src_ref, halo_ref, w_ref, b_ref, out_ref, *, reverse):
    margin = KCONV - 1
    src = src_ref[...]
    rows = src.shape[0]
    edge = halo_ref.shape[0]
    w = w_ref[...]
    if reverse:
        near = jnp.concatenate([src[rows - edge :], halo_ref[...]], axis=0)
    else:
        near = jnp.concatenate([halo_ref[...], src[:edge]], axis=0)
    span = near.shape[0]
    main = jnp.broadcast_to(b_ref[...], src.shape)
    side = jnp.broadcast_to(b_ref[...], (edge, src.shape[1]))
    for tap in range(KCONV):
        shift = margin - tap
        if shift == 0:
            piece, near_piece = src, near
        elif reverse:
            piece = pltpu.roll(src, rows - shift, 0)
            near_piece = pltpu.roll(near, span - shift, 0)
        else:
            piece = pltpu.roll(src, shift, 0)
            near_piece = pltpu.roll(near, shift, 0)
        main = main + w[tap : tap + 1] * piece
        part = near_piece[:edge] if reverse else near_piece[edge:]
        side = side + w[tap : tap + 1] * part
    out_ref[...] = jax.nn.silu(main).astype(out_ref.dtype)
    if reverse:
        out_ref[rows - edge :, :] = jax.nn.silu(side).astype(out_ref.dtype)
    else:
        out_ref[:edge, :] = jax.nn.silu(side).astype(out_ref.dtype)


def convolve(projected, halo, conv_w, conv_b, reverse):
    inner = H * P_SIZE
    count, rows, _ = projected.shape
    width = conv_w.shape[1]
    edge = 8
    margin = KCONV - 1
    pad = ((0, 0), (0, edge - margin), (0, 0)) if reverse else ((0, 0), (edge - margin, 0), (0, 0))
    halo8 = jnp.pad(halo, pad)
    lanes = CONV_LANES
    skip = inner // lanes
    return pl.pallas_call(
        partial(conv_kernel, reverse=reverse),
        grid=(count, width // lanes),
        in_specs=[
            pl.BlockSpec((None, rows, lanes), lambda g, j: (g, 0, j + skip)),
            pl.BlockSpec((None, edge, lanes), lambda g, j: (g, 0, j)),
            pl.BlockSpec((KCONV, lanes), lambda g, j: (0, j)),
            pl.BlockSpec((1, lanes), lambda g, j: (0, j)),
        ],
        out_specs=pl.BlockSpec((None, rows, lanes), lambda g, j: (g, 0, j)),
        out_shape=jax.ShapeDtypeStruct((count, rows, width), jnp.bfloat16),
    )(projected, halo8, conv_w, conv_b.reshape(1, width))


def strand_terms(projected, halo, step_size, conv_w, conv_b, rates, reverse):
    inner = H * P_SIZE
    count, rows, _ = projected.shape
    activated = convolve(projected, halo, conv_w, conv_b, reverse)
    spans = rows // Q
    state, total, from_start, inside_args = block_terms(activated, step_size, rates, reverse)
    order = list(range(spans))
    if reverse:
        order = order[::-1]
    before = {}
    sofar = (jnp.ones((count, H), jnp.float32), jnp.zeros((count, H, P_SIZE, N), jnp.float32))
    for j in order:
        before[j] = sofar
        sofar = chain(sofar, (total[:, j], state[:, j]))
    before_decay = jnp.stack([before[j][0] for j in range(spans)], axis=1)
    before_state = jnp.stack([before[j][1] for j in range(spans)], axis=1)
    pending = (before_decay, before_state, from_start, activated)
    return sofar, pending, inside_args


def finish(pending, inside, incoming, gate_part, d_skip, norm_gain):
    before_decay, before_state, from_start, activated = pending
    inner = H * P_SIZE
    count, rows, _ = activated.shape
    spans = rows // Q
    start_state = before_state + before_decay[..., None, None] * incoming[:, None]
    c_rows = activated[:, :, inner + N :].reshape(count, spans, Q, N)
    carried = jnp.einsum(
        "gjtn,gjkn->gjtk",
        c_rows.astype(jnp.float32),
        start_state.reshape(count, spans, inner, N),
        precision=lax.Precision.HIGHEST,
    ).reshape(count, rows, inner)
    heads = lax.broadcasted_iota(jnp.int32, (H, inner), 0)
    lanes = lax.broadcasted_iota(jnp.int32, (H, inner), 1)
    spread = (lanes // P_SIZE == heads).astype(jnp.float32)
    scale = jnp.einsum(
        "grh,hk->grk", from_start.reshape(count, rows, H), spread, precision=lax.Precision.HIGHEST
    )
    skip = jnp.repeat(d_skip, P_SIZE)
    scanned = inside + scale * carried + skip * activated[:, :, :inner].astype(jnp.float32)
    gated = scanned * jax.nn.silu(gate_part)
    return (
        gated
        * lax.rsqrt(jnp.mean(gated * gated, axis=-1, keepdims=True) + norm_epsilon)
        * norm_gain
    ).astype(jnp.bfloat16)


def on_device(
    tokens, hidden, base_table, w_in, w_dt, conv_w, conv_b, dt_bias, a_log, d_skip, norm_gain, w_out
):
    inner = H * P_SIZE
    margin = KCONV - 1
    one_hot = (tokens[:, :, None] == jnp.arange(4)[None, None, :]).astype(jnp.bfloat16)
    looked = jnp.einsum("gtb,bd->gtd", one_hot, base_table, preferred_element_type=jnp.float32)
    strand = (hidden.astype(jnp.float32) + looked).astype(jnp.bfloat16)
    rows = strand.shape[1]
    count = lax.axis_size("seq")
    low = lax.ppermute(strand[:, rows - margin :], "seq", [(i, i + 1) for i in range(count - 1)])
    high = lax.ppermute(strand[:, :margin], "seq", [(i + 1, i) for i in range(count - 1)])
    w_source = w_in[:, inner:]
    rates = -jnp.exp(a_log)
    proj_f = jnp.einsum("grd,de->gre", strand, w_in, preferred_element_type=jnp.float32)
    halo_f = jnp.einsum("grd,de->gre", low, w_source, preferred_element_type=jnp.float32)
    step_f = jax.nn.softplus(
        jnp.einsum("grd,dh->grh", strand, w_dt, preferred_element_type=jnp.float32) + dt_bias
    )
    sum_f, pend_f, args_f = strand_terms(proj_f, halo_f, step_f, conv_w, conv_b, rates, False)
    count_g = strand.shape[0]

    def reverse_prep(strand_late, high_late):
        mirrored = flip_lanes(strand_late)
        high_mirrored = flip_lanes(high_late)
        proj_r = jnp.einsum("grd,de->gre", mirrored, w_in, preferred_element_type=jnp.float32)
        halo_r = jnp.einsum(
            "grd,de->gre", high_mirrored, w_source, preferred_element_type=jnp.float32
        )
        step_r = jax.nn.softplus(
            jnp.einsum("grd,dh->grh", mirrored, w_dt, preferred_element_type=jnp.float32) + dt_bias
        )
        sum_r, pend_r, args_r = strand_terms(proj_r, halo_r, step_r, conv_w, conv_b, rates, True)
        return sum_r, pend_r, args_r, proj_r[:, :, :inner]

    def inside_f_fill(done):
        return (lambda *a: inside_terms(a, False, count_g, rows), args_f)

    def inside_r_fill(done):
        args_r = done[0][2]
        return (lambda *a: inside_terms(a, True, count_g, rows), args_r)

    in_f, done_f = scan(
        sum_f,
        "seq",
        False,
        [lambda done: (reverse_prep, (strand, high)), inside_f_fill, inside_r_fill],
    )
    sum_r, pend_r, args_r, gate_r = done_f[0]
    inside_f, inside_r = done_f[1], done_f[2]

    def forward_out(inside_f, in_state):
        normed_f = finish(pend_f, inside_f, in_state, proj_f[:, :, :inner], d_skip, norm_gain)
        return jnp.einsum("grk,kd->grd", normed_f, w_out, preferred_element_type=jnp.float32)

    in_r, done_r = scan(
        sum_r,
        "seq",
        True,
        [lambda done: None, lambda done: (forward_out, (inside_f, in_f[1]))],
    )
    out_f = done_r[0]
    normed_r = finish(pend_r, inside_r, in_r[1], gate_r, d_skip, norm_gain)
    w_out_mirrored = flip_lanes(w_out)
    out = out_f + jnp.einsum(
        "grk,kd->grd", normed_r, w_out_mirrored, preferred_element_type=jnp.float32
    )
    return out.astype(jnp.bfloat16)


def solution(mesh):
    placed = (
        P(("groups", "batch"), "seq"),
        P(("groups", "batch"), "seq", None),
        P(),
        P(),
        P(),
        P(),
        P(),
        P(),
        P(),
        P(),
        P(),
        P(),
    )
    return jax.shard_map(
        on_device,
        mesh=mesh,
        in_specs=placed,
        out_specs=P(("groups", "batch"), "seq", None),
        check_vma=False,
    )
```

```python
from functools import partial

import jax
import jax.numpy as jnp
from jax import lax
from jax.experimental import pallas as pl
from jax.experimental.pallas import tpu as pltpu
from jax.sharding import PartitionSpec as P

H = 16
P_SIZE = 64
N = 128
Q = 256
KCONV = 4


norm_epsilon = 1e-05


def exchange(size, dtype):
    row = lax.broadcasted_iota(jnp.int32, (size, size), 0)
    col = lax.broadcasted_iota(jnp.int32, (size, size), 1)
    return (row + col == size - 1).astype(dtype)


def flip_lanes(a):
    j = exchange(a.shape[-1], a.dtype)
    return jnp.einsum("...d,de->...e", a, j, preferred_element_type=jnp.float32).astype(a.dtype)


def chain(earlier, later):
    first_decay, first_state = earlier
    next_decay, next_state = later
    return (first_decay * next_decay, next_decay[..., None, None] * first_state + next_state)


def exclusive_scans(fwd, rev, axis):
    count = lax.axis_size(axis)
    place = lax.axis_index(axis)
    seen = [None, None]
    ahead = [fwd, rev]
    shift = 1
    while shift < count:
        up = [(i, i + shift) for i in range(count - shift)]
        down = [(i + shift, i) for i in range(count - shift)]
        got = []
        for k, pairs in ((0, up), (1, down)):
            decay, state = unpack(lax.ppermute(pack(*ahead[k]), axis, pairs))
            has = (place >= shift) if k == 0 else (place < count - shift)
            decay = jnp.where(has, decay, 1.0)
            got.append((decay, state))
        for k in range(2):
            seen[k] = got[k] if seen[k] is None else chain(got[k], seen[k])
            if 2 * shift < count:
                ahead[k] = chain(got[k], ahead[k])
        shift *= 2
    if seen[0] is None:
        return fwd_identity(fwd), fwd_identity(rev)
    return seen[0], seen[1]


def pack(decay, state):
    count = state.shape[0]
    flat = state.reshape(count, H * P_SIZE, N)
    extra = jnp.zeros((count, 8, N), jnp.float32).at[:, 0, :H].set(decay)
    return jnp.concatenate([flat, extra], axis=1)


def unpack(packed):
    count = packed.shape[0]
    rows = H * P_SIZE
    return packed[:, rows, :H], packed[:, :rows].reshape(count, H, P_SIZE, N)


def fwd_identity(summary):
    decay, state = summary
    return (jnp.ones_like(decay), jnp.zeros_like(state))


def inside_kernel(xbc_ref, cum_ref, cum_t_ref, step_t_ref, inside_ref, *, reverse):
    inner = H * P_SIZE
    b_rows = xbc_ref[:, inner : inner + N]
    c_rows = xbc_ref[:, inner + N :]
    scores = lax.dot_general(
        c_rows, b_rows, (((1,), (1,)), ((), ())), preferred_element_type=jnp.float32
    )
    t_idx = lax.broadcasted_iota(jnp.int32, (Q, Q), 0)
    s_idx = lax.broadcasted_iota(jnp.int32, (Q, Q), 1)
    keep = (s_idx >= t_idx) if reverse else (t_idx >= s_idx)
    for h in range(H):
        gaps = cum_ref[:, h : h + 1] - cum_t_ref[h : h + 1, :]
        decays = jnp.where(keep, jnp.exp(jnp.where(keep, gaps, 0.0)), 0.0)
        weights = (decays * scores * step_t_ref[h : h + 1, :]).astype(jnp.bfloat16)
        x_h = xbc_ref[:, h * P_SIZE : (h + 1) * P_SIZE]
        inside_ref[:, h * P_SIZE : (h + 1) * P_SIZE] = jnp.dot(
            weights, x_h, preferred_element_type=jnp.float32
        )


def state_kernel(xbc_ref, to_end_ref, state_ref):
    inner = H * P_SIZE
    b_wide = xbc_ref[:, inner : inner + N].astype(jnp.float32)
    for h in range(H):
        state_weights = (b_wide * to_end_ref[:, h : h + 1]).astype(jnp.bfloat16)
        x_h = xbc_ref[:, h * P_SIZE : (h + 1) * P_SIZE]
        state_ref[h] = lax.dot_general(
            x_h, state_weights, (((0,), (0,)), ((), ())), preferred_element_type=jnp.float32
        )


def block_terms(activated, step_size, rates, reverse):
    count, rows, width = activated.shape
    spans = rows // Q
    blocks = count * spans
    steps_cut = step_size.reshape(count, spans, Q, H)
    rated = steps_cut * rates
    log_decay = jnp.cumsum(rated, axis=2)
    if reverse:
        log_decay = log_decay[:, :, -1:] - log_decay + rated
    end = log_decay[:, :, 0] if reverse else log_decay[:, :, -1]
    to_end = jnp.exp(end[:, :, None, :] - log_decay) * steps_cut
    flat = lambda a: a.reshape((blocks,) + a.shape[2:])
    cum = flat(log_decay)
    cum_t = jnp.swapaxes(cum, 1, 2)
    step_t = jnp.swapaxes(flat(steps_cut), 1, 2)
    xbc = activated.reshape(blocks, Q, width)
    spec = lambda shape: pl.BlockSpec((None,) + shape, lambda i: (i,) + (0,) * len(shape))
    state = pl.pallas_call(
        state_kernel,
        grid=(blocks,),
        in_specs=[spec((Q, width)), spec((Q, H))],
        out_specs=spec((H, P_SIZE, N)),
        out_shape=jax.ShapeDtypeStruct((blocks, H, P_SIZE, N), jnp.float32),
    )(xbc, flat(to_end))
    inside = pl.pallas_call(
        partial(inside_kernel, reverse=reverse),
        grid=(blocks,),
        in_specs=[spec((Q, width)), spec((Q, H)), spec((H, Q)), spec((H, Q))],
        out_specs=spec((Q, H * P_SIZE)),
        out_shape=jax.ShapeDtypeStruct((blocks, Q, H * P_SIZE), jnp.float32),
    )(xbc, cum, cum_t, step_t)
    inside = inside.reshape(count, rows, H * P_SIZE)
    state = state.reshape(count, spans, H, P_SIZE, N)
    return inside, state, jnp.exp(end), jnp.exp(log_decay)


CONV_LANES = 256


def conv_kernel(src_ref, halo_ref, w_ref, b_ref, out_ref, *, reverse):
    margin = KCONV - 1
    src = src_ref[...]
    rows = src.shape[0]
    edge = halo_ref.shape[0]
    w = w_ref[...]
    if reverse:
        near = jnp.concatenate([src[rows - edge :], halo_ref[...]], axis=0)
    else:
        near = jnp.concatenate([halo_ref[...], src[:edge]], axis=0)
    span = near.shape[0]
    main = jnp.broadcast_to(b_ref[...], src.shape)
    side = jnp.broadcast_to(b_ref[...], (edge, src.shape[1]))
    for tap in range(KCONV):
        shift = margin - tap
        if shift == 0:
            piece, near_piece = src, near
        elif reverse:
            piece = pltpu.roll(src, rows - shift, 0)
            near_piece = pltpu.roll(near, span - shift, 0)
        else:
            piece = pltpu.roll(src, shift, 0)
            near_piece = pltpu.roll(near, shift, 0)
        main = main + w[tap : tap + 1] * piece
        part = near_piece[:edge] if reverse else near_piece[edge:]
        side = side + w[tap : tap + 1] * part
    out_ref[...] = jax.nn.silu(main).astype(out_ref.dtype)
    if reverse:
        out_ref[rows - edge :, :] = jax.nn.silu(side).astype(out_ref.dtype)
    else:
        out_ref[:edge, :] = jax.nn.silu(side).astype(out_ref.dtype)


def convolve(projected, halo, conv_w, conv_b, reverse):
    inner = H * P_SIZE
    count, rows, _ = projected.shape
    width = conv_w.shape[1]
    edge = 8
    margin = KCONV - 1
    pad = ((0, 0), (0, edge - margin), (0, 0)) if reverse else ((0, 0), (edge - margin, 0), (0, 0))
    halo8 = jnp.pad(halo, pad)
    lanes = CONV_LANES
    skip = inner // lanes
    return pl.pallas_call(
        partial(conv_kernel, reverse=reverse),
        grid=(count, width // lanes),
        in_specs=[
            pl.BlockSpec((None, rows, lanes), lambda g, j: (g, 0, j + skip)),
            pl.BlockSpec((None, edge, lanes), lambda g, j: (g, 0, j)),
            pl.BlockSpec((KCONV, lanes), lambda g, j: (0, j)),
            pl.BlockSpec((1, lanes), lambda g, j: (0, j)),
        ],
        out_specs=pl.BlockSpec((None, rows, lanes), lambda g, j: (g, 0, j)),
        out_shape=jax.ShapeDtypeStruct((count, rows, width), jnp.bfloat16),
    )(projected, halo8, conv_w, conv_b.reshape(1, width))


def strand_terms(projected, halo, step_size, conv_w, conv_b, rates, reverse):
    inner = H * P_SIZE
    count, rows, _ = projected.shape
    activated = convolve(projected, halo, conv_w, conv_b, reverse)
    spans = rows // Q
    inside, state, total, from_start = block_terms(activated, step_size, rates, reverse)
    order = list(range(spans))
    if reverse:
        order = order[::-1]
    before = {}
    sofar = (jnp.ones((count, H), jnp.float32), jnp.zeros((count, H, P_SIZE, N), jnp.float32))
    for j in order:
        before[j] = sofar
        sofar = chain(sofar, (total[:, j], state[:, j]))
    before_decay = jnp.stack([before[j][0] for j in range(spans)], axis=1)
    before_state = jnp.stack([before[j][1] for j in range(spans)], axis=1)
    pending = (before_decay, before_state, inside, from_start, activated)
    return sofar, pending


def finish(pending, incoming, gate_part, d_skip, norm_gain):
    before_decay, before_state, inside, from_start, activated = pending
    inner = H * P_SIZE
    count, rows, _ = activated.shape
    spans = rows // Q
    start_state = before_state + before_decay[..., None, None] * incoming[:, None]
    c_rows = activated[:, :, inner + N :].reshape(count, spans, Q, N)
    carried = jnp.einsum(
        "gjtn,gjkn->gjtk",
        c_rows.astype(jnp.float32),
        start_state.reshape(count, spans, inner, N),
        precision=lax.Precision.HIGHEST,
    ).reshape(count, rows, inner)
    heads = lax.broadcasted_iota(jnp.int32, (H, inner), 0)
    lanes = lax.broadcasted_iota(jnp.int32, (H, inner), 1)
    spread = (lanes // P_SIZE == heads).astype(jnp.float32)
    scale = jnp.einsum(
        "grh,hk->grk", from_start.reshape(count, rows, H), spread, precision=lax.Precision.HIGHEST
    )
    skip = jnp.repeat(d_skip, P_SIZE)
    scanned = inside + scale * carried + skip * activated[:, :, :inner].astype(jnp.float32)
    gated = scanned * jax.nn.silu(gate_part)
    return (
        gated
        * lax.rsqrt(jnp.mean(gated * gated, axis=-1, keepdims=True) + norm_epsilon)
        * norm_gain
    ).astype(jnp.bfloat16)


def on_device(
    tokens, hidden, base_table, w_in, w_dt, conv_w, conv_b, dt_bias, a_log, d_skip, norm_gain, w_out
):
    inner = H * P_SIZE
    margin = KCONV - 1
    one_hot = (tokens[:, :, None] == jnp.arange(4)[None, None, :]).astype(jnp.bfloat16)
    looked = jnp.einsum("gtb,bd->gtd", one_hot, base_table, preferred_element_type=jnp.float32)
    strand = (hidden.astype(jnp.float32) + looked).astype(jnp.bfloat16)
    rows = strand.shape[1]
    count = lax.axis_size("seq")
    low = lax.ppermute(strand[:, rows - margin :], "seq", [(i, i + 1) for i in range(count - 1)])
    high = lax.ppermute(strand[:, :margin], "seq", [(i + 1, i) for i in range(count - 1)])
    w_source = w_in[:, inner:]
    rates = -jnp.exp(a_log)
    proj_f = jnp.einsum("grd,de->gre", strand, w_in, preferred_element_type=jnp.float32)
    halo_f = jnp.einsum("grd,de->gre", low, w_source, preferred_element_type=jnp.float32)
    step_f = jax.nn.softplus(
        jnp.einsum("grd,dh->grh", strand, w_dt, preferred_element_type=jnp.float32) + dt_bias
    )
    sum_f, pend_f = strand_terms(proj_f, halo_f, step_f, conv_w, conv_b, rates, False)
    sum_f, (strand_late, high) = lax.optimization_barrier((sum_f, (strand, high)))
    mirrored = flip_lanes(strand_late)
    high_mirrored = flip_lanes(high)
    proj_r = jnp.einsum("grd,de->gre", mirrored, w_in, preferred_element_type=jnp.float32)
    halo_r = jnp.einsum("grd,de->gre", high_mirrored, w_source, preferred_element_type=jnp.float32)
    step_r = jax.nn.softplus(
        jnp.einsum("grd,dh->grh", mirrored, w_dt, preferred_element_type=jnp.float32) + dt_bias
    )
    sum_r, pend_r = strand_terms(proj_r, halo_r, step_r, conv_w, conv_b, rates, True)
    in_f, in_r = exclusive_scans(sum_f, sum_r, "seq")
    normed_f = finish(pend_f, in_f[1], proj_f[:, :, :inner], d_skip, norm_gain)
    normed_r = finish(pend_r, in_r[1], proj_r[:, :, :inner], d_skip, norm_gain)
    w_out_mirrored = flip_lanes(w_out)
    out = jnp.einsum(
        "grk,kd->grd", normed_f, w_out, preferred_element_type=jnp.float32
    ) + jnp.einsum("grk,kd->grd", normed_r, w_out_mirrored, preferred_element_type=jnp.float32)
    return out.astype(jnp.bfloat16)


def solution(mesh):
    placed = (
        P(("groups", "batch"), "seq"),
        P(("groups", "batch"), "seq", None),
        P(),
        P(),
        P(),
        P(),
        P(),
        P(),
        P(),
        P(),
        P(),
        P(),
    )
    return jax.shard_map(
        on_device,
        mesh=mesh,
        in_specs=placed,
        out_specs=P(("groups", "batch"), "seq", None),
        check_vma=False,
    )
```

```python
from functools import partial

import jax
import jax.numpy as jnp
from jax import lax
from jax.experimental import pallas as pl
from jax.experimental.pallas import tpu as pltpu
from jax.sharding import PartitionSpec as P

H = 16
P_SIZE = 64
N = 128
Q = 256
KCONV = 4


norm_epsilon = 1e-05


def exchange(size, dtype):
    row = lax.broadcasted_iota(jnp.int32, (size, size), 0)
    col = lax.broadcasted_iota(jnp.int32, (size, size), 1)
    return (row + col == size - 1).astype(dtype)


def flip_lanes(a):
    j = exchange(a.shape[-1], a.dtype)
    return jnp.einsum("...d,de->...e", a, j, preferred_element_type=jnp.float32).astype(a.dtype)


def chain(earlier, later):
    first_decay, first_state = earlier
    next_decay, next_state = later
    return (first_decay * next_decay, next_decay[..., None, None] * first_state + next_state)


def exclusive_scans(fwd, rev, axis):
    count = lax.axis_size(axis)
    place = lax.axis_index(axis)
    seen = [None, None]
    ahead = [fwd, rev]
    shift = 1
    while shift < count:
        up = [(i, i + shift) for i in range(count - shift)]
        down = [(i + shift, i) for i in range(count - shift)]
        got = []
        for k, pairs in ((0, up), (1, down)):
            decay, state = unpack(lax.ppermute(pack(*ahead[k]), axis, pairs))
            has = (place >= shift) if k == 0 else (place < count - shift)
            decay = jnp.where(has, decay, 1.0)
            got.append((decay, state))
        for k in range(2):
            seen[k] = got[k] if seen[k] is None else chain(got[k], seen[k])
            if 2 * shift < count:
                ahead[k] = chain(got[k], ahead[k])
        shift *= 2
    if seen[0] is None:
        return fwd_identity(fwd), fwd_identity(rev)
    return seen[0], seen[1]


def pack(decay, state):
    count = state.shape[0]
    flat = state.reshape(count, H * P_SIZE, N)
    extra = jnp.zeros((count, 8, N), jnp.float32).at[:, 0, :H].set(decay)
    return jnp.concatenate([flat, extra], axis=1)


def unpack(packed):
    count = packed.shape[0]
    rows = H * P_SIZE
    return packed[:, rows, :H], packed[:, :rows].reshape(count, H, P_SIZE, N)


def fwd_identity(summary):
    decay, state = summary
    return (jnp.ones_like(decay), jnp.zeros_like(state))


def inside_kernel(xbc_ref, cum_ref, cum_t_ref, step_t_ref, inside_ref, *, reverse):
    inner = H * P_SIZE
    b_rows = xbc_ref[:, inner : inner + N]
    c_rows = xbc_ref[:, inner + N :]
    scores = lax.dot_general(
        c_rows, b_rows, (((1,), (1,)), ((), ())), preferred_element_type=jnp.float32
    )
    t_idx = lax.broadcasted_iota(jnp.int32, (Q, Q), 0)
    s_idx = lax.broadcasted_iota(jnp.int32, (Q, Q), 1)
    keep = (s_idx >= t_idx) if reverse else (t_idx >= s_idx)
    for h in range(H):
        gaps = cum_ref[:, h : h + 1] - cum_t_ref[h : h + 1, :]
        decays = jnp.where(keep, jnp.exp(jnp.where(keep, gaps, 0.0)), 0.0)
        weights = (decays * scores * step_t_ref[h : h + 1, :]).astype(jnp.bfloat16)
        x_h = xbc_ref[:, h * P_SIZE : (h + 1) * P_SIZE]
        inside_ref[:, h * P_SIZE : (h + 1) * P_SIZE] = jnp.dot(
            weights, x_h, preferred_element_type=jnp.float32
        )


def state_kernel(xbc_ref, to_end_ref, state_ref):
    inner = H * P_SIZE
    b_wide = xbc_ref[:, inner : inner + N].astype(jnp.float32)
    for h in range(H):
        state_weights = (b_wide * to_end_ref[:, h : h + 1]).astype(jnp.bfloat16)
        x_h = xbc_ref[:, h * P_SIZE : (h + 1) * P_SIZE]
        state_ref[h] = lax.dot_general(
            x_h, state_weights, (((0,), (0,)), ((), ())), preferred_element_type=jnp.float32
        )


def block_terms(activated, step_size, rates, reverse):
    count, rows, width = activated.shape
    spans = rows // Q
    blocks = count * spans
    steps_cut = step_size.reshape(count, spans, Q, H)
    rated = steps_cut * rates
    log_decay = jnp.cumsum(rated, axis=2)
    if reverse:
        log_decay = log_decay[:, :, -1:] - log_decay + rated
    end = log_decay[:, :, 0] if reverse else log_decay[:, :, -1]
    to_end = jnp.exp(end[:, :, None, :] - log_decay) * steps_cut
    flat = lambda a: a.reshape((blocks,) + a.shape[2:])
    cum = flat(log_decay)
    cum_t = jnp.swapaxes(cum, 1, 2)
    step_t = jnp.swapaxes(flat(steps_cut), 1, 2)
    xbc = activated.reshape(blocks, Q, width)
    spec = lambda shape: pl.BlockSpec((None,) + shape, lambda i: (i,) + (0,) * len(shape))
    state = pl.pallas_call(
        state_kernel,
        grid=(blocks,),
        in_specs=[spec((Q, width)), spec((Q, H))],
        out_specs=spec((H, P_SIZE, N)),
        out_shape=jax.ShapeDtypeStruct((blocks, H, P_SIZE, N), jnp.float32),
    )(xbc, flat(to_end))
    inside = pl.pallas_call(
        partial(inside_kernel, reverse=reverse),
        grid=(blocks,),
        in_specs=[spec((Q, width)), spec((Q, H)), spec((H, Q)), spec((H, Q))],
        out_specs=spec((Q, H * P_SIZE)),
        out_shape=jax.ShapeDtypeStruct((blocks, Q, H * P_SIZE), jnp.float32),
    )(xbc, cum, cum_t, step_t)
    inside = inside.reshape(count, rows, H * P_SIZE)
    state = state.reshape(count, spans, H, P_SIZE, N)
    return inside, state, jnp.exp(end), jnp.exp(log_decay)


CONV_LANES = 256


def conv_kernel(src_ref, halo_ref, w_ref, b_ref, out_ref, *, reverse):
    margin = KCONV - 1
    src = src_ref[...]
    rows = src.shape[0]
    edge = halo_ref.shape[0]
    w = w_ref[...]
    if reverse:
        near = jnp.concatenate([src[rows - edge :], halo_ref[...]], axis=0)
    else:
        near = jnp.concatenate([halo_ref[...], src[:edge]], axis=0)
    span = near.shape[0]
    main = jnp.broadcast_to(b_ref[...], src.shape)
    side = jnp.broadcast_to(b_ref[...], (edge, src.shape[1]))
    for tap in range(KCONV):
        shift = margin - tap
        if shift == 0:
            piece, near_piece = src, near
        elif reverse:
            piece = pltpu.roll(src, rows - shift, 0)
            near_piece = pltpu.roll(near, span - shift, 0)
        else:
            piece = pltpu.roll(src, shift, 0)
            near_piece = pltpu.roll(near, shift, 0)
        main = main + w[tap : tap + 1] * piece
        part = near_piece[:edge] if reverse else near_piece[edge:]
        side = side + w[tap : tap + 1] * part
    out_ref[...] = jax.nn.silu(main).astype(out_ref.dtype)
    if reverse:
        out_ref[rows - edge :, :] = jax.nn.silu(side).astype(out_ref.dtype)
    else:
        out_ref[:edge, :] = jax.nn.silu(side).astype(out_ref.dtype)


def convolve(projected, rows, conv_w, conv_b, reverse):
    inner = H * P_SIZE
    count = projected.shape[0]
    width = conv_w.shape[1]
    edge = 8
    lanes = CONV_LANES
    skip = inner // lanes
    return pl.pallas_call(
        partial(conv_kernel, reverse=reverse),
        grid=(count, width // lanes),
        in_specs=[
            pl.BlockSpec((None, rows, lanes), lambda g, j: (g, 0, j + skip)),
            pl.BlockSpec((None, edge, lanes), lambda g, j: (g, rows // edge, j + skip)),
            pl.BlockSpec((KCONV, lanes), lambda g, j: (0, j)),
            pl.BlockSpec((1, lanes), lambda g, j: (0, j)),
        ],
        out_specs=pl.BlockSpec((None, rows, lanes), lambda g, j: (g, 0, j)),
        out_shape=jax.ShapeDtypeStruct((count, rows, width), jnp.bfloat16),
    )(projected, projected, conv_w, conv_b.reshape(1, width))


def strand_terms(projected, step_size, conv_w, conv_b, rates, reverse):
    inner = H * P_SIZE
    count, rows, _ = step_size.shape
    activated = convolve(projected, rows, conv_w, conv_b, reverse)
    spans = rows // Q
    inside, state, total, from_start = block_terms(activated, step_size, rates, reverse)
    order = list(range(spans))
    if reverse:
        order = order[::-1]
    before = {}
    sofar = (jnp.ones((count, H), jnp.float32), jnp.zeros((count, H, P_SIZE, N), jnp.float32))
    for j in order:
        before[j] = sofar
        sofar = chain(sofar, (total[:, j], state[:, j]))
    before_decay = jnp.stack([before[j][0] for j in range(spans)], axis=1)
    before_state = jnp.stack([before[j][1] for j in range(spans)], axis=1)
    pending = (before_decay, before_state, inside, from_start, activated)
    return sofar, pending


def finish(pending, incoming, gate_part, d_skip, norm_gain):
    before_decay, before_state, inside, from_start, activated = pending
    inner = H * P_SIZE
    count, rows, _ = activated.shape
    spans = rows // Q
    start_state = before_state + before_decay[..., None, None] * incoming[:, None]
    c_rows = activated[:, :, inner + N :].reshape(count, spans, Q, N)
    carried = jnp.einsum(
        "gjtn,gjkn->gjtk",
        c_rows.astype(jnp.float32),
        start_state.reshape(count, spans, inner, N),
        precision=lax.Precision.HIGHEST,
    ).reshape(count, rows, inner)
    heads = lax.broadcasted_iota(jnp.int32, (H, inner), 0)
    lanes = lax.broadcasted_iota(jnp.int32, (H, inner), 1)
    spread = (lanes // P_SIZE == heads).astype(jnp.float32)
    scale = jnp.einsum(
        "grh,hk->grk", from_start.reshape(count, rows, H), spread, precision=lax.Precision.HIGHEST
    )
    skip = jnp.repeat(d_skip, P_SIZE)
    scanned = inside + scale * carried + skip * activated[:, :, :inner].astype(jnp.float32)
    gated = scanned * jax.nn.silu(gate_part)
    return (
        gated
        * lax.rsqrt(jnp.mean(gated * gated, axis=-1, keepdims=True) + norm_epsilon)
        * norm_gain
    ).astype(jnp.bfloat16)


def on_device(
    tokens, hidden, base_table, w_in, w_dt, conv_w, conv_b, dt_bias, a_log, d_skip, norm_gain, w_out
):
    inner = H * P_SIZE
    margin = KCONV - 1
    one_hot = (tokens[:, :, None] == jnp.arange(4)[None, None, :]).astype(jnp.bfloat16)
    looked = jnp.einsum("gtb,bd->gtd", one_hot, base_table, preferred_element_type=jnp.float32)
    strand = (hidden.astype(jnp.float32) + looked).astype(jnp.bfloat16)
    rows = strand.shape[1]
    count = lax.axis_size("seq")
    low = lax.ppermute(strand[:, rows - margin :], "seq", [(i, i + 1) for i in range(count - 1)])
    high = lax.ppermute(strand[:, :margin], "seq", [(i + 1, i) for i in range(count - 1)])
    rates = -jnp.exp(a_log)
    gap = jnp.zeros((strand.shape[0], 8 - margin, strand.shape[2]), strand.dtype)
    ext_f = jnp.concatenate([strand, gap, low], axis=1)
    proj_f = jnp.einsum("grd,de->gre", ext_f, w_in, preferred_element_type=jnp.float32)
    step_f = jax.nn.softplus(
        jnp.einsum("grd,dh->grh", strand, w_dt, preferred_element_type=jnp.float32) + dt_bias
    )
    sum_f, pend_f = strand_terms(proj_f, step_f, conv_w, conv_b, rates, False)
    sum_f, (strand_late, high) = lax.optimization_barrier((sum_f, (strand, high)))
    ext_r = flip_lanes(jnp.concatenate([strand_late, high, gap], axis=1))
    mirrored = ext_r[:, :rows]
    proj_r = jnp.einsum("grd,de->gre", ext_r, w_in, preferred_element_type=jnp.float32)
    step_r = jax.nn.softplus(
        jnp.einsum("grd,dh->grh", mirrored, w_dt, preferred_element_type=jnp.float32) + dt_bias
    )
    sum_r, pend_r = strand_terms(proj_r, step_r, conv_w, conv_b, rates, True)
    in_f, in_r = exclusive_scans(sum_f, sum_r, "seq")
    normed_f = finish(pend_f, in_f[1], proj_f[:, :rows, :inner], d_skip, norm_gain)
    normed_r = finish(pend_r, in_r[1], proj_r[:, :rows, :inner], d_skip, norm_gain)
    w_out_mirrored = flip_lanes(w_out)
    out = jnp.einsum(
        "grk,kd->grd", normed_f, w_out, preferred_element_type=jnp.float32
    ) + jnp.einsum("grk,kd->grd", normed_r, w_out_mirrored, preferred_element_type=jnp.float32)
    return out.astype(jnp.bfloat16)


def solution(mesh):
    placed = (
        P(("groups", "batch"), "seq"),
        P(("groups", "batch"), "seq", None),
        P(),
        P(),
        P(),
        P(),
        P(),
        P(),
        P(),
        P(),
        P(),
        P(),
    )
    return jax.shard_map(
        on_device,
        mesh=mesh,
        in_specs=placed,
        out_specs=P(("groups", "batch"), "seq", None),
        check_vma=False,
    )
```

```python
from functools import partial

import jax
import jax.numpy as jnp
from jax import lax
from jax.experimental import pallas as pl
from jax.experimental.pallas import tpu as pltpu
from jax.sharding import PartitionSpec as P

H = 16
P_SIZE = 64
N = 128
Q = 256
KCONV = 4


norm_epsilon = 1e-05


def exchange(size, dtype):
    row = lax.broadcasted_iota(jnp.int32, (size, size), 0)
    col = lax.broadcasted_iota(jnp.int32, (size, size), 1)
    return (row + col == size - 1).astype(dtype)


def flip_lanes(a):
    j = exchange(a.shape[-1], a.dtype)
    return jnp.einsum("...d,de->...e", a, j, preferred_element_type=jnp.float32).astype(a.dtype)


def chain(earlier, later):
    first_decay, first_state = earlier
    next_decay, next_state = later
    return (first_decay * next_decay, next_decay[..., None, None] * first_state + next_state)


def exclusive_scans(fwd, rev, axis, after_fwd):
    count = lax.axis_size(axis)
    place = lax.axis_index(axis)
    seen = [None, None]
    ahead = [fwd, rev]
    shift = 1
    while shift < count:
        up = [(i, i + shift) for i in range(count - shift)]
        down = [(i + shift, i) for i in range(count - shift)]
        got = []
        for k, pairs in ((0, up), (1, down)):
            decay, state = unpack(lax.ppermute(pack(*ahead[k]), axis, pairs))
            has = (place >= shift) if k == 0 else (place < count - shift)
            decay = jnp.where(has, decay, 1.0)
            got.append((decay, state))
        last = 2 * shift >= count
        for k in range(2):
            if k == 1 and last:
                tail = after_fwd(seen[0][1])
                got[1], tail = lax.optimization_barrier((got[1], tail))
            seen[k] = got[k] if seen[k] is None else chain(got[k], seen[k])
            if not last:
                ahead[k] = chain(got[k], ahead[k])
        shift *= 2
    if seen[0] is None:
        return fwd_identity(rev), after_fwd(fwd_identity(fwd)[1])
    return seen[1], tail


def pack(decay, state):
    count = state.shape[0]
    flat = state.reshape(count, H * P_SIZE, N)
    extra = jnp.zeros((count, 8, N), jnp.float32).at[:, 0, :H].set(decay)
    return jnp.concatenate([flat, extra], axis=1)


def unpack(packed):
    count = packed.shape[0]
    rows = H * P_SIZE
    return packed[:, rows, :H], packed[:, :rows].reshape(count, H, P_SIZE, N)


def fwd_identity(summary):
    decay, state = summary
    return (jnp.ones_like(decay), jnp.zeros_like(state))


def inside_kernel(xbc_ref, cum_ref, cum_t_ref, step_t_ref, inside_ref, *, reverse):
    inner = H * P_SIZE
    b_rows = xbc_ref[:, inner : inner + N]
    c_rows = xbc_ref[:, inner + N :]
    scores = lax.dot_general(
        c_rows, b_rows, (((1,), (1,)), ((), ())), preferred_element_type=jnp.float32
    )
    t_idx = lax.broadcasted_iota(jnp.int32, (Q, Q), 0)
    s_idx = lax.broadcasted_iota(jnp.int32, (Q, Q), 1)
    keep = (s_idx >= t_idx) if reverse else (t_idx >= s_idx)
    for h in range(H):
        gaps = cum_ref[:, h : h + 1] - cum_t_ref[h : h + 1, :]
        decays = jnp.where(keep, jnp.exp(jnp.where(keep, gaps, 0.0)), 0.0)
        weights = (decays * scores * step_t_ref[h : h + 1, :]).astype(jnp.bfloat16)
        x_h = xbc_ref[:, h * P_SIZE : (h + 1) * P_SIZE]
        inside_ref[:, h * P_SIZE : (h + 1) * P_SIZE] = jnp.dot(
            weights, x_h, preferred_element_type=jnp.float32
        )


def state_kernel(xbc_ref, to_end_ref, state_ref):
    inner = H * P_SIZE
    b_wide = xbc_ref[:, inner : inner + N].astype(jnp.float32)
    for h in range(H):
        state_weights = (b_wide * to_end_ref[:, h : h + 1]).astype(jnp.bfloat16)
        x_h = xbc_ref[:, h * P_SIZE : (h + 1) * P_SIZE]
        state_ref[h] = lax.dot_general(
            x_h, state_weights, (((0,), (0,)), ((), ())), preferred_element_type=jnp.float32
        )


def block_terms(activated, step_size, rates, reverse):
    count, rows, width = activated.shape
    spans = rows // Q
    blocks = count * spans
    steps_cut = step_size.reshape(count, spans, Q, H)
    rated = steps_cut * rates
    log_decay = jnp.cumsum(rated, axis=2)
    if reverse:
        log_decay = log_decay[:, :, -1:] - log_decay + rated
    end = log_decay[:, :, 0] if reverse else log_decay[:, :, -1]
    to_end = jnp.exp(end[:, :, None, :] - log_decay) * steps_cut
    flat = lambda a: a.reshape((blocks,) + a.shape[2:])
    cum = flat(log_decay)
    cum_t = jnp.swapaxes(cum, 1, 2)
    step_t = jnp.swapaxes(flat(steps_cut), 1, 2)
    xbc = activated.reshape(blocks, Q, width)
    spec = lambda shape: pl.BlockSpec((None,) + shape, lambda i: (i,) + (0,) * len(shape))
    state = pl.pallas_call(
        state_kernel,
        grid=(blocks,),
        in_specs=[spec((Q, width)), spec((Q, H))],
        out_specs=spec((H, P_SIZE, N)),
        out_shape=jax.ShapeDtypeStruct((blocks, H, P_SIZE, N), jnp.float32),
    )(xbc, flat(to_end))
    inside = pl.pallas_call(
        partial(inside_kernel, reverse=reverse),
        grid=(blocks,),
        in_specs=[spec((Q, width)), spec((Q, H)), spec((H, Q)), spec((H, Q))],
        out_specs=spec((Q, H * P_SIZE)),
        out_shape=jax.ShapeDtypeStruct((blocks, Q, H * P_SIZE), jnp.float32),
    )(xbc, cum, cum_t, step_t)
    inside = inside.reshape(count, rows, H * P_SIZE)
    state = state.reshape(count, spans, H, P_SIZE, N)
    return inside, state, jnp.exp(end), jnp.exp(log_decay)


CONV_LANES = 256


def conv_kernel(src_ref, halo_ref, w_ref, b_ref, out_ref, *, reverse):
    margin = KCONV - 1
    src = src_ref[...]
    rows = src.shape[0]
    edge = halo_ref.shape[0]
    w = w_ref[...]
    if reverse:
        near = jnp.concatenate([src[rows - edge :], halo_ref[...]], axis=0)
    else:
        near = jnp.concatenate([halo_ref[...], src[:edge]], axis=0)
    span = near.shape[0]
    main = jnp.broadcast_to(b_ref[...], src.shape)
    side = jnp.broadcast_to(b_ref[...], (edge, src.shape[1]))
    for tap in range(KCONV):
        shift = margin - tap
        if shift == 0:
            piece, near_piece = src, near
        elif reverse:
            piece = pltpu.roll(src, rows - shift, 0)
            near_piece = pltpu.roll(near, span - shift, 0)
        else:
            piece = pltpu.roll(src, shift, 0)
            near_piece = pltpu.roll(near, shift, 0)
        main = main + w[tap : tap + 1] * piece
        part = near_piece[:edge] if reverse else near_piece[edge:]
        side = side + w[tap : tap + 1] * part
    out_ref[...] = jax.nn.silu(main).astype(out_ref.dtype)
    if reverse:
        out_ref[rows - edge :, :] = jax.nn.silu(side).astype(out_ref.dtype)
    else:
        out_ref[:edge, :] = jax.nn.silu(side).astype(out_ref.dtype)


def convolve(projected, rows, conv_w, conv_b, reverse):
    inner = H * P_SIZE
    count = projected.shape[0]
    width = conv_w.shape[1]
    edge = 8
    lanes = CONV_LANES
    skip = inner // lanes
    return pl.pallas_call(
        partial(conv_kernel, reverse=reverse),
        grid=(count, width // lanes),
        in_specs=[
            pl.BlockSpec((None, rows, lanes), lambda g, j: (g, 0, j + skip)),
            pl.BlockSpec((None, edge, lanes), lambda g, j: (g, rows // edge, j + skip)),
            pl.BlockSpec((KCONV, lanes), lambda g, j: (0, j)),
            pl.BlockSpec((1, lanes), lambda g, j: (0, j)),
        ],
        out_specs=pl.BlockSpec((None, rows, lanes), lambda g, j: (g, 0, j)),
        out_shape=jax.ShapeDtypeStruct((count, rows, width), jnp.bfloat16),
    )(projected, projected, conv_w, conv_b.reshape(1, width))


def strand_terms(projected, step_size, conv_w, conv_b, rates, reverse):
    inner = H * P_SIZE
    count, rows, _ = step_size.shape
    activated = convolve(projected, rows, conv_w, conv_b, reverse)
    spans = rows // Q
    inside, state, total, from_start = block_terms(activated, step_size, rates, reverse)
    order = list(range(spans))
    if reverse:
        order = order[::-1]
    before = {}
    sofar = (jnp.ones((count, H), jnp.float32), jnp.zeros((count, H, P_SIZE, N), jnp.float32))
    for j in order:
        before[j] = sofar
        sofar = chain(sofar, (total[:, j], state[:, j]))
    before_decay = jnp.stack([before[j][0] for j in range(spans)], axis=1)
    before_state = jnp.stack([before[j][1] for j in range(spans)], axis=1)
    pending = (before_decay, before_state, inside, from_start, activated)
    return sofar, pending


def finish(pending, incoming, gate_part, d_skip, norm_gain):
    before_decay, before_state, inside, from_start, activated = pending
    inner = H * P_SIZE
    count, rows, _ = activated.shape
    spans = rows // Q
    start_state = before_state + before_decay[..., None, None] * incoming[:, None]
    c_rows = activated[:, :, inner + N :].reshape(count, spans, Q, N)
    carried = jnp.einsum(
        "gjtn,gjkn->gjtk",
        c_rows.astype(jnp.float32),
        start_state.reshape(count, spans, inner, N),
        precision=lax.Precision.HIGHEST,
    ).reshape(count, rows, inner)
    heads = lax.broadcasted_iota(jnp.int32, (H, inner), 0)
    lanes = lax.broadcasted_iota(jnp.int32, (H, inner), 1)
    spread = (lanes // P_SIZE == heads).astype(jnp.float32)
    scale = jnp.einsum(
        "grh,hk->grk", from_start.reshape(count, rows, H), spread, precision=lax.Precision.HIGHEST
    )
    skip = jnp.repeat(d_skip, P_SIZE)
    scanned = inside + scale * carried + skip * activated[:, :, :inner].astype(jnp.float32)
    gated = scanned * jax.nn.silu(gate_part)
    return (
        gated
        * lax.rsqrt(jnp.mean(gated * gated, axis=-1, keepdims=True) + norm_epsilon)
        * norm_gain
    ).astype(jnp.bfloat16)


def on_device(
    tokens, hidden, base_table, w_in, w_dt, conv_w, conv_b, dt_bias, a_log, d_skip, norm_gain, w_out
):
    inner = H * P_SIZE
    margin = KCONV - 1
    one_hot = (tokens[:, :, None] == jnp.arange(4)[None, None, :]).astype(jnp.bfloat16)
    looked = jnp.einsum("gtb,bd->gtd", one_hot, base_table, preferred_element_type=jnp.float32)
    strand = (hidden.astype(jnp.float32) + looked).astype(jnp.bfloat16)
    rows = strand.shape[1]
    count = lax.axis_size("seq")
    low = lax.ppermute(strand[:, rows - margin :], "seq", [(i, i + 1) for i in range(count - 1)])
    high = lax.ppermute(strand[:, :margin], "seq", [(i + 1, i) for i in range(count - 1)])
    rates = -jnp.exp(a_log)
    gap = jnp.zeros((strand.shape[0], 8 - margin, strand.shape[2]), strand.dtype)
    ext_f = jnp.concatenate([strand, gap, low], axis=1)
    proj_f = jnp.einsum("grd,de->gre", ext_f, w_in, preferred_element_type=jnp.float32)
    step_f = jax.nn.softplus(
        jnp.einsum("grd,dh->grh", strand, w_dt, preferred_element_type=jnp.float32) + dt_bias
    )
    sum_f, pend_f = strand_terms(proj_f, step_f, conv_w, conv_b, rates, False)
    sum_f, (strand_late, high) = lax.optimization_barrier((sum_f, (strand, high)))
    ext_r = flip_lanes(jnp.concatenate([strand_late, high, gap], axis=1))
    mirrored = ext_r[:, :rows]
    proj_r = jnp.einsum("grd,de->gre", ext_r, w_in, preferred_element_type=jnp.float32)
    step_r = jax.nn.softplus(
        jnp.einsum("grd,dh->grh", mirrored, w_dt, preferred_element_type=jnp.float32) + dt_bias
    )
    sum_r, pend_r = strand_terms(proj_r, step_r, conv_w, conv_b, rates, True)
    def forward_out(incoming):
        normed_f = finish(pend_f, incoming, proj_f[:, :rows, :inner], d_skip, norm_gain)
        return jnp.einsum("grk,kd->grd", normed_f, w_out, preferred_element_type=jnp.float32)

    in_r, out_f = exclusive_scans(sum_f, sum_r, "seq", forward_out)
    normed_r = finish(pend_r, in_r[1], proj_r[:, :rows, :inner], d_skip, norm_gain)
    w_out_mirrored = flip_lanes(w_out)
    out = out_f + jnp.einsum(
        "grk,kd->grd", normed_r, w_out_mirrored, preferred_element_type=jnp.float32
    )
    return out.astype(jnp.bfloat16)


def solution(mesh):
    placed = (
        P(("groups", "batch"), "seq"),
        P(("groups", "batch"), "seq", None),
        P(),
        P(),
        P(),
        P(),
        P(),
        P(),
        P(),
        P(),
        P(),
        P(),
    )
    return jax.shard_map(
        on_device,
        mesh=mesh,
        in_specs=placed,
        out_specs=P(("groups", "batch"), "seq", None),
        check_vma=False,
    )
```

```python
from functools import partial

import jax
import jax.numpy as jnp
from jax import lax
from jax.experimental import pallas as pl
from jax.experimental.pallas import tpu as pltpu
from jax.sharding import PartitionSpec as P

H = 16
P_SIZE = 64
N = 128
Q = 256
KCONV = 4


norm_epsilon = 1e-05


def exchange(size, dtype):
    row = lax.broadcasted_iota(jnp.int32, (size, size), 0)
    col = lax.broadcasted_iota(jnp.int32, (size, size), 1)
    return (row + col == size - 1).astype(dtype)


def flip_lanes(a):
    j = exchange(a.shape[-1], a.dtype)
    return jnp.einsum("...d,de->...e", a, j, preferred_element_type=jnp.float32).astype(a.dtype)


def chain(earlier, later):
    first_decay, first_state = earlier
    next_decay, next_state = later
    return (first_decay * next_decay, next_decay[..., None, None] * first_state + next_state)


def exclusive_scans(fwd, rev, axis, after_fwd):
    count = lax.axis_size(axis)
    place = lax.axis_index(axis)
    seen = [None, None]
    ahead = [fwd, rev]
    shift = 1
    while shift < count:
        up = [(i, i + shift) for i in range(count - shift)]
        down = [(i + shift, i) for i in range(count - shift)]
        got = []
        for k, pairs in ((0, up), (1, down)):
            decay, state = unpack(lax.ppermute(pack(*ahead[k]), axis, pairs))
            has = (place >= shift) if k == 0 else (place < count - shift)
            decay = jnp.where(has, decay, 1.0)
            got.append((decay, state))
        last = 2 * shift >= count
        for k in range(2):
            if k == 1 and last:
                tail = after_fwd(seen[0][1])
                got[1], tail = lax.optimization_barrier((got[1], tail))
            seen[k] = got[k] if seen[k] is None else chain(got[k], seen[k])
            if not last:
                ahead[k] = chain(got[k], ahead[k])
        shift *= 2
    if seen[0] is None:
        return fwd_identity(rev), after_fwd(fwd_identity(fwd)[1])
    return seen[1], tail


def pack(decay, state):
    count = state.shape[0]
    flat = state.reshape(count, H * P_SIZE, N)
    extra = jnp.zeros((count, 8, N), jnp.float32).at[:, 0, :H].set(decay)
    return jnp.concatenate([flat, extra], axis=1)


def unpack(packed):
    count = packed.shape[0]
    rows = H * P_SIZE
    return packed[:, rows, :H], packed[:, :rows].reshape(count, H, P_SIZE, N)


def fwd_identity(summary):
    decay, state = summary
    return (jnp.ones_like(decay), jnp.zeros_like(state))


def inside_kernel(xbc_ref, cum_ref, cum_t_ref, step_t_ref, inside_ref, *, reverse):
    inner = H * P_SIZE
    b_rows = xbc_ref[:, inner : inner + N]
    c_rows = xbc_ref[:, inner + N :]
    scores = lax.dot_general(
        c_rows, b_rows, (((1,), (1,)), ((), ())), preferred_element_type=jnp.float32
    )
    t_idx = lax.broadcasted_iota(jnp.int32, (Q, Q), 0)
    s_idx = lax.broadcasted_iota(jnp.int32, (Q, Q), 1)
    keep = (s_idx >= t_idx) if reverse else (t_idx >= s_idx)
    for h in range(H):
        gaps = cum_ref[:, h : h + 1] - cum_t_ref[h : h + 1, :]
        decays = jnp.where(keep, jnp.exp(jnp.where(keep, gaps, 0.0)), 0.0)
        weights = (decays * scores * step_t_ref[h : h + 1, :]).astype(jnp.bfloat16)
        x_h = xbc_ref[:, h * P_SIZE : (h + 1) * P_SIZE]
        inside_ref[:, h * P_SIZE : (h + 1) * P_SIZE] = jnp.dot(
            weights, x_h, preferred_element_type=jnp.float32
        )


def state_kernel(xbc_ref, to_end_ref, state_ref):
    inner = H * P_SIZE
    b_wide = xbc_ref[:, inner : inner + N].astype(jnp.float32)
    for h in range(H):
        state_weights = (b_wide * to_end_ref[:, h : h + 1]).astype(jnp.bfloat16)
        x_h = xbc_ref[:, h * P_SIZE : (h + 1) * P_SIZE]
        state_ref[h] = lax.dot_general(
            x_h, state_weights, (((0,), (0,)), ((), ())), preferred_element_type=jnp.float32
        )


def block_terms(activated, step_size, rates, reverse):
    count, rows, width = activated.shape
    spans = rows // Q
    blocks = count * spans
    steps_cut = step_size.reshape(count, spans, Q, H)
    rated = steps_cut * rates
    log_decay = jnp.cumsum(rated, axis=2)
    if reverse:
        log_decay = log_decay[:, :, -1:] - log_decay + rated
    end = log_decay[:, :, 0] if reverse else log_decay[:, :, -1]
    to_end = jnp.exp(end[:, :, None, :] - log_decay) * steps_cut
    flat = lambda a: a.reshape((blocks,) + a.shape[2:])
    cum = flat(log_decay)
    cum_t = jnp.swapaxes(cum, 1, 2)
    step_t = jnp.swapaxes(flat(steps_cut), 1, 2)
    xbc = activated.reshape(blocks, Q, width)
    spec = lambda shape: pl.BlockSpec((None,) + shape, lambda i: (i,) + (0,) * len(shape))
    state = pl.pallas_call(
        state_kernel,
        grid=(blocks,),
        in_specs=[spec((Q, width)), spec((Q, H))],
        out_specs=spec((H, P_SIZE, N)),
        out_shape=jax.ShapeDtypeStruct((blocks, H, P_SIZE, N), jnp.float32),
    )(xbc, flat(to_end))
    inside = pl.pallas_call(
        partial(inside_kernel, reverse=reverse),
        grid=(blocks,),
        in_specs=[spec((Q, width)), spec((Q, H)), spec((H, Q)), spec((H, Q))],
        out_specs=spec((Q, H * P_SIZE)),
        out_shape=jax.ShapeDtypeStruct((blocks, Q, H * P_SIZE), jnp.float32),
    )(xbc, cum, cum_t, step_t)
    inside = inside.reshape(count, rows, H * P_SIZE)
    state = state.reshape(count, spans, H, P_SIZE, N)
    return inside, state, jnp.exp(end), jnp.exp(log_decay)


CONV_LANES = 256


def conv_kernel(src_ref, halo_ref, w_ref, b_ref, out_ref, *, reverse):
    margin = KCONV - 1
    src = src_ref[...]
    rows = src.shape[0]
    edge = halo_ref.shape[0]
    w = w_ref[...]
    if reverse:
        near = jnp.concatenate([src[rows - edge :], halo_ref[...]], axis=0)
    else:
        near = jnp.concatenate([halo_ref[...], src[:edge]], axis=0)
    span = near.shape[0]
    main = jnp.broadcast_to(b_ref[...], src.shape)
    side = jnp.broadcast_to(b_ref[...], (edge, src.shape[1]))
    for tap in range(KCONV):
        shift = margin - tap
        if shift == 0:
            piece, near_piece = src, near
        elif reverse:
            piece = pltpu.roll(src, rows - shift, 0)
            near_piece = pltpu.roll(near, span - shift, 0)
        else:
            piece = pltpu.roll(src, shift, 0)
            near_piece = pltpu.roll(near, shift, 0)
        main = main + w[tap : tap + 1] * piece
        part = near_piece[:edge] if reverse else near_piece[edge:]
        side = side + w[tap : tap + 1] * part
    out_ref[...] = jax.nn.silu(main).astype(out_ref.dtype)
    if reverse:
        out_ref[rows - edge :, :] = jax.nn.silu(side).astype(out_ref.dtype)
    else:
        out_ref[:edge, :] = jax.nn.silu(side).astype(out_ref.dtype)


def convolve(projected, rows, conv_w, conv_b, reverse):
    inner = H * P_SIZE
    count = projected.shape[0]
    width = conv_w.shape[1]
    edge = 8
    lanes = CONV_LANES
    skip = inner // lanes
    return pl.pallas_call(
        partial(conv_kernel, reverse=reverse),
        grid=(count, width // lanes),
        in_specs=[
            pl.BlockSpec((None, rows, lanes), lambda g, j: (g, 0, j + skip)),
            pl.BlockSpec((None, edge, lanes), lambda g, j: (g, rows // edge, j + skip)),
            pl.BlockSpec((KCONV, lanes), lambda g, j: (0, j)),
            pl.BlockSpec((1, lanes), lambda g, j: (0, j)),
        ],
        out_specs=pl.BlockSpec((None, rows, lanes), lambda g, j: (g, 0, j)),
        out_shape=jax.ShapeDtypeStruct((count, rows, width), jnp.bfloat16),
    )(projected, projected, conv_w, conv_b.reshape(1, width))


def strand_terms(projected, step_size, conv_w, conv_b, rates, reverse):
    inner = H * P_SIZE
    count, rows, _ = step_size.shape
    activated = convolve(projected, rows, conv_w, conv_b, reverse)
    spans = rows // Q
    inside, state, total, from_start = block_terms(activated, step_size, rates, reverse)
    order = list(range(spans))
    if reverse:
        order = order[::-1]
    before = {}
    sofar = (jnp.ones((count, H), jnp.float32), jnp.zeros((count, H, P_SIZE, N), jnp.float32))
    for j in order:
        before[j] = sofar
        sofar = chain(sofar, (total[:, j], state[:, j]))
    before_decay = jnp.stack([before[j][0] for j in range(spans)], axis=1)
    before_state = jnp.stack([before[j][1] for j in range(spans)], axis=1)
    pending = (before_decay, before_state, inside, from_start, activated)
    return sofar, pending


def finish(pending, incoming, gate_part, d_skip, norm_gain):
    before_decay, before_state, inside, from_start, activated = pending
    inner = H * P_SIZE
    count, rows, _ = activated.shape
    spans = rows // Q
    start_state = before_state + before_decay[..., None, None] * incoming[:, None]
    c_rows = activated[:, :, inner + N :].reshape(count, spans, Q, N)
    carried = jnp.einsum(
        "gjtn,gjkn->gjtk",
        c_rows.astype(jnp.float32),
        start_state.reshape(count, spans, inner, N),
        precision=lax.Precision.HIGHEST,
    ).reshape(count, rows, inner)
    heads = lax.broadcasted_iota(jnp.int32, (H, inner), 0)
    lanes = lax.broadcasted_iota(jnp.int32, (H, inner), 1)
    spread = (lanes // P_SIZE == heads).astype(jnp.float32)
    scale = jnp.einsum(
        "grh,hk->grk", from_start.reshape(count, rows, H), spread, precision=lax.Precision.HIGHEST
    )
    skip = jnp.repeat(d_skip, P_SIZE)
    scanned = inside + scale * carried + skip * activated[:, :, :inner].astype(jnp.float32)
    gated = scanned * jax.nn.silu(gate_part)
    return (
        gated
        * lax.rsqrt(jnp.mean(gated * gated, axis=-1, keepdims=True) + norm_epsilon)
        * norm_gain
    ).astype(jnp.bfloat16)


def project_kernel(a_ref, w_ref, add_ref, out_ref):
    total = add_ref[...] + jnp.dot(a_ref[...], w_ref[...], preferred_element_type=jnp.float32)
    out_ref[...] = total.astype(out_ref.dtype)


def project_add(normed, w, addend, lanes=256):
    count, rows, depth = normed.shape
    width = w.shape[1]
    return pl.pallas_call(
        project_kernel,
        grid=(count, width // lanes),
        in_specs=[
            pl.BlockSpec((None, rows, depth), lambda g, j: (g, 0, 0)),
            pl.BlockSpec((depth, lanes), lambda g, j: (0, j)),
            pl.BlockSpec((None, rows, lanes), lambda g, j: (g, 0, j)),
        ],
        out_specs=pl.BlockSpec((None, rows, lanes), lambda g, j: (g, 0, j)),
        out_shape=jax.ShapeDtypeStruct((count, rows, width), jnp.bfloat16),
    )(normed, w, addend)


def on_device(
    tokens, hidden, base_table, w_in, w_dt, conv_w, conv_b, dt_bias, a_log, d_skip, norm_gain, w_out
):
    inner = H * P_SIZE
    margin = KCONV - 1
    one_hot = (tokens[:, :, None] == jnp.arange(4)[None, None, :]).astype(jnp.bfloat16)
    looked = jnp.einsum("gtb,bd->gtd", one_hot, base_table, preferred_element_type=jnp.float32)
    strand = (hidden.astype(jnp.float32) + looked).astype(jnp.bfloat16)
    rows = strand.shape[1]
    count = lax.axis_size("seq")
    low = lax.ppermute(strand[:, rows - margin :], "seq", [(i, i + 1) for i in range(count - 1)])
    high = lax.ppermute(strand[:, :margin], "seq", [(i + 1, i) for i in range(count - 1)])
    rates = -jnp.exp(a_log)
    gap = jnp.zeros((strand.shape[0], 8 - margin, strand.shape[2]), strand.dtype)
    ext_f = jnp.concatenate([strand, gap, low], axis=1)
    proj_f = jnp.einsum("grd,de->gre", ext_f, w_in, preferred_element_type=jnp.float32)
    step_f = jax.nn.softplus(
        jnp.einsum("grd,dh->grh", strand, w_dt, preferred_element_type=jnp.float32) + dt_bias
    )
    sum_f, pend_f = strand_terms(proj_f, step_f, conv_w, conv_b, rates, False)
    sum_f, (strand_late, high) = lax.optimization_barrier((sum_f, (strand, high)))
    ext_r = flip_lanes(jnp.concatenate([strand_late, high, gap], axis=1))
    mirrored = ext_r[:, :rows]
    proj_r = jnp.einsum("grd,de->gre", ext_r, w_in, preferred_element_type=jnp.float32)
    step_r = jax.nn.softplus(
        jnp.einsum("grd,dh->grh", mirrored, w_dt, preferred_element_type=jnp.float32) + dt_bias
    )
    sum_r, pend_r = strand_terms(proj_r, step_r, conv_w, conv_b, rates, True)
    def forward_out(incoming):
        normed_f = finish(pend_f, incoming, proj_f[:, :rows, :inner], d_skip, norm_gain)
        return jnp.einsum("grk,kd->grd", normed_f, w_out, preferred_element_type=jnp.float32)

    in_r, out_f = exclusive_scans(sum_f, sum_r, "seq", forward_out)
    normed_r = finish(pend_r, in_r[1], proj_r[:, :rows, :inner], d_skip, norm_gain)
    w_out_mirrored = flip_lanes(w_out)
    return project_add(normed_r, w_out_mirrored, out_f)


def solution(mesh):
    placed = (
        P(("groups", "batch"), "seq"),
        P(("groups", "batch"), "seq", None),
        P(),
        P(),
        P(),
        P(),
        P(),
        P(),
        P(),
        P(),
        P(),
        P(),
    )
    return jax.shard_map(
        on_device,
        mesh=mesh,
        in_specs=placed,
        out_specs=P(("groups", "batch"), "seq", None),
        check_vma=False,
    )
```

```python
from functools import partial

import jax
import jax.numpy as jnp
from jax import lax
from jax.experimental import pallas as pl
from jax.experimental.pallas import tpu as pltpu
from jax.sharding import PartitionSpec as P

H = 16
P_SIZE = 64
N = 128
Q = 256
KCONV = 4


norm_epsilon = 1e-05


def exchange(size, dtype):
    row = lax.broadcasted_iota(jnp.int32, (size, size), 0)
    col = lax.broadcasted_iota(jnp.int32, (size, size), 1)
    return (row + col == size - 1).astype(dtype)


def flip_lanes(a):
    j = exchange(a.shape[-1], a.dtype)
    return jnp.einsum("...d,de->...e", a, j, preferred_element_type=jnp.float32).astype(a.dtype)


def chain(earlier, later):
    first_decay, first_state = earlier
    next_decay, next_state = later
    return (first_decay * next_decay, next_decay[..., None, None] * first_state + next_state)


def exclusive_scans(fwd, rev, axis, after_fwd):
    count = lax.axis_size(axis)
    place = lax.axis_index(axis)
    seen = [None, None]
    ahead = [fwd, rev]
    shift = 1
    while shift < count:
        up = [(i, i + shift) for i in range(count - shift)]
        down = [(i + shift, i) for i in range(count - shift)]
        got = []
        for k, pairs in ((0, up), (1, down)):
            decay, state = unpack(lax.ppermute(pack(*ahead[k]), axis, pairs))
            has = (place >= shift) if k == 0 else (place < count - shift)
            decay = jnp.where(has, decay, 1.0)
            got.append((decay, state))
        last = 2 * shift >= count
        for k in range(2):
            if k == 1 and last:
                tail = after_fwd(seen[0][1])
                got[1], tail = lax.optimization_barrier((got[1], tail))
            seen[k] = got[k] if seen[k] is None else chain(got[k], seen[k])
            if not last:
                ahead[k] = chain(got[k], ahead[k])
        shift *= 2
    if seen[0] is None:
        return fwd_identity(rev), after_fwd(fwd_identity(fwd)[1])
    return seen[1], tail


def pack(decay, state):
    count = state.shape[0]
    flat = state.reshape(count, H * P_SIZE, N)
    extra = jnp.zeros((count, 8, N), jnp.float32).at[:, 0, :H].set(decay)
    return jnp.concatenate([flat, extra], axis=1)


def unpack(packed):
    count = packed.shape[0]
    rows = H * P_SIZE
    return packed[:, rows, :H], packed[:, :rows].reshape(count, H, P_SIZE, N)


def fwd_identity(summary):
    decay, state = summary
    return (jnp.ones_like(decay), jnp.zeros_like(state))


def inside_kernel(xbc_ref, cum_ref, cum_t_ref, step_t_ref, inside_ref, *, reverse):
    inner = H * P_SIZE
    b_rows = xbc_ref[:, inner : inner + N]
    c_rows = xbc_ref[:, inner + N :]
    scores = lax.dot_general(
        c_rows, b_rows, (((1,), (1,)), ((), ())), preferred_element_type=jnp.float32
    )
    t_idx = lax.broadcasted_iota(jnp.int32, (Q, Q), 0)
    s_idx = lax.broadcasted_iota(jnp.int32, (Q, Q), 1)
    keep = (s_idx >= t_idx) if reverse else (t_idx >= s_idx)
    for h in range(H):
        gaps = cum_ref[:, h : h + 1] - cum_t_ref[h : h + 1, :]
        decays = jnp.where(keep, jnp.exp(jnp.where(keep, gaps, 0.0)), 0.0)
        weights = (decays * scores * step_t_ref[h : h + 1, :]).astype(jnp.bfloat16)
        x_h = xbc_ref[:, h * P_SIZE : (h + 1) * P_SIZE]
        inside_ref[:, h * P_SIZE : (h + 1) * P_SIZE] = jnp.dot(
            weights, x_h, preferred_element_type=jnp.float32
        )


def state_kernel(xbc_ref, x_t_ref, to_end_ref, state_ref):
    inner = H * P_SIZE
    b_wide = xbc_ref[:, inner : inner + N].astype(jnp.float32)
    for h in range(H):
        state_weights = (b_wide * to_end_ref[:, h : h + 1]).astype(jnp.bfloat16)
        state_ref[h] = jnp.dot(
            x_t_ref[h * P_SIZE : (h + 1) * P_SIZE, :],
            state_weights,
            preferred_element_type=jnp.float32,
        )


def block_terms(activated, activated_t, step_size, rates, reverse):
    count, rows, width = activated.shape
    spans = rows // Q
    blocks = count * spans
    steps_cut = step_size.reshape(count, spans, Q, H)
    rated = steps_cut * rates
    log_decay = jnp.cumsum(rated, axis=2)
    if reverse:
        log_decay = log_decay[:, :, -1:] - log_decay + rated
    end = log_decay[:, :, 0] if reverse else log_decay[:, :, -1]
    to_end = jnp.exp(end[:, :, None, :] - log_decay) * steps_cut
    flat = lambda a: a.reshape((blocks,) + a.shape[2:])
    cum = flat(log_decay)
    cum_t = jnp.swapaxes(cum, 1, 2)
    step_t = jnp.swapaxes(flat(steps_cut), 1, 2)
    xbc = activated.reshape(blocks, Q, width)
    spec = lambda shape: pl.BlockSpec((None,) + shape, lambda i: (i,) + (0,) * len(shape))
    state = pl.pallas_call(
        state_kernel,
        grid=(blocks,),
        in_specs=[
            spec((Q, width)),
            pl.BlockSpec((None, H * P_SIZE, Q), lambda i: (i // spans, 0, i % spans)),
            spec((Q, H)),
        ],
        out_specs=spec((H, P_SIZE, N)),
        out_shape=jax.ShapeDtypeStruct((blocks, H, P_SIZE, N), jnp.float32),
    )(xbc, activated_t, flat(to_end))
    inside = pl.pallas_call(
        partial(inside_kernel, reverse=reverse),
        grid=(blocks,),
        in_specs=[spec((Q, width)), spec((Q, H)), spec((H, Q)), spec((H, Q))],
        out_specs=spec((Q, H * P_SIZE)),
        out_shape=jax.ShapeDtypeStruct((blocks, Q, H * P_SIZE), jnp.float32),
    )(xbc, cum, cum_t, step_t)
    inside = inside.reshape(count, rows, H * P_SIZE)
    state = state.reshape(count, spans, H, P_SIZE, N)
    return inside, state, jnp.exp(end), jnp.exp(log_decay)


CONV_LANES = 256


def conv_kernel(src_ref, halo_ref, w_ref, b_ref, out_ref, out_t_ref, *, reverse):
    margin = KCONV - 1
    src = src_ref[...]
    rows = src.shape[0]
    edge = halo_ref.shape[0]
    w = w_ref[...]
    if reverse:
        near = jnp.concatenate([src[rows - edge :], halo_ref[...]], axis=0)
    else:
        near = jnp.concatenate([halo_ref[...], src[:edge]], axis=0)
    span = near.shape[0]
    main = jnp.broadcast_to(b_ref[...], src.shape)
    side = jnp.broadcast_to(b_ref[...], (edge, src.shape[1]))
    for tap in range(KCONV):
        shift = margin - tap
        if shift == 0:
            piece, near_piece = src, near
        elif reverse:
            piece = pltpu.roll(src, rows - shift, 0)
            near_piece = pltpu.roll(near, span - shift, 0)
        else:
            piece = pltpu.roll(src, shift, 0)
            near_piece = pltpu.roll(near, shift, 0)
        main = main + w[tap : tap + 1] * piece
        part = near_piece[:edge] if reverse else near_piece[edge:]
        side = side + w[tap : tap + 1] * part
    out_ref[...] = jax.nn.silu(main).astype(out_ref.dtype)
    if reverse:
        out_ref[rows - edge :, :] = jax.nn.silu(side).astype(out_ref.dtype)
    else:
        out_ref[:edge, :] = jax.nn.silu(side).astype(out_ref.dtype)
    out_t_ref[...] = jnp.transpose(out_ref[...].astype(jnp.float32)).astype(out_t_ref.dtype)


def convolve(projected, rows, conv_w, conv_b, reverse):
    inner = H * P_SIZE
    count = projected.shape[0]
    width = conv_w.shape[1]
    edge = 8
    lanes = CONV_LANES
    skip = inner // lanes
    return pl.pallas_call(
        partial(conv_kernel, reverse=reverse),
        grid=(count, width // lanes),
        in_specs=[
            pl.BlockSpec((None, rows, lanes), lambda g, j: (g, 0, j + skip)),
            pl.BlockSpec((None, edge, lanes), lambda g, j: (g, rows // edge, j + skip)),
            pl.BlockSpec((KCONV, lanes), lambda g, j: (0, j)),
            pl.BlockSpec((1, lanes), lambda g, j: (0, j)),
        ],
        out_specs=[
            pl.BlockSpec((None, rows, lanes), lambda g, j: (g, 0, j)),
            pl.BlockSpec((None, lanes, rows), lambda g, j: (g, j, 0)),
        ],
        out_shape=[
            jax.ShapeDtypeStruct((count, rows, width), jnp.bfloat16),
            jax.ShapeDtypeStruct((count, width, rows), jnp.bfloat16),
        ],
    )(projected, projected, conv_w, conv_b.reshape(1, width))


def strand_terms(projected, step_size, conv_w, conv_b, rates, reverse):
    inner = H * P_SIZE
    count, rows, _ = step_size.shape
    activated, activated_t = convolve(projected, rows, conv_w, conv_b, reverse)
    spans = rows // Q
    inside, state, total, from_start = block_terms(activated, activated_t, step_size, rates, reverse)
    order = list(range(spans))
    if reverse:
        order = order[::-1]
    before = {}
    sofar = (jnp.ones((count, H), jnp.float32), jnp.zeros((count, H, P_SIZE, N), jnp.float32))
    for j in order:
        before[j] = sofar
        sofar = chain(sofar, (total[:, j], state[:, j]))
    before_decay = jnp.stack([before[j][0] for j in range(spans)], axis=1)
    before_state = jnp.stack([before[j][1] for j in range(spans)], axis=1)
    pending = (before_decay, before_state, inside, from_start, activated)
    return sofar, pending


def finish(pending, incoming, gate_part, d_skip, norm_gain):
    before_decay, before_state, inside, from_start, activated = pending
    inner = H * P_SIZE
    count, rows, _ = activated.shape
    spans = rows // Q
    start_state = before_state + before_decay[..., None, None] * incoming[:, None]
    c_rows = activated[:, :, inner + N :].reshape(count, spans, Q, N)
    carried = jnp.einsum(
        "gjtn,gjkn->gjtk",
        c_rows.astype(jnp.float32),
        start_state.reshape(count, spans, inner, N),
        precision=lax.Precision.HIGHEST,
    ).reshape(count, rows, inner)
    heads = lax.broadcasted_iota(jnp.int32, (H, inner), 0)
    lanes = lax.broadcasted_iota(jnp.int32, (H, inner), 1)
    spread = (lanes // P_SIZE == heads).astype(jnp.float32)
    scale = jnp.einsum(
        "grh,hk->grk", from_start.reshape(count, rows, H), spread, precision=lax.Precision.HIGHEST
    )
    skip = jnp.repeat(d_skip, P_SIZE)
    scanned = inside + scale * carried + skip * activated[:, :, :inner].astype(jnp.float32)
    gated = scanned * jax.nn.silu(gate_part)
    return (
        gated
        * lax.rsqrt(jnp.mean(gated * gated, axis=-1, keepdims=True) + norm_epsilon)
        * norm_gain
    ).astype(jnp.bfloat16)


def on_device(
    tokens, hidden, base_table, w_in, w_dt, conv_w, conv_b, dt_bias, a_log, d_skip, norm_gain, w_out
):
    inner = H * P_SIZE
    margin = KCONV - 1
    one_hot = (tokens[:, :, None] == jnp.arange(4)[None, None, :]).astype(jnp.bfloat16)
    looked = jnp.einsum("gtb,bd->gtd", one_hot, base_table, preferred_element_type=jnp.float32)
    strand = (hidden.astype(jnp.float32) + looked).astype(jnp.bfloat16)
    rows = strand.shape[1]
    count = lax.axis_size("seq")
    low = lax.ppermute(strand[:, rows - margin :], "seq", [(i, i + 1) for i in range(count - 1)])
    high = lax.ppermute(strand[:, :margin], "seq", [(i + 1, i) for i in range(count - 1)])
    rates = -jnp.exp(a_log)
    gap = jnp.zeros((strand.shape[0], 8 - margin, strand.shape[2]), strand.dtype)
    ext_f = jnp.concatenate([strand, gap, low], axis=1)
    proj_f = jnp.einsum("grd,de->gre", ext_f, w_in, preferred_element_type=jnp.float32)
    step_f = jax.nn.softplus(
        jnp.einsum("grd,dh->grh", strand, w_dt, preferred_element_type=jnp.float32) + dt_bias
    )
    sum_f, pend_f = strand_terms(proj_f, step_f, conv_w, conv_b, rates, False)
    sum_f, (strand_late, high) = lax.optimization_barrier((sum_f, (strand, high)))
    ext_r = flip_lanes(jnp.concatenate([strand_late, high, gap], axis=1))
    mirrored = ext_r[:, :rows]
    proj_r = jnp.einsum("grd,de->gre", ext_r, w_in, preferred_element_type=jnp.float32)
    step_r = jax.nn.softplus(
        jnp.einsum("grd,dh->grh", mirrored, w_dt, preferred_element_type=jnp.float32) + dt_bias
    )
    sum_r, pend_r = strand_terms(proj_r, step_r, conv_w, conv_b, rates, True)
    def forward_out(incoming):
        normed_f = finish(pend_f, incoming, proj_f[:, :rows, :inner], d_skip, norm_gain)
        return jnp.einsum("grk,kd->grd", normed_f, w_out, preferred_element_type=jnp.float32)

    in_r, out_f = exclusive_scans(sum_f, sum_r, "seq", forward_out)
    normed_r = finish(pend_r, in_r[1], proj_r[:, :rows, :inner], d_skip, norm_gain)
    w_out_mirrored = flip_lanes(w_out)
    out = out_f + jnp.einsum(
        "grk,kd->grd", normed_r, w_out_mirrored, preferred_element_type=jnp.float32
    )
    return out.astype(jnp.bfloat16)


def solution(mesh):
    placed = (
        P(("groups", "batch"), "seq"),
        P(("groups", "batch"), "seq", None),
        P(),
        P(),
        P(),
        P(),
        P(),
        P(),
        P(),
        P(),
        P(),
        P(),
    )
    return jax.shard_map(
        on_device,
        mesh=mesh,
        in_specs=placed,
        out_specs=P(("groups", "batch"), "seq", None),
        check_vma=False,
    )
```

```python
from functools import partial

import jax
import jax.numpy as jnp
from jax import lax
from jax.experimental import pallas as pl
from jax.experimental.pallas import tpu as pltpu
from jax.sharding import PartitionSpec as P

H = 16
P_SIZE = 64
N = 128
Q = 256
KCONV = 4


norm_epsilon = 1e-05


def exchange(size, dtype):
    row = lax.broadcasted_iota(jnp.int32, (size, size), 0)
    col = lax.broadcasted_iota(jnp.int32, (size, size), 1)
    return (row + col == size - 1).astype(dtype)


def flip_lanes(a):
    j = exchange(a.shape[-1], a.dtype)
    return jnp.einsum("...d,de->...e", a, j, preferred_element_type=jnp.float32).astype(a.dtype)


def chain(earlier, later):
    first_decay, first_state = earlier
    next_decay, next_state = later
    return (first_decay * next_decay, next_decay[..., None, None] * first_state + next_state)


def exclusive_scans(fwd, rev, axis, after_fwd):
    count = lax.axis_size(axis)
    place = lax.axis_index(axis)
    seen = [None, None]
    ahead = [fwd, rev]
    shift = 1
    while shift < count:
        up = [(i, i + shift) for i in range(count - shift)]
        down = [(i + shift, i) for i in range(count - shift)]
        got = []
        for k, pairs in ((0, up), (1, down)):
            decay, state = unpack(lax.ppermute(pack(*ahead[k]), axis, pairs))
            has = (place >= shift) if k == 0 else (place < count - shift)
            decay = jnp.where(has, decay, 1.0)
            got.append((decay, state))
        last = 2 * shift >= count
        for k in range(2):
            if k == 1 and last:
                tail = after_fwd(seen[0][1])
                got[1], tail = lax.optimization_barrier((got[1], tail))
            seen[k] = got[k] if seen[k] is None else chain(got[k], seen[k])
            if not last:
                ahead[k] = chain(got[k], ahead[k])
        shift *= 2
    if seen[0] is None:
        return fwd_identity(rev), after_fwd(fwd_identity(fwd)[1])
    return seen[1], tail


def pack(decay, state):
    count = state.shape[0]
    flat = state.reshape(count, H * P_SIZE, N)
    extra = jnp.zeros((count, 8, N), jnp.float32).at[:, 0, :H].set(decay)
    return jnp.concatenate([flat, extra], axis=1)


def unpack(packed):
    count = packed.shape[0]
    rows = H * P_SIZE
    return packed[:, rows, :H], packed[:, :rows].reshape(count, H, P_SIZE, N)


def fwd_identity(summary):
    decay, state = summary
    return (jnp.ones_like(decay), jnp.zeros_like(state))


def inside_kernel(xbc_ref, cum_ref, cum_t_ref, step_t_ref, inside_ref, *, reverse):
    inner = H * P_SIZE
    b_rows = xbc_ref[:, inner : inner + N]
    c_rows = xbc_ref[:, inner + N :]
    scores = lax.dot_general(
        c_rows, b_rows, (((1,), (1,)), ((), ())), preferred_element_type=jnp.float32
    )
    t_idx = lax.broadcasted_iota(jnp.int32, (Q, Q), 0)
    s_idx = lax.broadcasted_iota(jnp.int32, (Q, Q), 1)
    keep = (s_idx >= t_idx) if reverse else (t_idx >= s_idx)
    for h in range(H):
        gaps = cum_ref[:, h : h + 1] - cum_t_ref[h : h + 1, :]
        decays = jnp.where(keep, jnp.exp(jnp.where(keep, gaps, 0.0)), 0.0)
        weights = (decays * scores * step_t_ref[h : h + 1, :]).astype(jnp.bfloat16)
        x_h = xbc_ref[:, h * P_SIZE : (h + 1) * P_SIZE]
        inside_ref[:, h * P_SIZE : (h + 1) * P_SIZE] = jnp.dot(
            weights, x_h, preferred_element_type=jnp.float32
        )


def state_kernel(xbc_ref, x_t_ref, to_end_ref, state_ref):
    inner = H * P_SIZE
    b_wide = xbc_ref[:, inner : inner + N].astype(jnp.float32)
    for h in range(H):
        state_weights = (b_wide * to_end_ref[:, h : h + 1]).astype(jnp.bfloat16)
        state_ref[h] = jnp.dot(
            x_t_ref[h * P_SIZE : (h + 1) * P_SIZE, :],
            state_weights,
            preferred_element_type=jnp.float32,
        )


def block_terms(activated, activated_t, step_size, rates, reverse):
    count, rows, width = activated.shape
    spans = rows // Q
    blocks = count * spans
    steps_cut = step_size.reshape(count, spans, Q, H)
    rated = steps_cut * rates
    log_decay = jnp.cumsum(rated, axis=2)
    if reverse:
        log_decay = log_decay[:, :, -1:] - log_decay + rated
    end = log_decay[:, :, 0] if reverse else log_decay[:, :, -1]
    to_end = jnp.exp(end[:, :, None, :] - log_decay) * steps_cut
    flat = lambda a: a.reshape((blocks,) + a.shape[2:])
    cum = flat(log_decay)
    cum_t = jnp.swapaxes(cum, 1, 2)
    step_t = jnp.swapaxes(flat(steps_cut), 1, 2)
    xbc = activated.reshape(blocks, Q, width)
    spec = lambda shape: pl.BlockSpec((None,) + shape, lambda i: (i,) + (0,) * len(shape))
    state = pl.pallas_call(
        state_kernel,
        grid=(blocks,),
        in_specs=[
            spec((Q, width)),
            pl.BlockSpec((None, H * P_SIZE, Q), lambda i: (i // spans, 0, i % spans)),
            spec((Q, H)),
        ],
        out_specs=spec((H, P_SIZE, N)),
        out_shape=jax.ShapeDtypeStruct((blocks, H, P_SIZE, N), jnp.float32),
    )(xbc, activated_t, flat(to_end))
    inside = pl.pallas_call(
        partial(inside_kernel, reverse=reverse),
        grid=(blocks,),
        in_specs=[spec((Q, width)), spec((Q, H)), spec((H, Q)), spec((H, Q))],
        out_specs=spec((Q, H * P_SIZE)),
        out_shape=jax.ShapeDtypeStruct((blocks, Q, H * P_SIZE), jnp.float32),
    )(xbc, cum, cum_t, step_t)
    inside = inside.reshape(count, rows, H * P_SIZE)
    state = state.reshape(count, spans, H, P_SIZE, N)
    return inside, state, jnp.exp(end), jnp.exp(log_decay)


CONV_LANES = 256


def conv_kernel(src_ref, halo_ref, w_ref, b_ref, out_ref, out_t_ref, *, reverse):
    margin = KCONV - 1
    src = src_ref[...]
    rows = src.shape[0]
    edge = halo_ref.shape[0]
    w = w_ref[...]
    if reverse:
        near = jnp.concatenate([src[rows - edge :], halo_ref[...]], axis=0)
    else:
        near = jnp.concatenate([halo_ref[...], src[:edge]], axis=0)
    span = near.shape[0]
    main = jnp.broadcast_to(b_ref[...], src.shape)
    side = jnp.broadcast_to(b_ref[...], (edge, src.shape[1]))
    for tap in range(KCONV):
        shift = margin - tap
        if shift == 0:
            piece, near_piece = src, near
        elif reverse:
            piece = pltpu.roll(src, rows - shift, 0)
            near_piece = pltpu.roll(near, span - shift, 0)
        else:
            piece = pltpu.roll(src, shift, 0)
            near_piece = pltpu.roll(near, shift, 0)
        main = main + w[tap : tap + 1] * piece
        part = near_piece[:edge] if reverse else near_piece[edge:]
        side = side + w[tap : tap + 1] * part
    out_ref[...] = jax.nn.silu(main).astype(out_ref.dtype)
    if reverse:
        out_ref[rows - edge :, :] = jax.nn.silu(side).astype(out_ref.dtype)
    else:
        out_ref[:edge, :] = jax.nn.silu(side).astype(out_ref.dtype)
    out_t_ref[...] = jnp.transpose(out_ref[...].astype(jnp.float32)).astype(out_t_ref.dtype)


def convolve(projected, rows, conv_w, conv_b, reverse):
    inner = H * P_SIZE
    count = projected.shape[0]
    width = conv_w.shape[1]
    edge = 8
    lanes = CONV_LANES
    skip = inner // lanes
    return pl.pallas_call(
        partial(conv_kernel, reverse=reverse),
        grid=(count, width // lanes),
        in_specs=[
            pl.BlockSpec((None, rows, lanes), lambda g, j: (g, 0, j + skip)),
            pl.BlockSpec((None, edge, lanes), lambda g, j: (g, rows // edge, j + skip)),
            pl.BlockSpec((KCONV, lanes), lambda g, j: (0, j)),
            pl.BlockSpec((1, lanes), lambda g, j: (0, j)),
        ],
        out_specs=[
            pl.BlockSpec((None, rows, lanes), lambda g, j: (g, 0, j)),
            pl.BlockSpec((None, lanes, rows), lambda g, j: (g, j, 0)),
        ],
        out_shape=[
            jax.ShapeDtypeStruct((count, rows, width), jnp.bfloat16),
            jax.ShapeDtypeStruct((count, width, rows), jnp.bfloat16),
        ],
    )(projected, projected, conv_w, conv_b.reshape(1, width))


def strand_terms(projected, step_size, conv_w, conv_b, rates, reverse):
    inner = H * P_SIZE
    count, rows, _ = step_size.shape
    activated, activated_t = convolve(projected, rows, conv_w, conv_b, reverse)
    spans = rows // Q
    inside, state, total, from_start = block_terms(activated, activated_t, step_size, rates, reverse)
    order = list(range(spans))
    if reverse:
        order = order[::-1]
    before = {}
    sofar = (jnp.ones((count, H), jnp.float32), jnp.zeros((count, H, P_SIZE, N), jnp.float32))
    for j in order:
        before[j] = sofar
        sofar = chain(sofar, (total[:, j], state[:, j]))
    before_decay = jnp.stack([before[j][0] for j in range(spans)], axis=1)
    before_state = jnp.stack([before[j][1] for j in range(spans)], axis=1)
    pending = (before_decay, before_state, inside, from_start, activated)
    return sofar, pending


def finish(pending, incoming, gate_part, d_skip, norm_gain):
    before_decay, before_state, inside, from_start, activated = pending
    inner = H * P_SIZE
    count, rows, _ = activated.shape
    spans = rows // Q
    start_state = before_state + before_decay[..., None, None] * incoming[:, None]
    c_rows = activated[:, :, inner + N :].reshape(count, spans, Q, N)
    carried = jnp.einsum(
        "gjtn,gjkn->gjtk",
        c_rows.astype(jnp.float32),
        start_state.reshape(count, spans, inner, N),
        precision=lax.Precision.HIGHEST,
    ).reshape(count, rows, inner)
    heads = lax.broadcasted_iota(jnp.int32, (H, inner), 0)
    lanes = lax.broadcasted_iota(jnp.int32, (H, inner), 1)
    spread = (lanes // P_SIZE == heads).astype(jnp.float32)
    scale = jnp.einsum(
        "grh,hk->grk", from_start.reshape(count, rows, H), spread, precision=lax.Precision.HIGHEST
    )
    skip = jnp.repeat(d_skip, P_SIZE)
    scanned = inside + scale * carried + skip * activated[:, :, :inner].astype(jnp.float32)
    gated = scanned * jax.nn.silu(gate_part)
    return (
        gated
        * lax.rsqrt(jnp.mean(gated * gated, axis=-1, keepdims=True) + norm_epsilon)
        * norm_gain
    ).astype(jnp.bfloat16)


def project_kernel(a_ref, w_ref, add_ref, out_ref):
    total = add_ref[...] + jnp.dot(a_ref[...], w_ref[...], preferred_element_type=jnp.float32)
    out_ref[...] = total.astype(out_ref.dtype)


def project_add(normed, w, addend, lanes=256):
    count, rows, depth = normed.shape
    width = w.shape[1]
    return pl.pallas_call(
        project_kernel,
        grid=(count, width // lanes),
        in_specs=[
            pl.BlockSpec((None, rows, depth), lambda g, j: (g, 0, 0)),
            pl.BlockSpec((depth, lanes), lambda g, j: (0, j)),
            pl.BlockSpec((None, rows, lanes), lambda g, j: (g, 0, j)),
        ],
        out_specs=pl.BlockSpec((None, rows, lanes), lambda g, j: (g, 0, j)),
        out_shape=jax.ShapeDtypeStruct((count, rows, width), jnp.bfloat16),
    )(normed, w, addend)


def on_device(
    tokens, hidden, base_table, w_in, w_dt, conv_w, conv_b, dt_bias, a_log, d_skip, norm_gain, w_out
):
    inner = H * P_SIZE
    margin = KCONV - 1
    one_hot = (tokens[:, :, None] == jnp.arange(4)[None, None, :]).astype(jnp.bfloat16)
    looked = jnp.einsum("gtb,bd->gtd", one_hot, base_table, preferred_element_type=jnp.float32)
    strand = (hidden.astype(jnp.float32) + looked).astype(jnp.bfloat16)
    rows = strand.shape[1]
    count = lax.axis_size("seq")
    low = lax.ppermute(strand[:, rows - margin :], "seq", [(i, i + 1) for i in range(count - 1)])
    high = lax.ppermute(strand[:, :margin], "seq", [(i + 1, i) for i in range(count - 1)])
    rates = -jnp.exp(a_log)
    gap = jnp.zeros((strand.shape[0], 8 - margin, strand.shape[2]), strand.dtype)
    ext_f = jnp.concatenate([strand, gap, low], axis=1)
    proj_f = jnp.einsum("grd,de->gre", ext_f, w_in, preferred_element_type=jnp.float32)
    step_f = jax.nn.softplus(
        jnp.einsum("grd,dh->grh", strand, w_dt, preferred_element_type=jnp.float32) + dt_bias
    )
    sum_f, pend_f = strand_terms(proj_f, step_f, conv_w, conv_b, rates, False)
    sum_f, (strand_late, high) = lax.optimization_barrier((sum_f, (strand, high)))
    ext_r = flip_lanes(jnp.concatenate([strand_late, high, gap], axis=1))
    mirrored = ext_r[:, :rows]
    proj_r = jnp.einsum("grd,de->gre", ext_r, w_in, preferred_element_type=jnp.float32)
    step_r = jax.nn.softplus(
        jnp.einsum("grd,dh->grh", mirrored, w_dt, preferred_element_type=jnp.float32) + dt_bias
    )
    sum_r, pend_r = strand_terms(proj_r, step_r, conv_w, conv_b, rates, True)
    def forward_out(incoming):
        normed_f = finish(pend_f, incoming, proj_f[:, :rows, :inner], d_skip, norm_gain)
        return jnp.einsum("grk,kd->grd", normed_f, w_out, preferred_element_type=jnp.float32)

    in_r, out_f = exclusive_scans(sum_f, sum_r, "seq", forward_out)
    normed_r = finish(pend_r, in_r[1], proj_r[:, :rows, :inner], d_skip, norm_gain)
    w_out_mirrored = flip_lanes(w_out)
    return project_add(normed_r, w_out_mirrored, out_f)


def solution(mesh):
    placed = (
        P(("groups", "batch"), "seq"),
        P(("groups", "batch"), "seq", None),
        P(),
        P(),
        P(),
        P(),
        P(),
        P(),
        P(),
        P(),
        P(),
        P(),
    )
    return jax.shard_map(
        on_device,
        mesh=mesh,
        in_specs=placed,
        out_specs=P(("groups", "batch"), "seq", None),
        check_vma=False,
    )
```

```python
from functools import partial

import jax
import jax.numpy as jnp
from jax import lax
from jax.experimental import pallas as pl
from jax.experimental.pallas import tpu as pltpu
from jax.sharding import PartitionSpec as P

H = 16
P_SIZE = 64
N = 128
Q = 256
KCONV = 4


norm_epsilon = 1e-05


def exchange(size, dtype):
    row = lax.broadcasted_iota(jnp.int32, (size, size), 0)
    col = lax.broadcasted_iota(jnp.int32, (size, size), 1)
    return (row + col == size - 1).astype(dtype)


def flip_lanes(a):
    j = exchange(a.shape[-1], a.dtype)
    return jnp.einsum("...d,de->...e", a, j, preferred_element_type=jnp.float32).astype(a.dtype)


def chain(earlier, later):
    first_decay, first_state = earlier
    next_decay, next_state = later
    return (first_decay * next_decay, next_decay[..., None, None] * first_state + next_state)


def exclusive_scans(fwd, rev, axis, after_fwd):
    count = lax.axis_size(axis)
    place = lax.axis_index(axis)
    seen = [None, None]
    ahead = [fwd, rev]
    shift = 1
    while shift < count:
        up = [(i, i + shift) for i in range(count - shift)]
        down = [(i + shift, i) for i in range(count - shift)]
        got = []
        for k, pairs in ((0, up), (1, down)):
            decay, state = unpack(lax.ppermute(pack(*ahead[k]), axis, pairs))
            has = (place >= shift) if k == 0 else (place < count - shift)
            decay = jnp.where(has, decay, 1.0)
            got.append((decay, state))
        last = 2 * shift >= count
        for k in range(2):
            if k == 1 and last:
                tail = after_fwd(seen[0][1])
                got[1], tail = lax.optimization_barrier((got[1], tail))
            seen[k] = got[k] if seen[k] is None else chain(got[k], seen[k])
            if not last:
                ahead[k] = chain(got[k], ahead[k])
        shift *= 2
    if seen[0] is None:
        return fwd_identity(rev), after_fwd(fwd_identity(fwd)[1])
    return seen[1], tail


def pack(decay, state):
    count = state.shape[0]
    flat = state.reshape(count, H * P_SIZE, N)
    extra = jnp.zeros((count, 8, N), jnp.float32).at[:, 0, :H].set(decay)
    return jnp.concatenate([flat, extra], axis=1)


def unpack(packed):
    count = packed.shape[0]
    rows = H * P_SIZE
    return packed[:, rows, :H], packed[:, :rows].reshape(count, H, P_SIZE, N)


def fwd_identity(summary):
    decay, state = summary
    return (jnp.ones_like(decay), jnp.zeros_like(state))


def inside_kernel(xbc_ref, cum_ref, cum_t_ref, step_t_ref, inside_ref, *, reverse):
    inner = H * P_SIZE
    b_rows = xbc_ref[:, inner : inner + N]
    c_rows = xbc_ref[:, inner + N :]
    scores = lax.dot_general(
        c_rows, b_rows, (((1,), (1,)), ((), ())), preferred_element_type=jnp.float32
    )
    t_idx = lax.broadcasted_iota(jnp.int32, (Q, Q), 0)
    s_idx = lax.broadcasted_iota(jnp.int32, (Q, Q), 1)
    keep = (s_idx >= t_idx) if reverse else (t_idx >= s_idx)
    for h in range(H):
        gaps = cum_ref[:, h : h + 1] - cum_t_ref[h : h + 1, :]
        decays = jnp.where(keep, jnp.exp(jnp.where(keep, gaps, 0.0)), 0.0)
        weights = (decays * scores * step_t_ref[h : h + 1, :]).astype(jnp.bfloat16)
        x_h = xbc_ref[:, h * P_SIZE : (h + 1) * P_SIZE]
        inside_ref[:, h * P_SIZE : (h + 1) * P_SIZE] = jnp.dot(
            weights, x_h, preferred_element_type=jnp.float32
        )


def state_kernel(xbc_ref, x_t_ref, to_end_ref, state_ref):
    inner = H * P_SIZE
    b_wide = xbc_ref[:, inner : inner + N].astype(jnp.float32)
    for h in range(H):
        state_weights = (b_wide * to_end_ref[:, h : h + 1]).astype(jnp.bfloat16)
        state_ref[h] = jnp.dot(
            x_t_ref[h * P_SIZE : (h + 1) * P_SIZE, :],
            state_weights,
            preferred_element_type=jnp.float32,
        )


def block_terms(activated, activated_t, step_size, rates, reverse):
    count, rows, width = activated.shape
    spans = rows // Q
    blocks = count * spans
    steps_cut = step_size.reshape(count, spans, Q, H)
    rated = steps_cut * rates
    log_decay = jnp.cumsum(rated, axis=2)
    if reverse:
        log_decay = log_decay[:, :, -1:] - log_decay + rated
    end = log_decay[:, :, 0] if reverse else log_decay[:, :, -1]
    to_end = jnp.exp(end[:, :, None, :] - log_decay) * steps_cut
    flat = lambda a: a.reshape((blocks,) + a.shape[2:])
    cum = flat(log_decay)
    cum_t = jnp.swapaxes(cum, 1, 2)
    step_t = jnp.swapaxes(flat(steps_cut), 1, 2)
    xbc = activated.reshape(blocks, Q, width)
    spec = lambda shape: pl.BlockSpec((None,) + shape, lambda i: (i,) + (0,) * len(shape))
    state = pl.pallas_call(
        state_kernel,
        grid=(blocks,),
        in_specs=[
            spec((Q, width)),
            pl.BlockSpec((None, H * P_SIZE, Q), lambda i: (i // spans, 0, i % spans)),
            spec((Q, H)),
        ],
        out_specs=spec((H, P_SIZE, N)),
        out_shape=jax.ShapeDtypeStruct((blocks, H, P_SIZE, N), jnp.float32),
    )(xbc, activated_t, flat(to_end))
    inside = pl.pallas_call(
        partial(inside_kernel, reverse=reverse),
        grid=(blocks,),
        in_specs=[spec((Q, width)), spec((Q, H)), spec((H, Q)), spec((H, Q))],
        out_specs=spec((Q, H * P_SIZE)),
        out_shape=jax.ShapeDtypeStruct((blocks, Q, H * P_SIZE), jnp.float32),
    )(xbc, cum, cum_t, step_t)
    inside = inside.reshape(count, rows, H * P_SIZE)
    state = state.reshape(count, spans, H, P_SIZE, N)
    return inside, state, jnp.exp(end), jnp.exp(log_decay)


CONV_LANES = 256


def conv_kernel(src_ref, halo_ref, w_ref, b_ref, out_ref, out_t_ref, *, reverse):
    margin = KCONV - 1
    src = src_ref[...]
    rows = src.shape[0]
    edge = halo_ref.shape[0]
    w = w_ref[...]
    if reverse:
        near = jnp.concatenate([src[rows - edge :], halo_ref[...]], axis=0)
    else:
        near = jnp.concatenate([halo_ref[...], src[:edge]], axis=0)
    span = near.shape[0]
    main = jnp.broadcast_to(b_ref[...], src.shape)
    side = jnp.broadcast_to(b_ref[...], (edge, src.shape[1]))
    for tap in range(KCONV):
        shift = margin - tap
        if shift == 0:
            piece, near_piece = src, near
        elif reverse:
            piece = pltpu.roll(src, rows - shift, 0)
            near_piece = pltpu.roll(near, span - shift, 0)
        else:
            piece = pltpu.roll(src, shift, 0)
            near_piece = pltpu.roll(near, shift, 0)
        main = main + w[tap : tap + 1] * piece
        part = near_piece[:edge] if reverse else near_piece[edge:]
        side = side + w[tap : tap + 1] * part
    out_ref[...] = jax.nn.silu(main).astype(out_ref.dtype)
    if reverse:
        out_ref[rows - edge :, :] = jax.nn.silu(side).astype(out_ref.dtype)
    else:
        out_ref[:edge, :] = jax.nn.silu(side).astype(out_ref.dtype)
    out_t_ref[...] = jnp.transpose(out_ref[...].astype(jnp.float32)).astype(out_t_ref.dtype)


def convolve(projected, rows, conv_w, conv_b, reverse):
    inner = H * P_SIZE
    count = projected.shape[0]
    width = conv_w.shape[1]
    edge = 8
    lanes = CONV_LANES
    skip = (projected.shape[2] - width) // lanes
    return pl.pallas_call(
        partial(conv_kernel, reverse=reverse),
        grid=(count, width // lanes),
        in_specs=[
            pl.BlockSpec((None, rows, lanes), lambda g, j: (g, 0, j + skip)),
            pl.BlockSpec((None, edge, lanes), lambda g, j: (g, rows // edge, j + skip)),
            pl.BlockSpec((KCONV, lanes), lambda g, j: (0, j)),
            pl.BlockSpec((1, lanes), lambda g, j: (0, j)),
        ],
        out_specs=[
            pl.BlockSpec((None, rows, lanes), lambda g, j: (g, 0, j)),
            pl.BlockSpec((None, lanes, rows), lambda g, j: (g, j, 0)),
        ],
        out_shape=[
            jax.ShapeDtypeStruct((count, rows, width), jnp.bfloat16),
            jax.ShapeDtypeStruct((count, width, rows), jnp.bfloat16),
        ],
    )(projected, projected, conv_w, conv_b.reshape(1, width))


def strand_terms(projected, step_size, conv_w, conv_b, rates, reverse):
    inner = H * P_SIZE
    count, rows, _ = step_size.shape
    activated, activated_t = convolve(projected, rows, conv_w, conv_b, reverse)
    spans = rows // Q
    inside, state, total, from_start = block_terms(activated, activated_t, step_size, rates, reverse)
    order = list(range(spans))
    if reverse:
        order = order[::-1]
    before = {}
    sofar = (jnp.ones((count, H), jnp.float32), jnp.zeros((count, H, P_SIZE, N), jnp.float32))
    for j in order:
        before[j] = sofar
        sofar = chain(sofar, (total[:, j], state[:, j]))
    before_decay = jnp.stack([before[j][0] for j in range(spans)], axis=1)
    before_state = jnp.stack([before[j][1] for j in range(spans)], axis=1)
    pending = (before_decay, before_state, inside, from_start, activated)
    return sofar, pending


def finish(pending, incoming, gate_part, d_skip, norm_gain):
    before_decay, before_state, inside, from_start, activated = pending
    inner = H * P_SIZE
    count, rows, _ = activated.shape
    spans = rows // Q
    start_state = before_state + before_decay[..., None, None] * incoming[:, None]
    c_rows = activated[:, :, inner + N :].reshape(count, spans, Q, N)
    carried = jnp.einsum(
        "gjtn,gjkn->gjtk",
        c_rows.astype(jnp.float32),
        start_state.reshape(count, spans, inner, N),
        precision=lax.Precision.HIGHEST,
    ).reshape(count, rows, inner)
    heads = lax.broadcasted_iota(jnp.int32, (H, inner), 0)
    lanes = lax.broadcasted_iota(jnp.int32, (H, inner), 1)
    spread = (lanes // P_SIZE == heads).astype(jnp.float32)
    scale = jnp.einsum(
        "grh,hk->grk", from_start.reshape(count, rows, H), spread, precision=lax.Precision.HIGHEST
    )
    skip = jnp.repeat(d_skip, P_SIZE)
    scanned = inside + scale * carried + skip * activated[:, :, :inner].astype(jnp.float32)
    gated = scanned * jax.nn.silu(gate_part)
    return (
        gated
        * lax.rsqrt(jnp.mean(gated * gated, axis=-1, keepdims=True) + norm_epsilon)
        * norm_gain
    ).astype(jnp.bfloat16)


def on_device(
    tokens, hidden, base_table, w_in, w_dt, conv_w, conv_b, dt_bias, a_log, d_skip, norm_gain, w_out
):
    inner = H * P_SIZE
    margin = KCONV - 1
    one_hot = (tokens[:, :, None] == jnp.arange(4)[None, None, :]).astype(jnp.bfloat16)
    looked = jnp.einsum("gtb,bd->gtd", one_hot, base_table, preferred_element_type=jnp.float32)
    strand = (hidden.astype(jnp.float32) + looked).astype(jnp.bfloat16)
    rows = strand.shape[1]
    count = lax.axis_size("seq")
    low = lax.ppermute(strand[:, rows - margin :], "seq", [(i, i + 1) for i in range(count - 1)])
    high = lax.ppermute(strand[:, :margin], "seq", [(i + 1, i) for i in range(count - 1)])
    rates = -jnp.exp(a_log)
    gap = jnp.zeros((strand.shape[0], 8 - margin, strand.shape[2]), strand.dtype)
    ext_f = jnp.concatenate([strand, gap, low], axis=1)
    w_source = w_in[:, inner:]
    w_gate = w_in[:, :inner]
    proj_f = jnp.einsum("grd,de->gre", ext_f, w_source, preferred_element_type=jnp.float32)
    step_f = jax.nn.softplus(
        jnp.einsum("grd,dh->grh", strand, w_dt, preferred_element_type=jnp.float32) + dt_bias
    )
    sum_f, pend_f = strand_terms(proj_f, step_f, conv_w, conv_b, rates, False)
    sum_f, (strand_late, high) = lax.optimization_barrier((sum_f, (strand, high)))
    ext_r = flip_lanes(jnp.concatenate([strand_late, high, gap], axis=1))
    mirrored = ext_r[:, :rows]
    proj_r = jnp.einsum("grd,de->gre", ext_r, w_source, preferred_element_type=jnp.float32)
    step_r = jax.nn.softplus(
        jnp.einsum("grd,dh->grh", mirrored, w_dt, preferred_element_type=jnp.float32) + dt_bias
    )
    sum_r, pend_r = strand_terms(proj_r, step_r, conv_w, conv_b, rates, True)
    def forward_out(incoming):
        gate_f = jnp.einsum("grd,de->gre", strand, w_gate, preferred_element_type=jnp.float32)
        normed_f = finish(pend_f, incoming, gate_f, d_skip, norm_gain)
        return jnp.einsum("grk,kd->grd", normed_f, w_out, preferred_element_type=jnp.float32)

    in_r, out_f = exclusive_scans(sum_f, sum_r, "seq", forward_out)
    gate_r = jnp.einsum("grd,de->gre", mirrored, w_gate, preferred_element_type=jnp.float32)
    normed_r = finish(pend_r, in_r[1], gate_r, d_skip, norm_gain)
    w_out_mirrored = flip_lanes(w_out)
    out = out_f + jnp.einsum(
        "grk,kd->grd", normed_r, w_out_mirrored, preferred_element_type=jnp.float32
    )
    return out.astype(jnp.bfloat16)


def solution(mesh):
    placed = (
        P(("groups", "batch"), "seq"),
        P(("groups", "batch"), "seq", None),
        P(),
        P(),
        P(),
        P(),
        P(),
        P(),
        P(),
        P(),
        P(),
        P(),
    )
    return jax.shard_map(
        on_device,
        mesh=mesh,
        in_specs=placed,
        out_specs=P(("groups", "batch"), "seq", None),
        check_vma=False,
    )
```

```python
from functools import partial

import jax
import jax.numpy as jnp
from jax import lax
from jax.experimental import pallas as pl
from jax.experimental.pallas import tpu as pltpu
from jax.sharding import PartitionSpec as P

H = 16
P_SIZE = 64
N = 128
Q = 256
KCONV = 4


norm_epsilon = 1e-05


def exchange(size, dtype):
    row = lax.broadcasted_iota(jnp.int32, (size, size), 0)
    col = lax.broadcasted_iota(jnp.int32, (size, size), 1)
    return (row + col == size - 1).astype(dtype)


def flip_lanes(a):
    j = exchange(a.shape[-1], a.dtype)
    return jnp.einsum("...d,de->...e", a, j, preferred_element_type=jnp.float32).astype(a.dtype)


def chain(earlier, later):
    first_decay, first_state = earlier
    next_decay, next_state = later
    return (first_decay * next_decay, next_decay[..., None, None] * first_state + next_state)


def exclusive_scans(fwd, rev, axis, after_fwd):
    count = lax.axis_size(axis)
    place = lax.axis_index(axis)
    seen = [None, None]
    ahead = [fwd, rev]
    shift = 1
    while shift < count:
        up = [(i, i + shift) for i in range(count - shift)]
        down = [(i + shift, i) for i in range(count - shift)]
        got = []
        for k, pairs in ((0, up), (1, down)):
            decay, state = unpack(lax.ppermute(pack(*ahead[k]), axis, pairs))
            has = (place >= shift) if k == 0 else (place < count - shift)
            decay = jnp.where(has, decay, 1.0)
            got.append((decay, state))
        last = 2 * shift >= count
        for k in range(2):
            if k == 1 and last:
                tail = after_fwd(seen[0][1])
                got[1], tail = lax.optimization_barrier((got[1], tail))
            seen[k] = got[k] if seen[k] is None else chain(got[k], seen[k])
            if not last:
                ahead[k] = chain(got[k], ahead[k])
        shift *= 2
    if seen[0] is None:
        return fwd_identity(rev), after_fwd(fwd_identity(fwd)[1])
    return seen[1], tail


def pack(decay, state):
    count = state.shape[0]
    flat = state.reshape(count, H * P_SIZE, N)
    extra = jnp.zeros((count, 8, N), jnp.float32).at[:, 0, :H].set(decay)
    return jnp.concatenate([flat, extra], axis=1)


def unpack(packed):
    count = packed.shape[0]
    rows = H * P_SIZE
    return packed[:, rows, :H], packed[:, :rows].reshape(count, H, P_SIZE, N)


def fwd_identity(summary):
    decay, state = summary
    return (jnp.ones_like(decay), jnp.zeros_like(state))


def inside_kernel(xbc_ref, cum_ref, cum_t_ref, step_t_ref, inside_ref, *, reverse):
    inner = H * P_SIZE
    b_rows = xbc_ref[:, inner : inner + N]
    c_rows = xbc_ref[:, inner + N :]
    scores = lax.dot_general(
        c_rows, b_rows, (((1,), (1,)), ((), ())), preferred_element_type=jnp.float32
    )
    t_idx = lax.broadcasted_iota(jnp.int32, (Q, Q), 0)
    s_idx = lax.broadcasted_iota(jnp.int32, (Q, Q), 1)
    keep = (s_idx >= t_idx) if reverse else (t_idx >= s_idx)
    for h in range(H):
        gaps = cum_ref[:, h : h + 1] - cum_t_ref[h : h + 1, :]
        decays = jnp.where(keep, jnp.exp(jnp.where(keep, gaps, 0.0)), 0.0)
        weights = (decays * scores * step_t_ref[h : h + 1, :]).astype(jnp.bfloat16)
        x_h = xbc_ref[:, h * P_SIZE : (h + 1) * P_SIZE]
        inside_ref[:, h * P_SIZE : (h + 1) * P_SIZE] = jnp.dot(
            weights, x_h, preferred_element_type=jnp.float32
        )


def state_kernel(xbc_ref, x_t_ref, to_end_ref, state_ref):
    inner = H * P_SIZE
    b_wide = xbc_ref[:, inner : inner + N].astype(jnp.float32)
    for h in range(H):
        state_weights = (b_wide * to_end_ref[:, h : h + 1]).astype(jnp.bfloat16)
        state_ref[h] = jnp.dot(
            x_t_ref[h * P_SIZE : (h + 1) * P_SIZE, :],
            state_weights,
            preferred_element_type=jnp.float32,
        )


def block_terms(activated, activated_t, step_size, rates, reverse):
    count, rows, width = activated.shape
    spans = rows // Q
    blocks = count * spans
    steps_cut = step_size.reshape(count, spans, Q, H)
    rated = steps_cut * rates
    log_decay = jnp.cumsum(rated, axis=2)
    if reverse:
        log_decay = log_decay[:, :, -1:] - log_decay + rated
    end = log_decay[:, :, 0] if reverse else log_decay[:, :, -1]
    to_end = jnp.exp(end[:, :, None, :] - log_decay) * steps_cut
    flat = lambda a: a.reshape((blocks,) + a.shape[2:])
    cum = flat(log_decay)
    cum_t = jnp.swapaxes(cum, 1, 2)
    step_t = jnp.swapaxes(flat(steps_cut), 1, 2)
    xbc = activated.reshape(blocks, Q, width)
    spec = lambda shape: pl.BlockSpec((None,) + shape, lambda i: (i,) + (0,) * len(shape))
    state = pl.pallas_call(
        state_kernel,
        grid=(blocks,),
        in_specs=[
            spec((Q, width)),
            pl.BlockSpec((None, H * P_SIZE, Q), lambda i: (i // spans, 0, i % spans)),
            spec((Q, H)),
        ],
        out_specs=spec((H, P_SIZE, N)),
        out_shape=jax.ShapeDtypeStruct((blocks, H, P_SIZE, N), jnp.float32),
    )(xbc, activated_t, flat(to_end))
    inside = pl.pallas_call(
        partial(inside_kernel, reverse=reverse),
        grid=(blocks,),
        in_specs=[spec((Q, width)), spec((Q, H)), spec((H, Q)), spec((H, Q))],
        out_specs=spec((Q, H * P_SIZE)),
        out_shape=jax.ShapeDtypeStruct((blocks, Q, H * P_SIZE), jnp.float32),
    )(xbc, cum, cum_t, step_t)
    inside = inside.reshape(count, rows, H * P_SIZE)
    state = state.reshape(count, spans, H, P_SIZE, N)
    return inside, state, jnp.exp(end), jnp.exp(log_decay)


CONV_LANES = 256


def conv_kernel(src_ref, halo_ref, w_ref, b_ref, out_ref, out_t_ref, *, reverse):
    margin = KCONV - 1
    src = src_ref[...]
    rows = src.shape[0]
    edge = halo_ref.shape[0]
    w = w_ref[...]
    if reverse:
        near = jnp.concatenate([src[rows - edge :], halo_ref[...]], axis=0)
    else:
        near = jnp.concatenate([halo_ref[...], src[:edge]], axis=0)
    span = near.shape[0]
    main = jnp.broadcast_to(b_ref[...], src.shape)
    side = jnp.broadcast_to(b_ref[...], (edge, src.shape[1]))
    for tap in range(KCONV):
        shift = margin - tap
        if shift == 0:
            piece, near_piece = src, near
        elif reverse:
            piece = pltpu.roll(src, rows - shift, 0)
            near_piece = pltpu.roll(near, span - shift, 0)
        else:
            piece = pltpu.roll(src, shift, 0)
            near_piece = pltpu.roll(near, shift, 0)
        main = main + w[tap : tap + 1] * piece
        part = near_piece[:edge] if reverse else near_piece[edge:]
        side = side + w[tap : tap + 1] * part
    out_ref[...] = jax.nn.silu(main).astype(out_ref.dtype)
    if reverse:
        out_ref[rows - edge :, :] = jax.nn.silu(side).astype(out_ref.dtype)
    else:
        out_ref[:edge, :] = jax.nn.silu(side).astype(out_ref.dtype)
    out_t_ref[...] = jnp.transpose(out_ref[...].astype(jnp.float32)).astype(out_t_ref.dtype)


def convolve(projected, rows, conv_w, conv_b, reverse):
    inner = H * P_SIZE
    count = projected.shape[0]
    width = conv_w.shape[1]
    edge = 8
    lanes = CONV_LANES
    skip = (projected.shape[2] - width) // lanes
    return pl.pallas_call(
        partial(conv_kernel, reverse=reverse),
        grid=(count, width // lanes),
        in_specs=[
            pl.BlockSpec((None, rows, lanes), lambda g, j: (g, 0, j + skip)),
            pl.BlockSpec((None, edge, lanes), lambda g, j: (g, rows // edge, j + skip)),
            pl.BlockSpec((KCONV, lanes), lambda g, j: (0, j)),
            pl.BlockSpec((1, lanes), lambda g, j: (0, j)),
        ],
        out_specs=[
            pl.BlockSpec((None, rows, lanes), lambda g, j: (g, 0, j)),
            pl.BlockSpec((None, lanes, rows), lambda g, j: (g, j, 0)),
        ],
        out_shape=[
            jax.ShapeDtypeStruct((count, rows, width), jnp.bfloat16),
            jax.ShapeDtypeStruct((count, width, rows), jnp.bfloat16),
        ],
    )(projected, projected, conv_w, conv_b.reshape(1, width))


def strand_terms(projected, step_size, conv_w, conv_b, rates, reverse):
    inner = H * P_SIZE
    count, rows, _ = step_size.shape
    activated, activated_t = convolve(projected, rows, conv_w, conv_b, reverse)
    spans = rows // Q
    inside, state, total, from_start = block_terms(activated, activated_t, step_size, rates, reverse)
    order = list(range(spans))
    if reverse:
        order = order[::-1]
    before = {}
    sofar = (jnp.ones((count, H), jnp.float32), jnp.zeros((count, H, P_SIZE, N), jnp.float32))
    for j in order:
        before[j] = sofar
        sofar = chain(sofar, (total[:, j], state[:, j]))
    before_decay = jnp.stack([before[j][0] for j in range(spans)], axis=1)
    before_state = jnp.stack([before[j][1] for j in range(spans)], axis=1)
    pending = (before_decay, before_state, inside, from_start, activated)
    return sofar, pending


def finish(pending, incoming, gate_part, d_skip, norm_gain):
    before_decay, before_state, inside, from_start, activated = pending
    inner = H * P_SIZE
    count, rows, _ = activated.shape
    spans = rows // Q
    start_state = before_state + before_decay[..., None, None] * incoming[:, None]
    c_rows = activated[:, :, inner + N :].reshape(count, spans, Q, N)
    carried = jnp.einsum(
        "gjtn,gjkn->gjtk",
        c_rows.astype(jnp.float32),
        start_state.reshape(count, spans, inner, N),
        precision=lax.Precision.HIGHEST,
    ).reshape(count, rows, inner)
    heads = lax.broadcasted_iota(jnp.int32, (H, inner), 0)
    lanes = lax.broadcasted_iota(jnp.int32, (H, inner), 1)
    spread = (lanes // P_SIZE == heads).astype(jnp.float32)
    scale = jnp.einsum(
        "grh,hk->grk", from_start.reshape(count, rows, H), spread, precision=lax.Precision.HIGHEST
    )
    skip = jnp.repeat(d_skip, P_SIZE)
    scanned = inside + scale * carried + skip * activated[:, :, :inner].astype(jnp.float32)
    gated = scanned * jax.nn.silu(gate_part)
    return (
        gated
        * lax.rsqrt(jnp.mean(gated * gated, axis=-1, keepdims=True) + norm_epsilon)
        * norm_gain
    ).astype(jnp.bfloat16)


def matmul_kernel(x_ref, w_ref, out_ref):
    out_ref[...] = jnp.dot(x_ref[...], w_ref[...], preferred_element_type=jnp.float32)


def column_matmul(x, w, start, width, lanes=256):
    count, rows, depth = x.shape
    first = start // lanes
    return pl.pallas_call(
        matmul_kernel,
        grid=(count, width // lanes),
        in_specs=[
            pl.BlockSpec((None, rows, depth), lambda g, j: (g, 0, 0)),
            pl.BlockSpec((depth, lanes), lambda g, j: (0, j + first)),
        ],
        out_specs=pl.BlockSpec((None, rows, lanes), lambda g, j: (g, 0, j)),
        out_shape=jax.ShapeDtypeStruct((count, rows, width), jnp.float32),
    )(x, w)


def on_device(
    tokens, hidden, base_table, w_in, w_dt, conv_w, conv_b, dt_bias, a_log, d_skip, norm_gain, w_out
):
    inner = H * P_SIZE
    margin = KCONV - 1
    one_hot = (tokens[:, :, None] == jnp.arange(4)[None, None, :]).astype(jnp.bfloat16)
    looked = jnp.einsum("gtb,bd->gtd", one_hot, base_table, preferred_element_type=jnp.float32)
    strand = (hidden.astype(jnp.float32) + looked).astype(jnp.bfloat16)
    rows = strand.shape[1]
    count = lax.axis_size("seq")
    low = lax.ppermute(strand[:, rows - margin :], "seq", [(i, i + 1) for i in range(count - 1)])
    high = lax.ppermute(strand[:, :margin], "seq", [(i + 1, i) for i in range(count - 1)])
    rates = -jnp.exp(a_log)
    gap = jnp.zeros((strand.shape[0], 8 - margin, strand.shape[2]), strand.dtype)
    ext_f = jnp.concatenate([strand, gap, low], axis=1)
    source_width = w_in.shape[1] - inner
    proj_f = column_matmul(ext_f, w_in, inner, source_width)
    step_f = jax.nn.softplus(
        jnp.einsum("grd,dh->grh", strand, w_dt, preferred_element_type=jnp.float32) + dt_bias
    )
    sum_f, pend_f = strand_terms(proj_f, step_f, conv_w, conv_b, rates, False)
    sum_f, (strand_late, high) = lax.optimization_barrier((sum_f, (strand, high)))
    ext_r = flip_lanes(jnp.concatenate([strand_late, high, gap], axis=1))
    mirrored = ext_r[:, :rows]
    proj_r = column_matmul(ext_r, w_in, inner, source_width)
    step_r = jax.nn.softplus(
        jnp.einsum("grd,dh->grh", mirrored, w_dt, preferred_element_type=jnp.float32) + dt_bias
    )
    sum_r, pend_r = strand_terms(proj_r, step_r, conv_w, conv_b, rates, True)
    def forward_out(incoming):
        gate_f = column_matmul(strand, w_in, 0, inner)
        normed_f = finish(pend_f, incoming, gate_f, d_skip, norm_gain)
        return jnp.einsum("grk,kd->grd", normed_f, w_out, preferred_element_type=jnp.float32)

    in_r, out_f = exclusive_scans(sum_f, sum_r, "seq", forward_out)
    gate_r = column_matmul(mirrored, w_in, 0, inner)
    normed_r = finish(pend_r, in_r[1], gate_r, d_skip, norm_gain)
    w_out_mirrored = flip_lanes(w_out)
    out = out_f + jnp.einsum(
        "grk,kd->grd", normed_r, w_out_mirrored, preferred_element_type=jnp.float32
    )
    return out.astype(jnp.bfloat16)


def solution(mesh):
    placed = (
        P(("groups", "batch"), "seq"),
        P(("groups", "batch"), "seq", None),
        P(),
        P(),
        P(),
        P(),
        P(),
        P(),
        P(),
        P(),
        P(),
        P(),
    )
    return jax.shard_map(
        on_device,
        mesh=mesh,
        in_specs=placed,
        out_specs=P(("groups", "batch"), "seq", None),
        check_vma=False,
    )
```

```python
from functools import partial

import jax
import jax.numpy as jnp
from jax import lax
from jax.experimental import pallas as pl
from jax.experimental.pallas import tpu as pltpu
from jax.sharding import PartitionSpec as P

H = 16
P_SIZE = 64
N = 128
Q = 256
KCONV = 4


norm_epsilon = 1e-05


def exchange(size, dtype):
    row = lax.broadcasted_iota(jnp.int32, (size, size), 0)
    col = lax.broadcasted_iota(jnp.int32, (size, size), 1)
    return (row + col == size - 1).astype(dtype)


def flip_lanes(a):
    j = exchange(a.shape[-1], a.dtype)
    return jnp.einsum("...d,de->...e", a, j, preferred_element_type=jnp.float32).astype(a.dtype)


def chain(earlier, later):
    first_decay, first_state = earlier
    next_decay, next_state = later
    return (first_decay * next_decay, next_decay[..., None, None] * first_state + next_state)


def exclusive_scans(fwd, rev, axis, after_fwd):
    count = lax.axis_size(axis)
    place = lax.axis_index(axis)
    seen = [None, None]
    ahead = [fwd, rev]
    shift = 1
    while shift < count:
        up = [(i, i + shift) for i in range(count - shift)]
        down = [(i + shift, i) for i in range(count - shift)]
        got = []
        for k, pairs in ((0, up), (1, down)):
            decay, state = unpack(lax.ppermute(pack(*ahead[k]), axis, pairs))
            has = (place >= shift) if k == 0 else (place < count - shift)
            decay = jnp.where(has, decay, 1.0)
            got.append((decay, state))
        last = 2 * shift >= count
        for k in range(2):
            if k == 1 and last:
                tail = after_fwd(seen[0][1])
                got[1], tail = lax.optimization_barrier((got[1], tail))
            seen[k] = got[k] if seen[k] is None else chain(got[k], seen[k])
            if not last:
                ahead[k] = chain(got[k], ahead[k])
        shift *= 2
    if seen[0] is None:
        return fwd_identity(rev), after_fwd(fwd_identity(fwd)[1])
    return seen[1], tail


def pack(decay, state):
    count = state.shape[0]
    flat = state.reshape(count, H * P_SIZE, N)
    extra = jnp.zeros((count, 8, N), jnp.float32).at[:, 0, :H].set(decay)
    return jnp.concatenate([flat, extra], axis=1)


def unpack(packed):
    count = packed.shape[0]
    rows = H * P_SIZE
    return packed[:, rows, :H], packed[:, :rows].reshape(count, H, P_SIZE, N)


def fwd_identity(summary):
    decay, state = summary
    return (jnp.ones_like(decay), jnp.zeros_like(state))


def inside_kernel(xbc_ref, cum_ref, cum_t_ref, step_t_ref, inside_ref, *, reverse):
    inner = H * P_SIZE
    b_rows = xbc_ref[:, inner : inner + N]
    c_rows = xbc_ref[:, inner + N :]
    scores = lax.dot_general(
        c_rows, b_rows, (((1,), (1,)), ((), ())), preferred_element_type=jnp.float32
    )
    t_idx = lax.broadcasted_iota(jnp.int32, (Q, Q), 0)
    s_idx = lax.broadcasted_iota(jnp.int32, (Q, Q), 1)
    keep = (s_idx >= t_idx) if reverse else (t_idx >= s_idx)
    for h in range(H):
        gaps = cum_ref[:, h : h + 1] - cum_t_ref[h : h + 1, :]
        decays = jnp.where(keep, jnp.exp(jnp.where(keep, gaps, 0.0)), 0.0)
        weights = (decays * scores * step_t_ref[h : h + 1, :]).astype(jnp.bfloat16)
        x_h = xbc_ref[:, h * P_SIZE : (h + 1) * P_SIZE]
        inside_ref[:, h * P_SIZE : (h + 1) * P_SIZE] = jnp.dot(
            weights, x_h, preferred_element_type=jnp.float32
        )


def state_kernel(xbc_ref, x_t_ref, to_end_ref, state_ref):
    inner = H * P_SIZE
    b_wide = xbc_ref[:, inner : inner + N].astype(jnp.float32)
    for h in range(H):
        state_weights = (b_wide * to_end_ref[:, h : h + 1]).astype(jnp.bfloat16)
        state_ref[h] = jnp.dot(
            x_t_ref[h * P_SIZE : (h + 1) * P_SIZE, :],
            state_weights,
            preferred_element_type=jnp.float32,
        )


def block_terms(activated, activated_t, step_size, rates, reverse):
    count, rows, width = activated.shape
    spans = rows // Q
    blocks = count * spans
    steps_cut = step_size.reshape(count, spans, Q, H)
    rated = steps_cut * rates
    log_decay = jnp.cumsum(rated, axis=2)
    if reverse:
        log_decay = log_decay[:, :, -1:] - log_decay + rated
    end = log_decay[:, :, 0] if reverse else log_decay[:, :, -1]
    to_end = jnp.exp(end[:, :, None, :] - log_decay) * steps_cut
    flat = lambda a: a.reshape((blocks,) + a.shape[2:])
    cum = flat(log_decay)
    cum_t = jnp.swapaxes(cum, 1, 2)
    step_t = jnp.swapaxes(flat(steps_cut), 1, 2)
    xbc = activated.reshape(blocks, Q, width)
    spec = lambda shape: pl.BlockSpec((None,) + shape, lambda i: (i,) + (0,) * len(shape))
    state = pl.pallas_call(
        state_kernel,
        grid=(blocks,),
        in_specs=[
            spec((Q, width)),
            pl.BlockSpec((None, H * P_SIZE, Q), lambda i: (i // spans, 0, i % spans)),
            spec((Q, H)),
        ],
        out_specs=spec((H, P_SIZE, N)),
        out_shape=jax.ShapeDtypeStruct((blocks, H, P_SIZE, N), jnp.float32),
    )(xbc, activated_t, flat(to_end))
    inside = pl.pallas_call(
        partial(inside_kernel, reverse=reverse),
        grid=(blocks,),
        in_specs=[spec((Q, width)), spec((Q, H)), spec((H, Q)), spec((H, Q))],
        out_specs=spec((Q, H * P_SIZE)),
        out_shape=jax.ShapeDtypeStruct((blocks, Q, H * P_SIZE), jnp.float32),
    )(xbc, cum, cum_t, step_t)
    inside = inside.reshape(count, rows, H * P_SIZE)
    state = state.reshape(count, spans, H, P_SIZE, N)
    return inside, state, jnp.exp(end), jnp.exp(log_decay)


CONV_LANES = 256


def conv_kernel(src_ref, halo_ref, w_ref, b_ref, out_ref, out_t_ref, *, reverse):
    margin = KCONV - 1
    src = src_ref[...]
    rows = src.shape[0]
    edge = halo_ref.shape[0]
    w = w_ref[...]
    if reverse:
        near = jnp.concatenate([src[rows - edge :], halo_ref[...]], axis=0)
    else:
        near = jnp.concatenate([halo_ref[...], src[:edge]], axis=0)
    span = near.shape[0]
    main = jnp.broadcast_to(b_ref[...], src.shape)
    side = jnp.broadcast_to(b_ref[...], (edge, src.shape[1]))
    for tap in range(KCONV):
        shift = margin - tap
        if shift == 0:
            piece, near_piece = src, near
        elif reverse:
            piece = pltpu.roll(src, rows - shift, 0)
            near_piece = pltpu.roll(near, span - shift, 0)
        else:
            piece = pltpu.roll(src, shift, 0)
            near_piece = pltpu.roll(near, shift, 0)
        main = main + w[tap : tap + 1] * piece
        part = near_piece[:edge] if reverse else near_piece[edge:]
        side = side + w[tap : tap + 1] * part
    out_ref[...] = jax.nn.silu(main).astype(out_ref.dtype)
    if reverse:
        out_ref[rows - edge :, :] = jax.nn.silu(side).astype(out_ref.dtype)
    else:
        out_ref[:edge, :] = jax.nn.silu(side).astype(out_ref.dtype)
    out_t_ref[...] = jnp.transpose(out_ref[...].astype(jnp.float32)).astype(out_t_ref.dtype)


def convolve(projected, rows, conv_w, conv_b, reverse):
    inner = H * P_SIZE
    count = projected.shape[0]
    width = conv_w.shape[1]
    edge = 8
    lanes = CONV_LANES
    skip = (projected.shape[2] - width) // lanes
    return pl.pallas_call(
        partial(conv_kernel, reverse=reverse),
        grid=(count, width // lanes),
        in_specs=[
            pl.BlockSpec((None, rows, lanes), lambda g, j: (g, 0, j + skip)),
            pl.BlockSpec((None, edge, lanes), lambda g, j: (g, rows // edge, j + skip)),
            pl.BlockSpec((KCONV, lanes), lambda g, j: (0, j)),
            pl.BlockSpec((1, lanes), lambda g, j: (0, j)),
        ],
        out_specs=[
            pl.BlockSpec((None, rows, lanes), lambda g, j: (g, 0, j)),
            pl.BlockSpec((None, lanes, rows), lambda g, j: (g, j, 0)),
        ],
        out_shape=[
            jax.ShapeDtypeStruct((count, rows, width), jnp.bfloat16),
            jax.ShapeDtypeStruct((count, width, rows), jnp.bfloat16),
        ],
    )(projected, projected, conv_w, conv_b.reshape(1, width))


def strand_terms(projected, step_size, conv_w, conv_b, rates, reverse):
    inner = H * P_SIZE
    count, rows, _ = step_size.shape
    activated, activated_t = convolve(projected, rows, conv_w, conv_b, reverse)
    spans = rows // Q
    inside, state, total, from_start = block_terms(activated, activated_t, step_size, rates, reverse)
    order = list(range(spans))
    if reverse:
        order = order[::-1]
    before = {}
    sofar = (jnp.ones((count, H), jnp.float32), jnp.zeros((count, H, P_SIZE, N), jnp.float32))
    for j in order:
        before[j] = sofar
        sofar = chain(sofar, (total[:, j], state[:, j]))
    before_decay = jnp.stack([before[j][0] for j in range(spans)], axis=1)
    before_state = jnp.stack([before[j][1] for j in range(spans)], axis=1)
    pending = (before_decay, before_state, inside, from_start, activated)
    return sofar, pending


def finish(pending, incoming, gate_part, d_skip, norm_gain):
    before_decay, before_state, inside, from_start, activated = pending
    inner = H * P_SIZE
    count, rows, _ = activated.shape
    spans = rows // Q
    start_state = before_state + before_decay[..., None, None] * incoming[:, None]
    c_rows = activated[:, :, inner + N :].reshape(count, spans, Q, N)
    carried = jnp.einsum(
        "gjtn,gjkn->gjtk",
        c_rows.astype(jnp.float32),
        start_state.reshape(count, spans, inner, N),
        precision=lax.Precision.HIGHEST,
    ).reshape(count, rows, inner)
    heads = lax.broadcasted_iota(jnp.int32, (H, inner), 0)
    lanes = lax.broadcasted_iota(jnp.int32, (H, inner), 1)
    spread = (lanes // P_SIZE == heads).astype(jnp.float32)
    scale = jnp.einsum(
        "grh,hk->grk", from_start.reshape(count, rows, H), spread, precision=lax.Precision.HIGHEST
    )
    skip = jnp.repeat(d_skip, P_SIZE)
    scanned = inside + scale * carried + skip * activated[:, :, :inner].astype(jnp.float32)
    gated = scanned * jax.nn.silu(gate_part)
    return (
        gated
        * lax.rsqrt(jnp.mean(gated * gated, axis=-1, keepdims=True) + norm_epsilon)
        * norm_gain
    ).astype(jnp.bfloat16)


def on_device(
    tokens, hidden, base_table, w_in, w_dt, conv_w, conv_b, dt_bias, a_log, d_skip, norm_gain, w_out
):
    inner = H * P_SIZE
    margin = KCONV - 1
    one_hot = (tokens[:, :, None] == jnp.arange(4)[None, None, :]).astype(jnp.bfloat16)
    looked = jnp.einsum("gtb,bd->gtd", one_hot, base_table, preferred_element_type=jnp.float32)
    strand = (hidden.astype(jnp.float32) + looked).astype(jnp.bfloat16)
    rows = strand.shape[1]
    count = lax.axis_size("seq")
    low = lax.ppermute(strand[:, rows - margin :], "seq", [(i, i + 1) for i in range(count - 1)])
    high = lax.ppermute(strand[:, :margin], "seq", [(i + 1, i) for i in range(count - 1)])
    rates = -jnp.exp(a_log)
    gap = jnp.zeros((strand.shape[0], 8 - margin, strand.shape[2]), strand.dtype)
    ext_f = jnp.concatenate([strand, gap, low], axis=1)
    w_source = w_in[:, inner:]
    w_gate = w_in[:, :inner]
    proj_f = jnp.einsum("grd,de->gre", ext_f, w_source, preferred_element_type=jnp.float32)
    step_f = jax.nn.softplus(
        jnp.einsum("grd,dh->grh", strand, w_dt, preferred_element_type=jnp.float32) + dt_bias
    )
    sum_f, pend_f = strand_terms(proj_f, step_f, conv_w, conv_b, rates, False)
    sum_f, (strand_late, high) = lax.optimization_barrier((sum_f, (strand, high)))
    ext_r = flip_lanes(jnp.concatenate([strand_late, high, gap], axis=1))
    mirrored = ext_r[:, :rows]
    proj_r = jnp.einsum("grd,de->gre", ext_r, w_source, preferred_element_type=jnp.float32)
    step_r = jax.nn.softplus(
        jnp.einsum("grd,dh->grh", mirrored, w_dt, preferred_element_type=jnp.float32) + dt_bias
    )
    sum_r, pend_r = strand_terms(proj_r, step_r, conv_w, conv_b, rates, True)
    def forward_out(incoming):
        incoming, (strand_gate, mirrored_gate) = lax.optimization_barrier(
            (incoming, (strand, mirrored))
        )
        gate_f = jnp.einsum("grd,de->gre", strand_gate, w_gate, preferred_element_type=jnp.float32)
        gate_r = jnp.einsum(
            "grd,de->gre", mirrored_gate, w_gate, preferred_element_type=jnp.float32
        )
        normed_f = finish(pend_f, incoming, gate_f, d_skip, norm_gain)
        out_f = jnp.einsum("grk,kd->grd", normed_f, w_out, preferred_element_type=jnp.float32)
        return out_f, gate_r

    in_r, (out_f, gate_r) = exclusive_scans(sum_f, sum_r, "seq", forward_out)
    normed_r = finish(pend_r, in_r[1], gate_r, d_skip, norm_gain)
    w_out_mirrored = flip_lanes(w_out)
    out = out_f + jnp.einsum(
        "grk,kd->grd", normed_r, w_out_mirrored, preferred_element_type=jnp.float32
    )
    return out.astype(jnp.bfloat16)


def solution(mesh):
    placed = (
        P(("groups", "batch"), "seq"),
        P(("groups", "batch"), "seq", None),
        P(),
        P(),
        P(),
        P(),
        P(),
        P(),
        P(),
        P(),
        P(),
        P(),
    )
    return jax.shard_map(
        on_device,
        mesh=mesh,
        in_specs=placed,
        out_specs=P(("groups", "batch"), "seq", None),
        check_vma=False,
    )
```

```python
from functools import partial

import jax
import jax.numpy as jnp
from jax import lax
from jax.experimental import pallas as pl
from jax.experimental.pallas import tpu as pltpu
from jax.sharding import PartitionSpec as P

H = 16
P_SIZE = 64
N = 128
Q = 256
KCONV = 4


norm_epsilon = 1e-05


def exchange(size, dtype):
    row = lax.broadcasted_iota(jnp.int32, (size, size), 0)
    col = lax.broadcasted_iota(jnp.int32, (size, size), 1)
    return (row + col == size - 1).astype(dtype)


def flip_lanes(a):
    j = exchange(a.shape[-1], a.dtype)
    return jnp.einsum("...d,de->...e", a, j, preferred_element_type=jnp.float32).astype(a.dtype)


def chain(earlier, later):
    first_decay, first_state = earlier
    next_decay, next_state = later
    return (first_decay * next_decay, next_decay[..., None, None] * first_state + next_state)


def exclusive_scans(fwd, rev, axis, after_fwd, middle=None):
    count = lax.axis_size(axis)
    place = lax.axis_index(axis)
    seen = [None, None]
    ahead = [fwd, rev]
    shift = 1
    while shift < count:
        up = [(i, i + shift) for i in range(count - shift)]
        down = [(i + shift, i) for i in range(count - shift)]
        got = []
        fill = middle if shift == 2 and fill_pending(middle) else None
        if fill is not None:
            ahead, fill_args = lax.optimization_barrier((ahead, fill[1]))
        for k, pairs in ((0, up), (1, down)):
            decay, state = unpack(lax.ppermute(pack(*ahead[k]), axis, pairs))
            has = (place >= shift) if k == 0 else (place < count - shift)
            decay = jnp.where(has, decay, 1.0)
            got.append((decay, state))
        if fill is not None:
            got, middle = lax.optimization_barrier((got, fill[0](*fill_args)))
        last = 2 * shift >= count
        for k in range(2):
            if k == 1 and last:
                if fill_pending(middle):
                    middle = middle[0](*middle[1])
                tail = after_fwd(seen[0][1], middle)
                got[1], tail = lax.optimization_barrier((got[1], tail))
            seen[k] = got[k] if seen[k] is None else chain(got[k], seen[k])
            if not last:
                ahead[k] = chain(got[k], ahead[k])
        shift *= 2
    if seen[0] is None:
        middle = middle[0](*middle[1])
        return fwd_identity(rev), after_fwd(fwd_identity(fwd)[1], middle), middle
    return seen[1], tail, middle


def fill_pending(item):
    return isinstance(item, tuple) and callable(item[0])


def pack(decay, state):
    count = state.shape[0]
    flat = state.reshape(count, H * P_SIZE, N)
    extra = jnp.zeros((count, 8, N), jnp.float32).at[:, 0, :H].set(decay)
    return jnp.concatenate([flat, extra], axis=1)


def unpack(packed):
    count = packed.shape[0]
    rows = H * P_SIZE
    return packed[:, rows, :H], packed[:, :rows].reshape(count, H, P_SIZE, N)


def fwd_identity(summary):
    decay, state = summary
    return (jnp.ones_like(decay), jnp.zeros_like(state))


def inside_kernel(xbc_ref, cum_ref, cum_t_ref, step_t_ref, inside_ref, *, reverse):
    inner = H * P_SIZE
    b_rows = xbc_ref[:, inner : inner + N]
    c_rows = xbc_ref[:, inner + N :]
    scores = lax.dot_general(
        c_rows, b_rows, (((1,), (1,)), ((), ())), preferred_element_type=jnp.float32
    )
    t_idx = lax.broadcasted_iota(jnp.int32, (Q, Q), 0)
    s_idx = lax.broadcasted_iota(jnp.int32, (Q, Q), 1)
    keep = (s_idx >= t_idx) if reverse else (t_idx >= s_idx)
    for h in range(H):
        gaps = cum_ref[:, h : h + 1] - cum_t_ref[h : h + 1, :]
        decays = jnp.where(keep, jnp.exp(jnp.where(keep, gaps, 0.0)), 0.0)
        weights = (decays * scores * step_t_ref[h : h + 1, :]).astype(jnp.bfloat16)
        x_h = xbc_ref[:, h * P_SIZE : (h + 1) * P_SIZE]
        inside_ref[:, h * P_SIZE : (h + 1) * P_SIZE] = jnp.dot(
            weights, x_h, preferred_element_type=jnp.float32
        )


def state_kernel(xbc_ref, x_t_ref, to_end_ref, state_ref):
    inner = H * P_SIZE
    b_wide = xbc_ref[:, inner : inner + N].astype(jnp.float32)
    for h in range(H):
        state_weights = (b_wide * to_end_ref[:, h : h + 1]).astype(jnp.bfloat16)
        state_ref[h] = jnp.dot(
            x_t_ref[h * P_SIZE : (h + 1) * P_SIZE, :],
            state_weights,
            preferred_element_type=jnp.float32,
        )


def block_terms(activated, activated_t, step_size, rates, reverse):
    count, rows, width = activated.shape
    spans = rows // Q
    blocks = count * spans
    steps_cut = step_size.reshape(count, spans, Q, H)
    rated = steps_cut * rates
    log_decay = jnp.cumsum(rated, axis=2)
    if reverse:
        log_decay = log_decay[:, :, -1:] - log_decay + rated
    end = log_decay[:, :, 0] if reverse else log_decay[:, :, -1]
    to_end = jnp.exp(end[:, :, None, :] - log_decay) * steps_cut
    flat = lambda a: a.reshape((blocks,) + a.shape[2:])
    cum = flat(log_decay)
    cum_t = jnp.swapaxes(cum, 1, 2)
    step_t = jnp.swapaxes(flat(steps_cut), 1, 2)
    xbc = activated.reshape(blocks, Q, width)
    spec = lambda shape: pl.BlockSpec((None,) + shape, lambda i: (i,) + (0,) * len(shape))
    state = pl.pallas_call(
        state_kernel,
        grid=(blocks,),
        in_specs=[
            spec((Q, width)),
            pl.BlockSpec((None, H * P_SIZE, Q), lambda i: (i // spans, 0, i % spans)),
            spec((Q, H)),
        ],
        out_specs=spec((H, P_SIZE, N)),
        out_shape=jax.ShapeDtypeStruct((blocks, H, P_SIZE, N), jnp.float32),
    )(xbc, activated_t, flat(to_end))
    inside = pl.pallas_call(
        partial(inside_kernel, reverse=reverse),
        grid=(blocks,),
        in_specs=[spec((Q, width)), spec((Q, H)), spec((H, Q)), spec((H, Q))],
        out_specs=spec((Q, H * P_SIZE)),
        out_shape=jax.ShapeDtypeStruct((blocks, Q, H * P_SIZE), jnp.float32),
    )(xbc, cum, cum_t, step_t)
    inside = inside.reshape(count, rows, H * P_SIZE)
    state = state.reshape(count, spans, H, P_SIZE, N)
    return inside, state, jnp.exp(end), jnp.exp(log_decay)


CONV_LANES = 256


def conv_kernel(src_ref, halo_ref, w_ref, b_ref, out_ref, out_t_ref, *, reverse):
    margin = KCONV - 1
    src = src_ref[...]
    rows = src.shape[0]
    edge = halo_ref.shape[0]
    w = w_ref[...]
    if reverse:
        near = jnp.concatenate([src[rows - edge :], halo_ref[...]], axis=0)
    else:
        near = jnp.concatenate([halo_ref[...], src[:edge]], axis=0)
    span = near.shape[0]
    main = jnp.broadcast_to(b_ref[...], src.shape)
    side = jnp.broadcast_to(b_ref[...], (edge, src.shape[1]))
    for tap in range(KCONV):
        shift = margin - tap
        if shift == 0:
            piece, near_piece = src, near
        elif reverse:
            piece = pltpu.roll(src, rows - shift, 0)
            near_piece = pltpu.roll(near, span - shift, 0)
        else:
            piece = pltpu.roll(src, shift, 0)
            near_piece = pltpu.roll(near, shift, 0)
        main = main + w[tap : tap + 1] * piece
        part = near_piece[:edge] if reverse else near_piece[edge:]
        side = side + w[tap : tap + 1] * part
    out_ref[...] = jax.nn.silu(main).astype(out_ref.dtype)
    if reverse:
        out_ref[rows - edge :, :] = jax.nn.silu(side).astype(out_ref.dtype)
    else:
        out_ref[:edge, :] = jax.nn.silu(side).astype(out_ref.dtype)
    out_t_ref[...] = jnp.transpose(out_ref[...].astype(jnp.float32)).astype(out_t_ref.dtype)


def convolve(projected, rows, conv_w, conv_b, reverse):
    inner = H * P_SIZE
    count = projected.shape[0]
    width = conv_w.shape[1]
    edge = 8
    lanes = CONV_LANES
    skip = (projected.shape[2] - width) // lanes
    return pl.pallas_call(
        partial(conv_kernel, reverse=reverse),
        grid=(count, width // lanes),
        in_specs=[
            pl.BlockSpec((None, rows, lanes), lambda g, j: (g, 0, j + skip)),
            pl.BlockSpec((None, edge, lanes), lambda g, j: (g, rows // edge, j + skip)),
            pl.BlockSpec((KCONV, lanes), lambda g, j: (0, j)),
            pl.BlockSpec((1, lanes), lambda g, j: (0, j)),
        ],
        out_specs=[
            pl.BlockSpec((None, rows, lanes), lambda g, j: (g, 0, j)),
            pl.BlockSpec((None, lanes, rows), lambda g, j: (g, j, 0)),
        ],
        out_shape=[
            jax.ShapeDtypeStruct((count, rows, width), jnp.bfloat16),
            jax.ShapeDtypeStruct((count, width, rows), jnp.bfloat16),
        ],
    )(projected, projected, conv_w, conv_b.reshape(1, width))


def strand_terms(projected, step_size, conv_w, conv_b, rates, reverse):
    inner = H * P_SIZE
    count, rows, _ = step_size.shape
    activated, activated_t = convolve(projected, rows, conv_w, conv_b, reverse)
    spans = rows // Q
    inside, state, total, from_start = block_terms(activated, activated_t, step_size, rates, reverse)
    order = list(range(spans))
    if reverse:
        order = order[::-1]
    before = {}
    sofar = (jnp.ones((count, H), jnp.float32), jnp.zeros((count, H, P_SIZE, N), jnp.float32))
    for j in order:
        before[j] = sofar
        sofar = chain(sofar, (total[:, j], state[:, j]))
    before_decay = jnp.stack([before[j][0] for j in range(spans)], axis=1)
    before_state = jnp.stack([before[j][1] for j in range(spans)], axis=1)
    pending = (before_decay, before_state, inside, from_start, activated)
    return sofar, pending


def finish(pending, incoming, gate_part, d_skip, norm_gain):
    before_decay, before_state, inside, from_start, activated = pending
    inner = H * P_SIZE
    count, rows, _ = activated.shape
    spans = rows // Q
    start_state = before_state + before_decay[..., None, None] * incoming[:, None]
    c_rows = activated[:, :, inner + N :].reshape(count, spans, Q, N)
    carried = jnp.einsum(
        "gjtn,gjkn->gjtk",
        c_rows.astype(jnp.float32),
        start_state.reshape(count, spans, inner, N),
        precision=lax.Precision.HIGHEST,
    ).reshape(count, rows, inner)
    heads = lax.broadcasted_iota(jnp.int32, (H, inner), 0)
    lanes = lax.broadcasted_iota(jnp.int32, (H, inner), 1)
    spread = (lanes // P_SIZE == heads).astype(jnp.float32)
    scale = jnp.einsum(
        "grh,hk->grk", from_start.reshape(count, rows, H), spread, precision=lax.Precision.HIGHEST
    )
    skip = jnp.repeat(d_skip, P_SIZE)
    scanned = inside + scale * carried + skip * activated[:, :, :inner].astype(jnp.float32)
    gated = scanned * jax.nn.silu(gate_part)
    return (
        gated
        * lax.rsqrt(jnp.mean(gated * gated, axis=-1, keepdims=True) + norm_epsilon)
        * norm_gain
    ).astype(jnp.bfloat16)


def on_device(
    tokens, hidden, base_table, w_in, w_dt, conv_w, conv_b, dt_bias, a_log, d_skip, norm_gain, w_out
):
    inner = H * P_SIZE
    margin = KCONV - 1
    one_hot = (tokens[:, :, None] == jnp.arange(4)[None, None, :]).astype(jnp.bfloat16)
    looked = jnp.einsum("gtb,bd->gtd", one_hot, base_table, preferred_element_type=jnp.float32)
    strand = (hidden.astype(jnp.float32) + looked).astype(jnp.bfloat16)
    rows = strand.shape[1]
    count = lax.axis_size("seq")
    low = lax.ppermute(strand[:, rows - margin :], "seq", [(i, i + 1) for i in range(count - 1)])
    high = lax.ppermute(strand[:, :margin], "seq", [(i + 1, i) for i in range(count - 1)])
    rates = -jnp.exp(a_log)
    gap = jnp.zeros((strand.shape[0], 8 - margin, strand.shape[2]), strand.dtype)
    ext_f = jnp.concatenate([strand, gap, low], axis=1)
    w_source = w_in[:, inner:]
    w_gate = w_in[:, :inner]
    proj_f = jnp.einsum("grd,de->gre", ext_f, w_source, preferred_element_type=jnp.float32)
    step_f = jax.nn.softplus(
        jnp.einsum("grd,dh->grh", strand, w_dt, preferred_element_type=jnp.float32) + dt_bias
    )
    sum_f, pend_f = strand_terms(proj_f, step_f, conv_w, conv_b, rates, False)
    sum_f, (strand_late, high) = lax.optimization_barrier((sum_f, (strand, high)))
    ext_r = flip_lanes(jnp.concatenate([strand_late, high, gap], axis=1))
    mirrored = ext_r[:, :rows]
    proj_r = jnp.einsum("grd,de->gre", ext_r, w_source, preferred_element_type=jnp.float32)
    step_r = jax.nn.softplus(
        jnp.einsum("grd,dh->grh", mirrored, w_dt, preferred_element_type=jnp.float32) + dt_bias
    )
    sum_r, pend_r = strand_terms(proj_r, step_r, conv_w, conv_b, rates, True)
    def forward_out(incoming, gates):
        normed_f = finish(pend_f, incoming, gates[0], d_skip, norm_gain)
        return jnp.einsum("grk,kd->grd", normed_f, w_out, preferred_element_type=jnp.float32)

    def gate_pair(a, b):
        return (
            jnp.einsum("grd,de->gre", a, w_gate, preferred_element_type=jnp.float32),
            jnp.einsum("grd,de->gre", b, w_gate, preferred_element_type=jnp.float32),
        )

    in_r, out_f, gates = exclusive_scans(
        sum_f, sum_r, "seq", forward_out, (gate_pair, (strand, mirrored))
    )
    gate_r = gates[1]
    normed_r = finish(pend_r, in_r[1], gate_r, d_skip, norm_gain)
    w_out_mirrored = flip_lanes(w_out)
    out = out_f + jnp.einsum(
        "grk,kd->grd", normed_r, w_out_mirrored, preferred_element_type=jnp.float32
    )
    return out.astype(jnp.bfloat16)


def solution(mesh):
    placed = (
        P(("groups", "batch"), "seq"),
        P(("groups", "batch"), "seq", None),
        P(),
        P(),
        P(),
        P(),
        P(),
        P(),
        P(),
        P(),
        P(),
        P(),
    )
    return jax.shard_map(
        on_device,
        mesh=mesh,
        in_specs=placed,
        out_specs=P(("groups", "batch"), "seq", None),
        check_vma=False,
    )
```
